128 devices in a mesh: space: 16 (over y, x), spec: 8 (over z, core).
Axes of the slice: x: 4, y: 4, z: 4, core: 2. Of those that a mesh axis runs over, the one named last changes fastest.
Arguments:
- action: float32 [64, 1296, 1024], P('space', 'spec'), may hold values from 0.2 to 1.5
- coupling: float32 [1296], replicated, may hold values from 0.05 to 0.5
- active: int32 [64], P('space'), may hold values from 0 to 1, as said below
- neighbours: int32 [64, 4], P('space'), may hold values from -1 to 63, as said below
- pairs: int32 [1296, 2], replicated, may hold values from 0 to 1295, as said below
Outputs:
- evolved: float32 [64, 1296, 1024], P('space', 'spec')
The draws below stay inside these ranges and needn't reach their ends.
Inputs may be any that keep to these rules, and one draw needn't show every extreme that they name: `active`: 1 where the slot holds a sea block of the window, 0 where it holds land; some slot is 0 in every draw. The window is 8 blocks wide and 8 blocks high, its blocks placed on slots in any order. neighbours[s, k] is the slot holding the sea block beside slot s's block on side k (west, east, south, north), or -1 where that side is the window's edge or land, or where slot s is land; the relation is mutual. pairs[c, 0] is a component of a higher or equal frequency, pairs[c, 1] one of a lower or equal frequency.
All inputs are finite; a program needn't handle non-finite values.
Results may differ from the reference program's by a relative error of at most 0.0003.
Values sent between devices are 32-bit elements; how exact they have to be, the bound alone decides.
No kernel may reach another device: no remote copies, remote signals or barrier semaphores. Data moves between devices by JAX's collectives and lax.ppermute only.
A program may use at most 192 MiB of HBM per device.

```python
import math
import jax
import jax.numpy as jnp
from jax import lax

NDIR = 36
NFREQ = 36
BLOCK_SIDE = 32
SUBSTEPS = 3
BASIN_BLOCKS_X = 8
SLOT_COUNT = 64
SPECTRAL_COUNT = 1296
BLOCK_CELLS = 1024


def basin_layout(key):
    base_key = jax.random.fold_in(key, 5)
    shuffle_key, land_key, picking_key = jax.random.split(base_key, 3)
    block_numbers = jnp.arange(SLOT_COUNT, dtype=jnp.int32)
    owning_slot = jax.random.permutation(shuffle_key, SLOT_COUNT).astype(jnp.int32)
    forcing_value = jax.random.randint(picking_key, (), 0, SLOT_COUNT)
    land_mask = (jax.random.randint(land_key, (SLOT_COUNT,), 0, 4) == 0) | (block_numbers == forcing_value)
    sea_block = jnp.logical_not(land_mask)
    column = block_numbers % BASIN_BLOCKS_X
    row_idx = block_numbers // BASIN_BLOCKS_X
    wave_height = SLOT_COUNT // BASIN_BLOCKS_X
    inside_list = (column > 0, column < BASIN_BLOCKS_X - 1, row_idx > 0, row_idx < wave_height - 1)
    other_list = (block_numbers - 1, block_numbers + 1, block_numbers - BASIN_BLOCKS_X, block_numbers + BASIN_BLOCKS_X)
    by_block = []
    for inside, partner_index in zip(inside_list, other_list):
        clamped_partner = jnp.clip(partner_index, 0, SLOT_COUNT - 1)
        usable = inside & sea_block & sea_block[clamped_partner]
        by_block.append(jnp.where(usable, owning_slot[clamped_partner], -1))
    by_block = jnp.stack(by_block, axis=1)
    owning_block = jnp.zeros((SLOT_COUNT,), jnp.int32).at[owning_slot].set(block_numbers)
    active_slots = sea_block[owning_block].astype(jnp.int32)
    neighbour_slots = by_block[owning_block].astype(jnp.int32)
    return (active_slots, neighbour_slots)


def draw_active(key, part):
    return basin_layout(key)[0]


def draw_neighbours(key, part):
    return basin_layout(key)[1]


def draw_pairs(key, part):
    keys = jax.random.split(jax.random.fold_in(key, 11), 4)
    component = jnp.arange(NDIR * NFREQ, dtype=jnp.int32)
    frequency = component // NDIR
    direction = component % NDIR
    up_step = jax.random.randint(keys[0], (NDIR * NFREQ,), 1, 3)
    down_step = jax.random.randint(keys[1], (NDIR * NFREQ,), 1, 3)
    up_turn = jax.random.randint(keys[2], (NFREQ,), 1, NDIR)
    down_turn = jax.random.randint(keys[3], (NFREQ,), 1, NDIR)
    plus_comp = jnp.minimum(frequency + up_step, NFREQ - 1) * NDIR + (direction + up_turn[frequency]) % NDIR
    minus_comp = jnp.maximum(frequency - down_step, 0) * NDIR + (direction - down_turn[frequency]) % NDIR
    return jnp.stack([plus_comp, minus_comp], axis=1).astype(jnp.int32)


def shard_levels(own_key, extent, cuts, smallest, high):
    def one(dim, blocks):
        draws = jax.random.uniform(jax.random.fold_in(jax.random.fold_in(own_key, 6), dim), (blocks,), jnp.float32, smallest / len(cuts), high / len(cuts))
        return jnp.repeat(jnp.exp(draws), extent[dim] // blocks).reshape((-1,) + (1,) * (len(extent) - dim - 1))

    loudness = one(*cuts[0])
    for cut in cuts[1:]:
        loudness = loudness * one(*cut)
    return loudness


def setup_inputs(seed: int = 0) -> dict:
    streams_of = jax.random.split(jax.random.key(seed), 6)
    action = jnp.clip(jnp.exp(math.log(1.5) - 2.014903 * jax.random.uniform(streams_of[0], (SLOT_COUNT, SPECTRAL_COUNT, BLOCK_CELLS), jnp.float32) ** shard_levels(streams_of[0], (SLOT_COUNT, SPECTRAL_COUNT, BLOCK_CELLS), ((0, 16), (1, 8)), -0.2, 0.2)), 0.2, 1.5)
    coupling = jnp.clip(jnp.exp(jax.random.uniform(streams_of[1], (SPECTRAL_COUNT,), jnp.float32, math.log(0.05), math.log(0.5))), 0.05, 0.5)
    active = draw_active(jax.random.fold_in(streams_of[5], 71), 0)
    neighbours = draw_neighbours(jax.random.fold_in(streams_of[5], 71), 0)
    pairs = draw_pairs(jax.random.fold_in(streams_of[5], 71), 0)
    return dict(action=action, coupling=coupling, active=active, neighbours=neighbours, pairs=pairs)


CFL = 0.68


def courant(comp_ids):
    frequency = (comp_ids // NDIR).astype(jnp.float32)
    direction = comp_ids % NDIR
    half_dirs = NDIR // 2
    angles = (2.0 * math.pi / NDIR) * ((2 * (direction % half_dirs) + direction // half_dirs).astype(jnp.float32) + 0.5)
    speeds = CFL * jnp.exp(-frequency * math.log(1.1))
    return speeds * jnp.cos(angles), speeds * jnp.sin(angles)


def substep(current_action, neighbours, courant_x, courant_y):
    slot_layout = current_action.reshape(SLOT_COUNT, SPECTRAL_COUNT, BLOCK_SIDE, BLOCK_SIDE)
    sources_by_side = (slot_layout[:, :, :, -1], slot_layout[:, :, :, 0], slot_layout[:, :, -1, :], slot_layout[:, :, 0, :])
    x_plus = jnp.maximum(courant_x, 0.0)[:, None, None]
    x_minus = jnp.minimum(courant_x, 0.0)[:, None, None]
    y_plus = jnp.maximum(courant_y, 0.0)[:, None, None]
    y_minus = jnp.minimum(courant_y, 0.0)[:, None, None]

    def single_slot(slot_id):
        field = slot_layout[slot_id]
        ghosts = []
        for side_idx in range(4):
            neighbour = neighbours[slot_id, side_idx]
            present = neighbour >= 0
            safe_slot = jnp.where(present, neighbour, 0).astype(jnp.int32)
            ghosts.append(jnp.where(present, sources_by_side[side_idx][safe_slot], 0.0))
        ghost_west, ghost_east, ghost_south, ghost_north = ghosts
        from_west = jnp.concatenate([ghost_west[:, :, None], field[:, :, :-1]], axis=2)
        from_east = jnp.concatenate([field[:, :, 1:], ghost_east[:, :, None]], axis=2)
        from_south = jnp.concatenate([ghost_south[:, None, :], field[:, :-1, :]], axis=1)
        from_north = jnp.concatenate([field[:, 1:, :], ghost_north[:, None, :]], axis=1)
        updated = field - (x_plus * (field - from_west) + x_minus * (from_east - field)) - (y_plus * (field - from_south) + y_minus * (from_north - field))
        return updated.reshape(SPECTRAL_COUNT, BLOCK_CELLS)

    return lax.map(single_slot, jnp.arange(SLOT_COUNT, dtype=jnp.int32))


def interact(spectra, pairs, coupling):
    plus_vals = spectra[pairs[:, 0]]
    minus_vals = spectra[pairs[:, 1]]
    interaction = coupling[:, None] * (spectra * spectra * (plus_vals + minus_vals) - 2.0 * spectra * plus_vals * minus_vals)
    change = jax.ops.segment_sum(interaction, pairs[:, 0], num_segments=SPECTRAL_COUNT) + jax.ops.segment_sum(interaction, pairs[:, 1], num_segments=SPECTRAL_COUNT) - 2.0 * interaction
    return spectra + change


def reference(action, coupling, active, neighbours, pairs):
    courant_x, courant_y = courant(jnp.arange(SPECTRAL_COUNT, dtype=jnp.int32))
    current_action = action
    for substep_idx in range(SUBSTEPS):
        current_action = substep(current_action, neighbours, courant_x, courant_y)
    evolved = lax.map(lambda spectra: interact(spectra, pairs, coupling), current_action)
    return jnp.where(active[:, None, None] > 0, evolved, 0.0)
```

```python
import functools
import math

import jax
import jax.numpy as jnp
from jax import lax
from jax.experimental import pallas as pl
from jax.experimental.pallas import tpu as pltpu
from jax.sharding import PartitionSpec as P

NDIR = 36
BLOCK_SIDE = 32
BLOCK_CELLS = BLOCK_SIDE * BLOCK_SIDE
SUBSTEPS = 3
SPECTRAL_COUNT = 1296
CAPACITY = 4
HIGH = lax.Precision.HIGHEST
INTERPRET = False

CFL = 0.68


def courant(comp_ids):
    frequency = (comp_ids // NDIR).astype(jnp.float32)
    direction = comp_ids % NDIR
    half_dirs = NDIR // 2
    angles = (
        2.0
        * math.pi
        / NDIR
        * ((2 * (direction % half_dirs) + direction // half_dirs).astype(jnp.float32) + 0.5)
    )
    speeds = CFL * jnp.exp(-frequency * math.log(1.1))
    return (speeds * jnp.cos(angles), speeds * jnp.sin(angles))


def _edge_hits():
    row = lax.broadcasted_iota(jnp.int32, (4 * BLOCK_SIDE, BLOCK_CELLS), 0)
    cell = lax.broadcasted_iota(jnp.int32, (4 * BLOCK_SIDE, BLOCK_CELLS), 1)
    side = row // BLOCK_SIDE
    t = row % BLOCK_SIDE
    target = jnp.where(
        side == 0,
        t * BLOCK_SIDE,
        jnp.where(
            side == 1,
            t * BLOCK_SIDE + BLOCK_SIDE - 1,
            jnp.where(side == 2, t, BLOCK_CELLS - BLOCK_SIDE + t),
        ),
    )
    return side, cell == target


def _edges_of(field, hit):
    return lax.dot_general(
        field,
        hit.astype(jnp.float32),
        (((1,), (1,)), ((), ())),
        precision=HIGH,
        preferred_element_type=jnp.float32,
    )


def _edge_kernel(a_ref, e_ref):
    _, hit = _edge_hits()
    e_ref[0] = _edges_of(a_ref[0], hit)


def _step_kernel(a_ref, g_ref, c_ref, o_ref, e_ref):
    a = a_ref[0]
    g = g_ref[0]
    side, hit = _edge_hits()
    g_we = jnp.dot(g, (hit & (side < 2)).astype(jnp.float32), precision=HIGH,
                   preferred_element_type=jnp.float32)
    g_sn = jnp.dot(g, (hit & (side >= 2)).astype(jnp.float32), precision=HIGH,
                   preferred_element_type=jnp.float32)
    cell = lax.broadcasted_iota(jnp.int32, (1, BLOCK_CELLS), 1)
    x = cell % BLOCK_SIDE
    y = cell // BLOCK_SIDE
    from_west = jnp.where(x == 0, g_we, pltpu.roll(a, 1, 1))
    from_east = jnp.where(x == BLOCK_SIDE - 1, g_we, pltpu.roll(a, BLOCK_CELLS - 1, 1))
    from_south = jnp.where(y == 0, g_sn, pltpu.roll(a, BLOCK_SIDE, 1))
    from_north = jnp.where(y == BLOCK_SIDE - 1, g_sn, pltpu.roll(a, BLOCK_CELLS - BLOCK_SIDE, 1))
    x_plus = c_ref[0]
    x_minus = c_ref[1]
    y_plus = c_ref[2]
    y_minus = c_ref[3]
    new = (
        a
        - (x_plus * (a - from_west) + x_minus * (from_east - a))
        - (y_plus * (a - from_south) + y_minus * (from_north - a))
    )
    o_ref[0] = new
    e_ref[0] = _edges_of(new, hit)


def edges_call(action):
    blocks, comps, cells = action.shape
    return pl.pallas_call(
        _edge_kernel,
        grid=(blocks,),
        in_specs=[pl.BlockSpec((1, comps, cells), lambda b: (b, 0, 0))],
        out_specs=pl.BlockSpec((1, comps, 4 * BLOCK_SIDE), lambda b: (b, 0, 0)),
        out_shape=jax.ShapeDtypeStruct((blocks, comps, 4 * BLOCK_SIDE), jnp.float32),
        interpret=INTERPRET,
    )(action)


def step_call(action, ghosts, coefs):
    blocks, comps, cells = action.shape
    return pl.pallas_call(
        _step_kernel,
        grid=(blocks,),
        in_specs=[
            pl.BlockSpec((1, comps, cells), lambda b: (b, 0, 0)),
            pl.BlockSpec((1, comps, 4 * BLOCK_SIDE), lambda b: (b, 0, 0)),
            pl.BlockSpec((4, comps, 1), lambda b: (0, 0, 0)),
        ],
        out_specs=[
            pl.BlockSpec((1, comps, cells), lambda b: (b, 0, 0)),
            pl.BlockSpec((1, comps, 4 * BLOCK_SIDE), lambda b: (b, 0, 0)),
        ],
        out_shape=[
            jax.ShapeDtypeStruct((blocks, comps, cells), jnp.float32),
            jax.ShapeDtypeStruct((blocks, comps, 4 * BLOCK_SIDE), jnp.float32),
        ],
        interpret=INTERPRET,
    )(action, ghosts, coefs)


def _lane_expand(sel):
    eye = jnp.eye(BLOCK_SIDE, dtype=jnp.float32)
    shp = sel.shape
    out = sel.astype(jnp.float32)[..., :, None, :, None] * eye[:, None, :]
    return out.reshape(shp[:-2] + (shp[-2] * BLOCK_SIDE, shp[-1] * BLOCK_SIDE))


def routing(neighbours, blocks, devices):
    me = lax.axis_index("space")
    opp = jnp.array([1, 0, 3, 2], jnp.int32)
    table = lax.all_gather(neighbours, "space", axis=0, tiled=True)
    src = table.reshape(devices, blocks * 4)
    valid = src >= 0
    srcdev = jnp.where(valid, src // blocks, -1)
    r = jnp.arange(blocks * 4)
    earlier = (
        (srcdev[:, None, :] == srcdev[:, :, None])
        & valid[:, None, :]
        & (r[None, None, :] < r[None, :, None])
    )
    pos_all = earlier.sum(-1).astype(jnp.int32)
    remote = valid & (srcdev != jnp.arange(devices)[:, None])
    overflow = jnp.any(remote & (pos_all >= CAPACITY))

    dev_ids = jnp.arange(devices)[:, None, None, None]
    cap_ids = jnp.arange(CAPACITY)[None, :, None, None]
    slot_ids = jnp.arange(blocks)

    nb = neighbours
    ok = nb >= 0
    dest_dev = jnp.where(ok, nb // blocks, -1)
    dest_r = (nb % blocks) * 4 + opp[None, :]
    p_send = pos_all[jnp.clip(dest_dev, 0, devices - 1), jnp.clip(dest_r, 0, blocks * 4 - 1)]
    send_ok = ok & (dest_dev != me) & (p_send < CAPACITY)
    ssel = (
        send_ok[None, None]
        & (dest_dev[None, None] == dev_ids)
        & (p_send[None, None] == cap_ids)
    )
    send_mat = _lane_expand(jnp.transpose(ssel, (0, 2, 3, 1)))

    src_dev = jnp.where(ok, nb // blocks, -1)
    p_recv = lax.dynamic_index_in_dim(pos_all, me, 0, keepdims=False).reshape(blocks, 4)
    rsel_remote = (
        ok[None, None]
        & (src_dev != me)[None, None]
        & (src_dev[None, None] == dev_ids)
        & (p_recv[None, None] == cap_ids)
    )
    rsel_local = (
        (ok & (src_dev == me))[None, None]
        & ((nb % blocks)[None, None] == slot_ids[:, None, None, None])
        & (opp[None, None, None, :] == jnp.arange(4)[None, :, None, None])
    )
    recv_mat = jnp.concatenate(
        [_lane_expand(rsel_remote.reshape(devices, CAPACITY, blocks * 4)),
         _lane_expand(rsel_local.reshape(blocks, 4, blocks * 4))],
        axis=0,
    ).reshape(devices + blocks, 4 * BLOCK_SIDE, blocks, 4 * BLOCK_SIDE)

    all_slots = jnp.arange(devices * blocks)
    fsel = (
        ok[None, None]
        & (nb[None, None] == all_slots[:, None, None, None])
        & (opp[None, None, None, :] == jnp.arange(4)[None, :, None, None])
    )
    return overflow, send_mat, recv_mat, fsel


def exchange(edges, tables):
    overflow, send_mat, recv_mat, fsel = tables
    blocks = edges.shape[0]

    def fast(e):
        send_buf = jnp.einsum("lci,bliq->bcq", e, send_mat, precision=HIGH)
        recv = lax.all_to_all(send_buf, "space", 0, 0, tiled=True)
        srcs = jnp.concatenate([recv, e], axis=0)
        return jnp.einsum("aci,aiLq->Lcq", srcs, recv_mat, precision=HIGH)

    def slow(e):
        gathered = lax.all_gather(e, "space", axis=0, tiled=True)
        nsl = gathered.shape[0]
        fmat = _lane_expand(fsel.reshape(nsl, 4, blocks * 4)).reshape(
            nsl, 4 * BLOCK_SIDE, blocks, 4 * BLOCK_SIDE
        )
        return jnp.einsum("aci,aiLq->Lcq", gathered, fmat, precision=HIGH)

    return lax.cond(overflow, slow, fast, edges)


def interaction_of(spectra, pairs, coupling):
    plus_vals = jnp.take(spectra, pairs[:, 0], axis=1)
    minus_vals = jnp.take(spectra, pairs[:, 1], axis=1)
    return coupling[None, :, None] * (
        spectra * spectra * (plus_vals + minus_vals) - 2.0 * spectra * plus_vals * minus_vals
    )


def shards(devices, action, coupling, active, neighbours, pairs):
    blocks, comp_dev, cell_count = action.shape
    spec_rank = lax.axis_index("spec")
    comp_ids = spec_rank * comp_dev + jnp.arange(comp_dev, dtype=jnp.int32)
    courant_x, courant_y = courant(comp_ids)
    coefs = jnp.stack(
        [
            jnp.maximum(courant_x, 0.0),
            jnp.minimum(courant_x, 0.0),
            jnp.maximum(courant_y, 0.0),
            jnp.minimum(courant_y, 0.0),
        ]
    )[:, :, None]
    tables = routing(neighbours, blocks, devices)
    current_action = action
    edges = edges_call(action)
    for substep_idx in range(SUBSTEPS):
        ghosts = exchange(edges, tables)
        current_action, edges = step_call(current_action, ghosts, coefs)
    mixing = (
        jax.nn.one_hot(pairs[:, 0], SPECTRAL_COUNT, dtype=jnp.float32)
        + jax.nn.one_hot(pairs[:, 1], SPECTRAL_COUNT, dtype=jnp.float32)
        - 2.0 * jnp.eye(SPECTRAL_COUNT, dtype=jnp.float32)
    )
    points = lax.all_to_all(current_action, "spec", split_axis=2, concat_axis=1, tiled=True)
    interaction = interaction_of(points, pairs, coupling)
    change = jnp.einsum("cj,bcx->bjx", mixing, interaction, precision=HIGH)
    result = lax.all_to_all(points + change, "spec", split_axis=1, concat_axis=2, tiled=True)
    return jnp.where(active[:, None, None] > 0, result, 0.0)


def solution(mesh):
    placed = (P("space", "spec", None), P(), P("space"), P("space", None), P())
    return jax.shard_map(
        functools.partial(shards, mesh.shape["space"]), mesh=mesh, in_specs=placed, out_specs=P("space", "spec", None), check_vma=False
    )
```

```python
import functools
import math

import jax
import jax.numpy as jnp
from jax import lax
from jax.experimental import pallas as pl
from jax.experimental.pallas import tpu as pltpu
from jax.sharding import PartitionSpec as P

NDIR = 36
BLOCK_SIDE = 32
BLOCK_CELLS = BLOCK_SIDE * BLOCK_SIDE
SUBSTEPS = 3
SPECTRAL_COUNT = 1296
CAPACITY = 4
HIGH = lax.Precision.HIGHEST
INTERPRET = False

CFL = 0.68


def courant(comp_ids):
    frequency = (comp_ids // NDIR).astype(jnp.float32)
    direction = comp_ids % NDIR
    half_dirs = NDIR // 2
    angles = (
        2.0
        * math.pi
        / NDIR
        * ((2 * (direction % half_dirs) + direction // half_dirs).astype(jnp.float32) + 0.5)
    )
    speeds = CFL * jnp.exp(-frequency * math.log(1.1))
    return (speeds * jnp.cos(angles), speeds * jnp.sin(angles))


def _edge_hits():
    row = lax.broadcasted_iota(jnp.int32, (4 * BLOCK_SIDE, BLOCK_CELLS), 0)
    cell = lax.broadcasted_iota(jnp.int32, (4 * BLOCK_SIDE, BLOCK_CELLS), 1)
    side = row // BLOCK_SIDE
    t = row % BLOCK_SIDE
    target = jnp.where(
        side == 0,
        t * BLOCK_SIDE,
        jnp.where(
            side == 1,
            t * BLOCK_SIDE + BLOCK_SIDE - 1,
            jnp.where(side == 2, t, BLOCK_CELLS - BLOCK_SIDE + t),
        ),
    )
    return side, cell == target


def _edges_of(field, hit):
    return lax.dot_general(
        field,
        hit.astype(jnp.float32),
        (((1,), (1,)), ((), ())),
        precision=HIGH,
        preferred_element_type=jnp.float32,
    )


def _edge_kernel(a_ref, e_ref):
    _, hit = _edge_hits()
    e_ref[0] = _edges_of(a_ref[0], hit)


def _step_kernel(a_ref, g_ref, c_ref, o_ref, e_ref):
    a = a_ref[0]
    g = g_ref[0]
    side, hit = _edge_hits()
    g_we = jnp.dot(g, (hit & (side < 2)).astype(jnp.float32), precision=HIGH,
                   preferred_element_type=jnp.float32)
    g_sn = jnp.dot(g, (hit & (side >= 2)).astype(jnp.float32), precision=HIGH,
                   preferred_element_type=jnp.float32)
    cell = lax.broadcasted_iota(jnp.int32, (1, BLOCK_CELLS), 1)
    x = cell % BLOCK_SIDE
    y = cell // BLOCK_SIDE
    from_west = jnp.where(x == 0, g_we, pltpu.roll(a, 1, 1))
    from_east = jnp.where(x == BLOCK_SIDE - 1, g_we, pltpu.roll(a, BLOCK_CELLS - 1, 1))
    from_south = jnp.where(y == 0, g_sn, pltpu.roll(a, BLOCK_SIDE, 1))
    from_north = jnp.where(y == BLOCK_SIDE - 1, g_sn, pltpu.roll(a, BLOCK_CELLS - BLOCK_SIDE, 1))
    x_plus = c_ref[0]
    x_minus = c_ref[1]
    y_plus = c_ref[2]
    y_minus = c_ref[3]
    new = (
        a
        - (x_plus * (a - from_west) + x_minus * (from_east - a))
        - (y_plus * (a - from_south) + y_minus * (from_north - a))
    )
    o_ref[0] = new
    e_ref[0] = _edges_of(new, hit)


def edges_call(action):
    blocks, comps, cells = action.shape
    return pl.pallas_call(
        _edge_kernel,
        grid=(blocks,),
        in_specs=[pl.BlockSpec((1, comps, cells), lambda b: (b, 0, 0))],
        out_specs=pl.BlockSpec((1, comps, 4 * BLOCK_SIDE), lambda b: (b, 0, 0)),
        out_shape=jax.ShapeDtypeStruct((blocks, comps, 4 * BLOCK_SIDE), jnp.float32),
        interpret=INTERPRET,
    )(action)


def step_call(action, ghosts, coefs):
    blocks, comps, cells = action.shape
    return pl.pallas_call(
        _step_kernel,
        grid=(blocks,),
        in_specs=[
            pl.BlockSpec((1, comps, cells), lambda b: (b, 0, 0)),
            pl.BlockSpec((1, comps, 4 * BLOCK_SIDE), lambda b: (b, 0, 0)),
            pl.BlockSpec((4, comps, 1), lambda b: (0, 0, 0)),
        ],
        out_specs=[
            pl.BlockSpec((1, comps, cells), lambda b: (b, 0, 0)),
            pl.BlockSpec((1, comps, 4 * BLOCK_SIDE), lambda b: (b, 0, 0)),
        ],
        out_shape=[
            jax.ShapeDtypeStruct((blocks, comps, cells), jnp.float32),
            jax.ShapeDtypeStruct((blocks, comps, 4 * BLOCK_SIDE), jnp.float32),
        ],
        interpret=INTERPRET,
    )(action, ghosts, coefs)


def _per_lane(table):
    return jnp.repeat(table, BLOCK_SIDE, axis=1)


def _select_matrix(rows, use, row_of, group_of):
    blocks = use.shape[0]
    shape = (rows, 4 * BLOCK_SIDE, blocks, 4 * BLOCK_SIDE)
    a = lax.broadcasted_iota(jnp.int32, shape, 0)
    i = lax.broadcasted_iota(jnp.int32, shape, 1)
    q = lax.broadcasted_iota(jnp.int32, shape, 3)
    hit = (
        _per_lane(use)[None, None]
        & (_per_lane(row_of)[None, None] == a)
        & (_per_lane(group_of)[None, None] == i // BLOCK_SIDE)
        & (i % BLOCK_SIDE == q % BLOCK_SIDE)
    )
    return hit.astype(jnp.float32)


def routing(neighbours, blocks, devices):
    me = lax.axis_index("space")
    opp = jnp.array([1, 0, 3, 2], jnp.int32)[None, :]
    nb = neighbours
    ok = nb >= 0
    other = jnp.where(ok, nb // blocks, -1)
    own_key = jnp.arange(blocks * 4, dtype=jnp.int32).reshape(blocks, 4)
    src_key = (nb % blocks) * 4 + opp

    def rank(key):
        same = (other.reshape(-1)[None, :] == other.reshape(-1)[:, None]) & ok.reshape(-1)[None, :]
        before = key.reshape(-1)[None, :] < key.reshape(-1)[:, None]
        return (same & before).sum(-1).astype(jnp.int32).reshape(blocks, 4)

    pos_send = rank(own_key)
    pos_recv = rank(src_key)
    remote = ok & (other != me)
    overflow = jnp.any(remote & (pos_send >= CAPACITY)) | jnp.any(remote & (pos_recv >= CAPACITY))
    overflow = lax.pmax(overflow.astype(jnp.int32), "space") > 0

    shape = (devices, blocks, 4 * BLOCK_SIDE, CAPACITY * BLOCK_SIDE)
    b = lax.broadcasted_iota(jnp.int32, shape, 0)
    i = lax.broadcasted_iota(jnp.int32, shape, 2)
    q = lax.broadcasted_iota(jnp.int32, shape, 3)
    send_mat = (
        _per_lane(remote)[None, :, :, None]
        & (_per_lane(other)[None, :, :, None] == b)
        & (_per_lane(pos_send)[None, :, :, None] == q // BLOCK_SIDE)
        & (i % BLOCK_SIDE == q % BLOCK_SIDE)
    ).astype(jnp.float32)

    local = ok & (other == me)
    recv_mat = _select_matrix(
        devices + blocks,
        ok & (local | (pos_recv < CAPACITY)),
        jnp.where(local, devices + nb % blocks, other),
        jnp.where(local, jnp.broadcast_to(opp, nb.shape), pos_recv),
    )
    return overflow, send_mat, recv_mat, (nb, ok, jnp.broadcast_to(opp, nb.shape))


def exchange(edges, tables):
    overflow, send_mat, recv_mat, fallback = tables

    def fast(e):
        send_buf = jnp.einsum("lci,bliq->bcq", e, send_mat, precision=HIGH)
        recv = lax.all_to_all(send_buf, "space", 0, 0, tiled=True)
        srcs = jnp.concatenate([recv, e], axis=0)
        return jnp.einsum("aci,aiLq->Lcq", srcs, recv_mat, precision=HIGH)

    def slow(e):
        nb, ok, opp = fallback
        gathered = lax.all_gather(e, "space", axis=0, tiled=True)
        fmat = _select_matrix(gathered.shape[0], ok, nb, opp)
        return jnp.einsum("aci,aiLq->Lcq", gathered, fmat, precision=HIGH)

    return lax.cond(overflow, slow, fast, edges)


def interaction_of(spectra, pairs, coupling):
    plus_vals = jnp.take(spectra, pairs[:, 0], axis=1)
    minus_vals = jnp.take(spectra, pairs[:, 1], axis=1)
    return coupling[None, :, None] * (
        spectra * spectra * (plus_vals + minus_vals) - 2.0 * spectra * plus_vals * minus_vals
    )


def shards(devices, action, coupling, active, neighbours, pairs):
    blocks, comp_dev, cell_count = action.shape
    spec_rank = lax.axis_index("spec")
    comp_ids = spec_rank * comp_dev + jnp.arange(comp_dev, dtype=jnp.int32)
    courant_x, courant_y = courant(comp_ids)
    coefs = jnp.stack(
        [
            jnp.maximum(courant_x, 0.0),
            jnp.minimum(courant_x, 0.0),
            jnp.maximum(courant_y, 0.0),
            jnp.minimum(courant_y, 0.0),
        ]
    )[:, :, None]
    tables = routing(neighbours, blocks, devices)
    current_action = action
    edges = edges_call(action)
    for substep_idx in range(SUBSTEPS):
        ghosts = exchange(edges, tables)
        current_action, edges = step_call(current_action, ghosts, coefs)
    mixing = (
        jax.nn.one_hot(pairs[:, 0], SPECTRAL_COUNT, dtype=jnp.float32)
        + jax.nn.one_hot(pairs[:, 1], SPECTRAL_COUNT, dtype=jnp.float32)
        - 2.0 * jnp.eye(SPECTRAL_COUNT, dtype=jnp.float32)
    )
    points = lax.all_to_all(current_action, "spec", split_axis=2, concat_axis=1, tiled=True)
    interaction = interaction_of(points, pairs, coupling)
    change = jnp.einsum("cj,bcx->bjx", mixing, interaction, precision=HIGH)
    result = lax.all_to_all(points + change, "spec", split_axis=1, concat_axis=2, tiled=True)
    return jnp.where(active[:, None, None] > 0, result, 0.0)


def solution(mesh):
    placed = (P("space", "spec", None), P(), P("space"), P("space", None), P())
    return jax.shard_map(
        functools.partial(shards, mesh.shape["space"]), mesh=mesh, in_specs=placed, out_specs=P("space", "spec", None), check_vma=False
    )
```

```python
import functools
import math

import jax
import jax.numpy as jnp
from jax import lax
from jax.experimental import pallas as pl
from jax.experimental.pallas import tpu as pltpu
from jax.sharding import PartitionSpec as P

NDIR = 36
BLOCK_SIDE = 32
BLOCK_CELLS = BLOCK_SIDE * BLOCK_SIDE
SUBSTEPS = 3
SPECTRAL_COUNT = 1296
CAPACITY = 4
INTERPRET = False

CFL = 0.68


def courant(comp_ids):
    frequency = (comp_ids // NDIR).astype(jnp.float32)
    direction = comp_ids % NDIR
    half_dirs = NDIR // 2
    angles = (
        2.0
        * math.pi
        / NDIR
        * ((2 * (direction % half_dirs) + direction // half_dirs).astype(jnp.float32) + 0.5)
    )
    speeds = CFL * jnp.exp(-frequency * math.log(1.1))
    return (speeds * jnp.cos(angles), speeds * jnp.sin(angles))


def _split3(x):
    hi = x.astype(jnp.bfloat16)
    rest = x - hi.astype(jnp.float32)
    mid = rest.astype(jnp.bfloat16)
    lo = (rest - mid.astype(jnp.float32)).astype(jnp.bfloat16)
    return hi, mid, lo


def _split3_xla(x):
    hi = lax.reduce_precision(x, exponent_bits=8, mantissa_bits=7)
    rest = x - hi
    mid = lax.reduce_precision(rest, exponent_bits=8, mantissa_bits=7)
    lo = rest - mid
    return tuple(p.astype(jnp.bfloat16) for p in (hi, mid, lo))


def _select_dot(x, sel, dims):
    hi, mid, lo = _split3(x)
    run = lambda part: lax.dot_general(part, sel, (dims, ((), ())), preferred_element_type=jnp.float32)
    return (run(hi) + run(mid)) + run(lo)


def _we_hits():
    row = lax.broadcasted_iota(jnp.int32, (4 * BLOCK_SIDE, BLOCK_CELLS), 0)
    cell = lax.broadcasted_iota(jnp.int32, (4 * BLOCK_SIDE, BLOCK_CELLS), 1)
    side = row // BLOCK_SIDE
    t = row % BLOCK_SIDE
    target = jnp.where(side == 0, t * BLOCK_SIDE, t * BLOCK_SIDE + BLOCK_SIDE - 1)
    return ((cell == target) & (side < 2)).astype(jnp.bfloat16)


def _edges_of(field, we_hit):
    we = _select_dot(field, we_hit, ((1,), (1,)))
    lane = lax.broadcasted_iota(jnp.int32, (1, 4 * BLOCK_SIDE), 1)
    south = pltpu.roll(field[:, : 4 * BLOCK_SIDE], 2 * BLOCK_SIDE, 1)
    north = field[:, BLOCK_CELLS - 4 * BLOCK_SIDE :]
    return jnp.where(lane < 2 * BLOCK_SIDE, we, jnp.where(lane < 3 * BLOCK_SIDE, south, north))


def _edge_kernel(a_ref, e_ref):
    e_ref[0] = _edges_of(a_ref[0], _we_hits())


def _step_kernel(a_ref, g_ref, c_ref, o_ref, e_ref):
    a = a_ref[0]
    g = g_ref[0]
    we_hit = _we_hits()
    g_we = _select_dot(g, we_hit, ((1,), (0,)))
    cell = lax.broadcasted_iota(jnp.int32, (1, BLOCK_CELLS), 1)
    lane = lax.broadcasted_iota(jnp.int32, (1, 4 * BLOCK_SIDE), 1)
    x = cell % BLOCK_SIDE
    tile = 4 * BLOCK_SIDE
    from_west = jnp.where(x == 0, g_we, pltpu.roll(a, 1, 1))
    from_east = jnp.where(x == BLOCK_SIDE - 1, g_we, pltpu.roll(a, BLOCK_CELLS - 1, 1))
    south_in = pltpu.roll(a, BLOCK_SIDE, 1)
    from_south = jnp.concatenate(
        [jnp.where(lane < BLOCK_SIDE, pltpu.roll(g, 2 * BLOCK_SIDE, 1), south_in[:, :tile]),
         south_in[:, tile:]],
        axis=1,
    )
    north_in = pltpu.roll(a, BLOCK_CELLS - BLOCK_SIDE, 1)
    from_north = jnp.concatenate(
        [north_in[:, : BLOCK_CELLS - tile],
         jnp.where(lane >= 3 * BLOCK_SIDE, g, north_in[:, BLOCK_CELLS - tile :])],
        axis=1,
    )
    x_plus = c_ref[0]
    x_minus = c_ref[1]
    y_plus = c_ref[2]
    y_minus = c_ref[3]
    new = (
        a
        - (x_plus * (a - from_west) + x_minus * (from_east - a))
        - (y_plus * (a - from_south) + y_minus * (from_north - a))
    )
    o_ref[0] = new
    e_ref[0] = _edges_of(new, we_hit)


def edges_call(action):
    blocks, comps, cells = action.shape
    return pl.pallas_call(
        _edge_kernel,
        grid=(blocks,),
        in_specs=[pl.BlockSpec((1, comps, cells), lambda b: (b, 0, 0))],
        out_specs=pl.BlockSpec((1, comps, 4 * BLOCK_SIDE), lambda b: (b, 0, 0)),
        out_shape=jax.ShapeDtypeStruct((blocks, comps, 4 * BLOCK_SIDE), jnp.float32),
        interpret=INTERPRET,
    )(action)


def step_call(action, ghosts, coefs):
    blocks, comps, cells = action.shape
    return pl.pallas_call(
        _step_kernel,
        grid=(blocks,),
        in_specs=[
            pl.BlockSpec((1, comps, cells), lambda b: (b, 0, 0)),
            pl.BlockSpec((1, comps, 4 * BLOCK_SIDE), lambda b: (b, 0, 0)),
            pl.BlockSpec((4, comps, 1), lambda b: (0, 0, 0)),
        ],
        out_specs=[
            pl.BlockSpec((1, comps, cells), lambda b: (b, 0, 0)),
            pl.BlockSpec((1, comps, 4 * BLOCK_SIDE), lambda b: (b, 0, 0)),
        ],
        out_shape=[
            jax.ShapeDtypeStruct((blocks, comps, cells), jnp.float32),
            jax.ShapeDtypeStruct((blocks, comps, 4 * BLOCK_SIDE), jnp.float32),
        ],
        interpret=INTERPRET,
    )(action, ghosts, coefs)


def _per_lane(table):
    return jnp.repeat(table, BLOCK_SIDE, axis=1)


def _select_matrix(rows, use, row_of, group_of):
    blocks = use.shape[0]
    shape = (rows, 4 * BLOCK_SIDE, blocks, 4 * BLOCK_SIDE)
    a = lax.broadcasted_iota(jnp.int32, shape, 0)
    i = lax.broadcasted_iota(jnp.int32, shape, 1)
    q = lax.broadcasted_iota(jnp.int32, shape, 3)
    hit = (
        _per_lane(use)[None, None]
        & (_per_lane(row_of)[None, None] == a)
        & (_per_lane(group_of)[None, None] == i // BLOCK_SIDE)
        & (i % BLOCK_SIDE == q % BLOCK_SIDE)
    )
    return hit.astype(jnp.float32)


def routing(neighbours, blocks, devices):
    me = lax.axis_index("space")
    opp = jnp.array([1, 0, 3, 2], jnp.int32)[None, :]
    nb = neighbours
    ok = nb >= 0
    other = jnp.where(ok, nb // blocks, -1)
    own_key = jnp.arange(blocks * 4, dtype=jnp.int32).reshape(blocks, 4)
    src_key = (nb % blocks) * 4 + opp

    def rank(key):
        same = (other.reshape(-1)[None, :] == other.reshape(-1)[:, None]) & ok.reshape(-1)[None, :]
        before = key.reshape(-1)[None, :] < key.reshape(-1)[:, None]
        return (same & before).sum(-1).astype(jnp.int32).reshape(blocks, 4)

    pos_send = rank(own_key)
    pos_recv = rank(src_key)
    remote = ok & (other != me)
    overflow = jnp.any(remote & (pos_send >= CAPACITY)) | jnp.any(remote & (pos_recv >= CAPACITY))
    overflow = lax.pmax(overflow.astype(jnp.int32), "space") > 0

    shape = (devices, blocks, 4 * BLOCK_SIDE, CAPACITY * BLOCK_SIDE)
    b = lax.broadcasted_iota(jnp.int32, shape, 0)
    i = lax.broadcasted_iota(jnp.int32, shape, 2)
    q = lax.broadcasted_iota(jnp.int32, shape, 3)
    send_mat = (
        _per_lane(remote)[None, :, :, None]
        & (_per_lane(other)[None, :, :, None] == b)
        & (_per_lane(pos_send)[None, :, :, None] == q // BLOCK_SIDE)
        & (i % BLOCK_SIDE == q % BLOCK_SIDE)
    ).astype(jnp.float32)

    local = ok & (other == me)
    recv_mat = _select_matrix(
        devices + blocks,
        ok & (local | (pos_recv < CAPACITY)),
        jnp.where(local, devices + nb % blocks, other),
        jnp.where(local, jnp.broadcast_to(opp, nb.shape), pos_recv),
    )
    return overflow, send_mat, recv_mat, (nb, ok, jnp.broadcast_to(opp, nb.shape))


def _split_einsum(spec, x, sel):
    sel = sel.astype(jnp.bfloat16)
    run = lambda part: jnp.einsum(spec, part, sel, preferred_element_type=jnp.float32)
    hi, mid, lo = _split3_xla(x)
    return (run(hi) + run(mid)) + run(lo)


def exchange(edges, tables):
    overflow, send_mat, recv_mat, fallback = tables

    def fast(e):
        send_buf = _split_einsum("lci,bliq->bcq", e, send_mat)
        recv = lax.all_to_all(send_buf, "space", 0, 0, tiled=True)
        srcs = jnp.concatenate([recv, e], axis=0)
        return _split_einsum("aci,aiLq->Lcq", srcs, recv_mat)

    def slow(e):
        nb, ok, opp = fallback
        gathered = lax.all_gather(e, "space", axis=0, tiled=True)
        fmat = _select_matrix(gathered.shape[0], ok, nb, opp)
        return _split_einsum("aci,aiLq->Lcq", gathered, fmat)

    return lax.cond(overflow, slow, fast, edges)


def interaction_of(spectra, pairs, coupling):
    plus_vals = jnp.take(spectra, pairs[:, 0], axis=1)
    minus_vals = jnp.take(spectra, pairs[:, 1], axis=1)
    return coupling[None, :, None] * (
        spectra * spectra * (plus_vals + minus_vals) - 2.0 * spectra * plus_vals * minus_vals
    )


def shards(devices, action, coupling, active, neighbours, pairs):
    blocks, comp_dev, cell_count = action.shape
    spec_rank = lax.axis_index("spec")
    comp_ids = spec_rank * comp_dev + jnp.arange(comp_dev, dtype=jnp.int32)
    courant_x, courant_y = courant(comp_ids)
    coefs = jnp.stack(
        [
            jnp.maximum(courant_x, 0.0),
            jnp.minimum(courant_x, 0.0),
            jnp.maximum(courant_y, 0.0),
            jnp.minimum(courant_y, 0.0),
        ]
    )[:, :, None]
    tables = routing(neighbours, blocks, devices)
    current_action = action
    edges = edges_call(action)
    for substep_idx in range(SUBSTEPS):
        ghosts = exchange(edges, tables)
        current_action, edges = step_call(current_action, ghosts, coefs)
    mixing = (
        jax.nn.one_hot(pairs[:, 0], SPECTRAL_COUNT, dtype=jnp.float32)
        + jax.nn.one_hot(pairs[:, 1], SPECTRAL_COUNT, dtype=jnp.float32)
        - 2.0 * jnp.eye(SPECTRAL_COUNT, dtype=jnp.float32)
    ).astype(jnp.bfloat16)
    points = lax.all_to_all(current_action, "spec", split_axis=2, concat_axis=1, tiled=True)
    interaction = interaction_of(points, pairs, coupling)
    hi, mid, lo = _split3_xla(interaction)
    mix = lambda part: jnp.einsum("cj,bcx->bjx", mixing, part, preferred_element_type=jnp.float32)
    change = (mix(hi) + mix(mid)) + mix(lo)
    result = lax.all_to_all(points + change, "spec", split_axis=1, concat_axis=2, tiled=True)
    return jnp.where(active[:, None, None] > 0, result, 0.0)


def solution(mesh):
    placed = (P("space", "spec", None), P(), P("space"), P("space", None), P())
    return jax.shard_map(
        functools.partial(shards, mesh.shape["space"]), mesh=mesh, in_specs=placed, out_specs=P("space", "spec", None), check_vma=False
    )
```

```python
import functools
import math

import jax
import jax.numpy as jnp
from jax import lax
from jax.experimental import pallas as pl
from jax.experimental.pallas import tpu as pltpu
from jax.sharding import PartitionSpec as P

NDIR = 36
BLOCK_SIDE = 32
BLOCK_CELLS = BLOCK_SIDE * BLOCK_SIDE
SUBSTEPS = 3
SPECTRAL_COUNT = 1296
CAPACITY = 4
INTERPRET = False

CFL = 0.68


def courant(comp_ids):
    frequency = (comp_ids // NDIR).astype(jnp.float32)
    direction = comp_ids % NDIR
    half_dirs = NDIR // 2
    angles = (
        2.0
        * math.pi
        / NDIR
        * ((2 * (direction % half_dirs) + direction // half_dirs).astype(jnp.float32) + 0.5)
    )
    speeds = CFL * jnp.exp(-frequency * math.log(1.1))
    return (speeds * jnp.cos(angles), speeds * jnp.sin(angles))


def _split3(x):
    hi = x.astype(jnp.bfloat16)
    rest = x - hi.astype(jnp.float32)
    mid = rest.astype(jnp.bfloat16)
    lo = (rest - mid.astype(jnp.float32)).astype(jnp.bfloat16)
    return hi, mid, lo


def _split3_xla(x):
    hi = lax.reduce_precision(x, exponent_bits=8, mantissa_bits=7)
    rest = x - hi
    mid = lax.reduce_precision(rest, exponent_bits=8, mantissa_bits=7)
    lo = rest - mid
    return tuple(p.astype(jnp.bfloat16) for p in (hi, mid, lo))


def _select_dot(x, sel, dims):
    hi, mid, lo = _split3(x)
    run = lambda part: lax.dot_general(part, sel, (dims, ((), ())), preferred_element_type=jnp.float32)
    return (run(hi) + run(mid)) + run(lo)


def _we_hits():
    row = lax.broadcasted_iota(jnp.int32, (4 * BLOCK_SIDE, BLOCK_CELLS), 0)
    cell = lax.broadcasted_iota(jnp.int32, (4 * BLOCK_SIDE, BLOCK_CELLS), 1)
    side = row // BLOCK_SIDE
    t = row % BLOCK_SIDE
    target = jnp.where(side == 0, t * BLOCK_SIDE, t * BLOCK_SIDE + BLOCK_SIDE - 1)
    return ((cell == target) & (side < 2)).astype(jnp.bfloat16)


def _edges_of(field, we_hit):
    we = _select_dot(field, we_hit, ((1,), (1,)))
    lane = lax.broadcasted_iota(jnp.int32, (1, 4 * BLOCK_SIDE), 1)
    south = pltpu.roll(field[:, : 4 * BLOCK_SIDE], 2 * BLOCK_SIDE, 1)
    north = field[:, BLOCK_CELLS - 4 * BLOCK_SIDE :]
    return jnp.where(lane < 2 * BLOCK_SIDE, we, jnp.where(lane < 3 * BLOCK_SIDE, south, north))


def _edge_kernel(a_ref, e_ref):
    e_ref[0] = _edges_of(a_ref[0], _we_hits())


def _step_kernel(a_ref, g_ref, c_ref, o_ref, e_ref):
    a = a_ref[0]
    g = g_ref[0]
    we_hit = _we_hits()
    g_we = _select_dot(g, we_hit, ((1,), (0,)))
    cell = lax.broadcasted_iota(jnp.int32, (1, BLOCK_CELLS), 1)
    lane = lax.broadcasted_iota(jnp.int32, (1, 4 * BLOCK_SIDE), 1)
    x = cell % BLOCK_SIDE
    tile = 4 * BLOCK_SIDE
    from_west = jnp.where(x == 0, g_we, pltpu.roll(a, 1, 1))
    from_east = jnp.where(x == BLOCK_SIDE - 1, g_we, pltpu.roll(a, BLOCK_CELLS - 1, 1))
    south_in = pltpu.roll(a, BLOCK_SIDE, 1)
    from_south = jnp.concatenate(
        [jnp.where(lane < BLOCK_SIDE, pltpu.roll(g, 2 * BLOCK_SIDE, 1), south_in[:, :tile]),
         south_in[:, tile:]],
        axis=1,
    )
    north_in = pltpu.roll(a, BLOCK_CELLS - BLOCK_SIDE, 1)
    from_north = jnp.concatenate(
        [north_in[:, : BLOCK_CELLS - tile],
         jnp.where(lane >= 3 * BLOCK_SIDE, g, north_in[:, BLOCK_CELLS - tile :])],
        axis=1,
    )
    x_plus = c_ref[0]
    x_minus = c_ref[1]
    y_plus = c_ref[2]
    y_minus = c_ref[3]
    new = (
        a
        - (x_plus * (a - from_west) + x_minus * (from_east - a))
        - (y_plus * (a - from_south) + y_minus * (from_north - a))
    )
    o_ref[0] = new
    e_ref[0] = _edges_of(new, we_hit)


def edges_call(action):
    blocks, comps, cells = action.shape
    return pl.pallas_call(
        _edge_kernel,
        grid=(blocks,),
        in_specs=[pl.BlockSpec((1, comps, cells), lambda b: (b, 0, 0))],
        out_specs=pl.BlockSpec((1, comps, 4 * BLOCK_SIDE), lambda b: (b, 0, 0)),
        out_shape=jax.ShapeDtypeStruct((blocks, comps, 4 * BLOCK_SIDE), jnp.float32),
        interpret=INTERPRET,
    )(action)


def step_call(action, ghosts, coefs):
    blocks, comps, cells = action.shape
    return pl.pallas_call(
        _step_kernel,
        grid=(blocks,),
        in_specs=[
            pl.BlockSpec((1, comps, cells), lambda b: (b, 0, 0)),
            pl.BlockSpec((1, comps, 4 * BLOCK_SIDE), lambda b: (b, 0, 0)),
            pl.BlockSpec((4, comps, 1), lambda b: (0, 0, 0)),
        ],
        out_specs=[
            pl.BlockSpec((1, comps, cells), lambda b: (b, 0, 0)),
            pl.BlockSpec((1, comps, 4 * BLOCK_SIDE), lambda b: (b, 0, 0)),
        ],
        out_shape=[
            jax.ShapeDtypeStruct((blocks, comps, cells), jnp.float32),
            jax.ShapeDtypeStruct((blocks, comps, 4 * BLOCK_SIDE), jnp.float32),
        ],
        interpret=INTERPRET,
    )(action, ghosts, coefs)


def _per_lane(table):
    return jnp.repeat(table, BLOCK_SIDE, axis=1)


def _select_matrix(rows, use, row_of, group_of):
    blocks = use.shape[0]
    shape = (rows, 4 * BLOCK_SIDE, blocks, 4 * BLOCK_SIDE)
    a = lax.broadcasted_iota(jnp.int32, shape, 0)
    i = lax.broadcasted_iota(jnp.int32, shape, 1)
    q = lax.broadcasted_iota(jnp.int32, shape, 3)
    hit = (
        _per_lane(use)[None, None]
        & (_per_lane(row_of)[None, None] == a)
        & (_per_lane(group_of)[None, None] == i // BLOCK_SIDE)
        & (i % BLOCK_SIDE == q % BLOCK_SIDE)
    )
    return hit.astype(jnp.float32)


def routing(neighbours, blocks, devices):
    me = lax.axis_index("space")
    opp = jnp.array([1, 0, 3, 2], jnp.int32)[None, :]
    nb = neighbours
    ok = nb >= 0
    other = jnp.where(ok, nb // blocks, -1)
    own_key = jnp.arange(blocks * 4, dtype=jnp.int32).reshape(blocks, 4)
    src_key = (nb % blocks) * 4 + opp

    def rank(key):
        same = (other.reshape(-1)[None, :] == other.reshape(-1)[:, None]) & ok.reshape(-1)[None, :]
        before = key.reshape(-1)[None, :] < key.reshape(-1)[:, None]
        return (same & before).sum(-1).astype(jnp.int32).reshape(blocks, 4)

    pos_send = rank(own_key)
    pos_recv = rank(src_key)
    remote = ok & (other != me)
    overflow = jnp.any(remote & (pos_send >= CAPACITY)) | jnp.any(remote & (pos_recv >= CAPACITY))
    overflow = lax.pmax(overflow.astype(jnp.int32), "space") > 0

    shape = (devices, blocks, 4 * BLOCK_SIDE, CAPACITY * BLOCK_SIDE)
    b = lax.broadcasted_iota(jnp.int32, shape, 0)
    i = lax.broadcasted_iota(jnp.int32, shape, 2)
    q = lax.broadcasted_iota(jnp.int32, shape, 3)
    send_mat = (
        _per_lane(remote)[None, :, :, None]
        & (_per_lane(other)[None, :, :, None] == b)
        & (_per_lane(pos_send)[None, :, :, None] == q // BLOCK_SIDE)
        & (i % BLOCK_SIDE == q % BLOCK_SIDE)
    ).astype(jnp.float32)

    local = ok & (other == me)
    recv_mat = _select_matrix(
        devices + blocks,
        ok & (local | (pos_recv < CAPACITY)),
        jnp.where(local, devices + nb % blocks, other),
        jnp.where(local, jnp.broadcast_to(opp, nb.shape), pos_recv),
    )
    return overflow, send_mat, recv_mat, (nb, ok, jnp.broadcast_to(opp, nb.shape))


def _split_einsum(spec, x, sel):
    sel = sel.astype(jnp.bfloat16)
    run = lambda part: jnp.einsum(spec, part, sel, preferred_element_type=jnp.float32)
    hi, mid, lo = _split3_xla(x)
    return (run(hi) + run(mid)) + run(lo)


def exchange(edges, tables):
    overflow, send_mat, recv_mat, fallback = tables

    def fast(e):
        send_buf = _split_einsum("lci,bliq->bcq", e, send_mat)
        recv = lax.all_to_all(send_buf, "space", 0, 0, tiled=True)
        srcs = jnp.concatenate([recv, e], axis=0)
        return jnp.einsum("aci,aiLq->Lcq", srcs, recv_mat, precision=lax.Precision.HIGHEST)

    def slow(e):
        nb, ok, opp = fallback
        gathered = lax.all_gather(e, "space", axis=0, tiled=True)
        fmat = _select_matrix(gathered.shape[0], ok, nb, opp)
        return _split_einsum("aci,aiLq->Lcq", gathered, fmat)

    return lax.cond(overflow, slow, fast, edges)


def interaction_of(spectra, pairs, coupling):
    plus_vals = jnp.take(spectra, pairs[:, 0], axis=1)
    minus_vals = jnp.take(spectra, pairs[:, 1], axis=1)
    return coupling[None, :, None] * (
        spectra * spectra * (plus_vals + minus_vals) - 2.0 * spectra * plus_vals * minus_vals
    )


def shards(devices, action, coupling, active, neighbours, pairs):
    blocks, comp_dev, cell_count = action.shape
    spec_rank = lax.axis_index("spec")
    comp_ids = spec_rank * comp_dev + jnp.arange(comp_dev, dtype=jnp.int32)
    courant_x, courant_y = courant(comp_ids)
    coefs = jnp.stack(
        [
            jnp.maximum(courant_x, 0.0),
            jnp.minimum(courant_x, 0.0),
            jnp.maximum(courant_y, 0.0),
            jnp.minimum(courant_y, 0.0),
        ]
    )[:, :, None]
    tables = routing(neighbours, blocks, devices)
    current_action = action
    edges = edges_call(action)
    for substep_idx in range(SUBSTEPS):
        ghosts = exchange(edges, tables)
        current_action, edges = step_call(current_action, ghosts, coefs)
    mixing = (
        jax.nn.one_hot(pairs[:, 0], SPECTRAL_COUNT, dtype=jnp.float32)
        + jax.nn.one_hot(pairs[:, 1], SPECTRAL_COUNT, dtype=jnp.float32)
        - 2.0 * jnp.eye(SPECTRAL_COUNT, dtype=jnp.float32)
    ).astype(jnp.bfloat16)
    results = []
    for b in range(blocks):
        points = lax.all_to_all(
            current_action[b : b + 1], "spec", split_axis=2, concat_axis=1, tiled=True
        )
        interaction = interaction_of(points, pairs, coupling)
        hi, mid, lo = _split3_xla(interaction)
        mix = lambda part: jnp.einsum("cj,bcx->bjx", mixing, part, preferred_element_type=jnp.float32)
        change = (mix(hi) + mix(mid)) + mix(lo)
        results.append(
            lax.all_to_all(points + change, "spec", split_axis=1, concat_axis=2, tiled=True)
        )
    result = jnp.concatenate(results, axis=0)
    return jnp.where(active[:, None, None] > 0, result, 0.0)


def solution(mesh):
    placed = (P("space", "spec", None), P(), P("space"), P("space", None), P())
    return jax.shard_map(
        functools.partial(shards, mesh.shape["space"]), mesh=mesh, in_specs=placed, out_specs=P("space", "spec", None), check_vma=False
    )
```

```python
import functools
import math

import jax
import jax.numpy as jnp
from jax import lax
from jax.experimental import pallas as pl
from jax.experimental.pallas import tpu as pltpu
from jax.sharding import PartitionSpec as P

NDIR = 36
BLOCK_SIDE = 32
BLOCK_CELLS = BLOCK_SIDE * BLOCK_SIDE
SUBSTEPS = 3
SPECTRAL_COUNT = 1296
CAPACITY = 4
INTERPRET = False

CFL = 0.68


def courant(comp_ids):
    frequency = (comp_ids // NDIR).astype(jnp.float32)
    direction = comp_ids % NDIR
    half_dirs = NDIR // 2
    angles = (
        2.0
        * math.pi
        / NDIR
        * ((2 * (direction % half_dirs) + direction // half_dirs).astype(jnp.float32) + 0.5)
    )
    speeds = CFL * jnp.exp(-frequency * math.log(1.1))
    return (speeds * jnp.cos(angles), speeds * jnp.sin(angles))


def _split3(x):
    hi = x.astype(jnp.bfloat16)
    rest = x - hi.astype(jnp.float32)
    mid = rest.astype(jnp.bfloat16)
    lo = (rest - mid.astype(jnp.float32)).astype(jnp.bfloat16)
    return hi, mid, lo


def _split3_xla(x):
    hi = lax.reduce_precision(x, exponent_bits=8, mantissa_bits=7)
    rest = x - hi
    mid = lax.reduce_precision(rest, exponent_bits=8, mantissa_bits=7)
    lo = rest - mid
    return tuple(p.astype(jnp.bfloat16) for p in (hi, mid, lo))


def _select_dot(x, sel, dims):
    hi, mid, lo = _split3(x)
    run = lambda part: lax.dot_general(part, sel, (dims, ((), ())), preferred_element_type=jnp.float32)
    return (run(hi) + run(mid)) + run(lo)


def _we_hits():
    row = lax.broadcasted_iota(jnp.int32, (4 * BLOCK_SIDE, BLOCK_CELLS), 0)
    cell = lax.broadcasted_iota(jnp.int32, (4 * BLOCK_SIDE, BLOCK_CELLS), 1)
    side = row // BLOCK_SIDE
    t = row % BLOCK_SIDE
    target = jnp.where(side == 0, t * BLOCK_SIDE, t * BLOCK_SIDE + BLOCK_SIDE - 1)
    return ((cell == target) & (side < 2)).astype(jnp.bfloat16)


def _edges_of(field, we_hit):
    we = _select_dot(field, we_hit, ((1,), (1,)))
    lane = lax.broadcasted_iota(jnp.int32, (1, 4 * BLOCK_SIDE), 1)
    south = pltpu.roll(field[:, : 4 * BLOCK_SIDE], 2 * BLOCK_SIDE, 1)
    north = field[:, BLOCK_CELLS - 4 * BLOCK_SIDE :]
    return jnp.where(lane < 2 * BLOCK_SIDE, we, jnp.where(lane < 3 * BLOCK_SIDE, south, north))


def _edge_kernel(a_ref, e_ref):
    e_ref[0] = _edges_of(a_ref[0], _we_hits())


def _step_kernel(a_ref, g_ref, c_ref, o_ref, e_ref):
    a = a_ref[0]
    g = g_ref[0]
    we_hit = _we_hits()
    g_we = _select_dot(g, we_hit, ((1,), (0,)))
    cell = lax.broadcasted_iota(jnp.int32, (1, BLOCK_CELLS), 1)
    lane = lax.broadcasted_iota(jnp.int32, (1, 4 * BLOCK_SIDE), 1)
    x = cell % BLOCK_SIDE
    tile = 4 * BLOCK_SIDE
    from_west = jnp.where(x == 0, g_we, pltpu.roll(a, 1, 1))
    from_east = jnp.where(x == BLOCK_SIDE - 1, g_we, pltpu.roll(a, BLOCK_CELLS - 1, 1))
    south_in = pltpu.roll(a, BLOCK_SIDE, 1)
    from_south = jnp.concatenate(
        [jnp.where(lane < BLOCK_SIDE, pltpu.roll(g, 2 * BLOCK_SIDE, 1), south_in[:, :tile]),
         south_in[:, tile:]],
        axis=1,
    )
    north_in = pltpu.roll(a, BLOCK_CELLS - BLOCK_SIDE, 1)
    from_north = jnp.concatenate(
        [north_in[:, : BLOCK_CELLS - tile],
         jnp.where(lane >= 3 * BLOCK_SIDE, g, north_in[:, BLOCK_CELLS - tile :])],
        axis=1,
    )
    x_plus = c_ref[0]
    x_minus = c_ref[1]
    y_plus = c_ref[2]
    y_minus = c_ref[3]
    new = (
        a
        - (x_plus * (a - from_west) + x_minus * (from_east - a))
        - (y_plus * (a - from_south) + y_minus * (from_north - a))
    )
    o_ref[0] = new
    e_ref[0] = _edges_of(new, we_hit)


def edges_call(action):
    blocks, comps, cells = action.shape
    return pl.pallas_call(
        _edge_kernel,
        grid=(blocks,),
        in_specs=[pl.BlockSpec((1, comps, cells), lambda b: (b, 0, 0))],
        out_specs=pl.BlockSpec((1, comps, 4 * BLOCK_SIDE), lambda b: (b, 0, 0)),
        out_shape=jax.ShapeDtypeStruct((blocks, comps, 4 * BLOCK_SIDE), jnp.float32),
        interpret=INTERPRET,
    )(action)


def step_call(action, ghosts, coefs):
    blocks, comps, cells = action.shape
    return pl.pallas_call(
        _step_kernel,
        grid=(blocks,),
        in_specs=[
            pl.BlockSpec((1, comps, cells), lambda b: (b, 0, 0)),
            pl.BlockSpec((1, comps, 4 * BLOCK_SIDE), lambda b: (b, 0, 0)),
            pl.BlockSpec((4, comps, 1), lambda b: (0, 0, 0)),
        ],
        out_specs=[
            pl.BlockSpec((1, comps, cells), lambda b: (b, 0, 0)),
            pl.BlockSpec((1, comps, 4 * BLOCK_SIDE), lambda b: (b, 0, 0)),
        ],
        out_shape=[
            jax.ShapeDtypeStruct((blocks, comps, cells), jnp.float32),
            jax.ShapeDtypeStruct((blocks, comps, 4 * BLOCK_SIDE), jnp.float32),
        ],
        interpret=INTERPRET,
    )(action, ghosts, coefs)


def _per_lane(table):
    return jnp.repeat(table, BLOCK_SIDE, axis=1)


def _select_matrix(rows, use, row_of, group_of):
    blocks = use.shape[0]
    shape = (rows, 4 * BLOCK_SIDE, blocks, 4 * BLOCK_SIDE)
    a = lax.broadcasted_iota(jnp.int32, shape, 0)
    i = lax.broadcasted_iota(jnp.int32, shape, 1)
    q = lax.broadcasted_iota(jnp.int32, shape, 3)
    hit = (
        _per_lane(use)[None, None]
        & (_per_lane(row_of)[None, None] == a)
        & (_per_lane(group_of)[None, None] == i // BLOCK_SIDE)
        & (i % BLOCK_SIDE == q % BLOCK_SIDE)
    )
    return hit.astype(jnp.float32)


def routing(neighbours, blocks, devices):
    me = lax.axis_index("space")
    opp = jnp.array([1, 0, 3, 2], jnp.int32)[None, :]
    nb = neighbours
    ok = nb >= 0
    other = jnp.where(ok, nb // blocks, -1)
    own_key = jnp.arange(blocks * 4, dtype=jnp.int32).reshape(blocks, 4)
    src_key = (nb % blocks) * 4 + opp

    def rank(key):
        same = (other.reshape(-1)[None, :] == other.reshape(-1)[:, None]) & ok.reshape(-1)[None, :]
        before = key.reshape(-1)[None, :] < key.reshape(-1)[:, None]
        return (same & before).sum(-1).astype(jnp.int32).reshape(blocks, 4)

    pos_send = rank(own_key)
    pos_recv = rank(src_key)
    remote = ok & (other != me)
    overflow = jnp.any(remote & (pos_send >= CAPACITY)) | jnp.any(remote & (pos_recv >= CAPACITY))

    shape = (devices, blocks, 4 * BLOCK_SIDE, CAPACITY * BLOCK_SIDE)
    b = lax.broadcasted_iota(jnp.int32, shape, 0)
    i = lax.broadcasted_iota(jnp.int32, shape, 2)
    q = lax.broadcasted_iota(jnp.int32, shape, 3)
    send_mat = (
        _per_lane(remote)[None, :, :, None]
        & (_per_lane(other)[None, :, :, None] == b)
        & (_per_lane(pos_send)[None, :, :, None] == q // BLOCK_SIDE)
        & (i % BLOCK_SIDE == q % BLOCK_SIDE)
    ).astype(jnp.float32)

    local = ok & (other == me)
    recv_mat = _select_matrix(
        devices + blocks,
        ok & (local | (pos_recv < CAPACITY)),
        jnp.where(local, devices + nb % blocks, other),
        jnp.where(local, jnp.broadcast_to(opp, nb.shape), pos_recv),
    )
    return overflow, send_mat, recv_mat, (nb, ok, jnp.broadcast_to(opp, nb.shape))


def _split_einsum(spec, x, sel):
    sel = sel.astype(jnp.bfloat16)
    run = lambda part: jnp.einsum(spec, part, sel, preferred_element_type=jnp.float32)
    hi, mid, lo = _split3_xla(x)
    return (run(hi) + run(mid)) + run(lo)


def exchange(edges, tables, first):
    overflow, send_mat, recv_mat, fallback = tables
    comps = edges.shape[1]

    def fast(e, flag=None):
        send_buf = _split_einsum("lci,bliq->bcq", e, send_mat)
        if flag is not None:
            row = jnp.broadcast_to(flag.astype(jnp.float32), (send_buf.shape[0], 1, send_buf.shape[2]))
            send_buf = jnp.concatenate([send_buf, row], axis=1)
        recv = lax.all_to_all(send_buf, "space", 0, 0, tiled=True)
        srcs = jnp.concatenate([recv[:, :comps], e], axis=0)
        ghosts = jnp.einsum("aci,aiLq->Lcq", srcs, recv_mat, precision=lax.Precision.HIGHEST)
        return ghosts, recv

    def slow(e):
        nb, ok, opp = fallback
        gathered = lax.all_gather(e, "space", axis=0, tiled=True)
        fmat = _select_matrix(gathered.shape[0], ok, nb, opp)
        return _split_einsum("aci,aiLq->Lcq", gathered, fmat)

    if first:
        ghosts, recv = fast(edges, overflow)
        anywhere = jnp.any(recv[:, comps, 0] > 0.5)
        return lax.cond(anywhere, slow, lambda e: ghosts, edges), anywhere
    return lax.cond(overflow, slow, lambda e: fast(e)[0], edges), overflow


def interaction_of(spectra, pairs, coupling):
    plus_vals = jnp.take(spectra, pairs[:, 0], axis=1)
    minus_vals = jnp.take(spectra, pairs[:, 1], axis=1)
    return coupling[None, :, None] * (
        spectra * spectra * (plus_vals + minus_vals) - 2.0 * spectra * plus_vals * minus_vals
    )


def shards(devices, action, coupling, active, neighbours, pairs):
    blocks, comp_dev, cell_count = action.shape
    spec_rank = lax.axis_index("spec")
    comp_ids = spec_rank * comp_dev + jnp.arange(comp_dev, dtype=jnp.int32)
    courant_x, courant_y = courant(comp_ids)
    coefs = jnp.stack(
        [
            jnp.maximum(courant_x, 0.0),
            jnp.minimum(courant_x, 0.0),
            jnp.maximum(courant_y, 0.0),
            jnp.minimum(courant_y, 0.0),
        ]
    )[:, :, None]
    tables = routing(neighbours, blocks, devices)
    current_action = action
    edges = edges_call(action)
    for substep_idx in range(SUBSTEPS):
        ghosts, anywhere = exchange(edges, tables, substep_idx == 0)
        tables = (anywhere,) + tables[1:]
        current_action, edges = step_call(current_action, ghosts, coefs)
    mixing = (
        jax.nn.one_hot(pairs[:, 0], SPECTRAL_COUNT, dtype=jnp.float32)
        + jax.nn.one_hot(pairs[:, 1], SPECTRAL_COUNT, dtype=jnp.float32)
        - 2.0 * jnp.eye(SPECTRAL_COUNT, dtype=jnp.float32)
    ).astype(jnp.bfloat16)
    points = lax.all_to_all(current_action, "spec", split_axis=2, concat_axis=1, tiled=True)
    interaction = interaction_of(points, pairs, coupling)
    hi, mid, lo = _split3_xla(interaction)
    mix = lambda part: jnp.einsum("cj,bcx->bjx", mixing, part, preferred_element_type=jnp.float32)
    change = (mix(hi) + mix(mid)) + mix(lo)
    result = lax.all_to_all(points + change, "spec", split_axis=1, concat_axis=2, tiled=True)
    return jnp.where(active[:, None, None] > 0, result, 0.0)


def solution(mesh):
    placed = (P("space", "spec", None), P(), P("space"), P("space", None), P())
    return jax.shard_map(
        functools.partial(shards, mesh.shape["space"]), mesh=mesh, in_specs=placed, out_specs=P("space", "spec", None), check_vma=False
    )
```

```python
import functools
import math

import jax
import jax.numpy as jnp
from jax import lax
from jax.experimental import pallas as pl
from jax.experimental.pallas import tpu as pltpu
from jax.sharding import PartitionSpec as P

NDIR = 36
BLOCK_SIDE = 32
BLOCK_CELLS = BLOCK_SIDE * BLOCK_SIDE
SUBSTEPS = 3
SPECTRAL_COUNT = 1296
CAPACITY = 4
INTERPRET = False

CFL = 0.68


def courant(comp_ids):
    frequency = (comp_ids // NDIR).astype(jnp.float32)
    direction = comp_ids % NDIR
    half_dirs = NDIR // 2
    angles = (
        2.0
        * math.pi
        / NDIR
        * ((2 * (direction % half_dirs) + direction // half_dirs).astype(jnp.float32) + 0.5)
    )
    speeds = CFL * jnp.exp(-frequency * math.log(1.1))
    return (speeds * jnp.cos(angles), speeds * jnp.sin(angles))


def _split3(x):
    hi = x.astype(jnp.bfloat16)
    rest = x - hi.astype(jnp.float32)
    mid = rest.astype(jnp.bfloat16)
    lo = (rest - mid.astype(jnp.float32)).astype(jnp.bfloat16)
    return hi, mid, lo


def _split3_xla(x):
    hi = lax.reduce_precision(x, exponent_bits=8, mantissa_bits=7)
    rest = x - hi
    mid = lax.reduce_precision(rest, exponent_bits=8, mantissa_bits=7)
    lo = rest - mid
    return tuple(p.astype(jnp.bfloat16) for p in (hi, mid, lo))


def _select_dot(x, sel, dims):
    hi, mid, lo = _split3(x)
    run = lambda part: lax.dot_general(part, sel, (dims, ((), ())), preferred_element_type=jnp.float32)
    return (run(hi) + run(mid)) + run(lo)


def _we_hits():
    row = lax.broadcasted_iota(jnp.int32, (4 * BLOCK_SIDE, BLOCK_CELLS), 0)
    cell = lax.broadcasted_iota(jnp.int32, (4 * BLOCK_SIDE, BLOCK_CELLS), 1)
    side = row // BLOCK_SIDE
    t = row % BLOCK_SIDE
    target = jnp.where(side == 0, t * BLOCK_SIDE, t * BLOCK_SIDE + BLOCK_SIDE - 1)
    return ((cell == target) & (side < 2)).astype(jnp.bfloat16)


def _edges_of(field, we_hit):
    we = _select_dot(field, we_hit, ((1,), (1,)))
    lane = lax.broadcasted_iota(jnp.int32, (1, 4 * BLOCK_SIDE), 1)
    south = pltpu.roll(field[:, : 4 * BLOCK_SIDE], 2 * BLOCK_SIDE, 1)
    north = field[:, BLOCK_CELLS - 4 * BLOCK_SIDE :]
    return jnp.where(lane < 2 * BLOCK_SIDE, we, jnp.where(lane < 3 * BLOCK_SIDE, south, north))


def _edge_kernel(a_ref, e_ref):
    e_ref[0] = _edges_of(a_ref[0], _we_hits())


def _step_kernel(a_ref, g_ref, c_ref, o_ref, e_ref=None):
    a = a_ref[0]
    g = g_ref[0]
    we_hit = _we_hits()
    g_we = _select_dot(g, we_hit, ((1,), (0,)))
    cell = lax.broadcasted_iota(jnp.int32, (1, BLOCK_CELLS), 1)
    lane = lax.broadcasted_iota(jnp.int32, (1, 4 * BLOCK_SIDE), 1)
    x = cell % BLOCK_SIDE
    tile = 4 * BLOCK_SIDE
    from_west = jnp.where(x == 0, g_we, pltpu.roll(a, 1, 1))
    from_east = jnp.where(x == BLOCK_SIDE - 1, g_we, pltpu.roll(a, BLOCK_CELLS - 1, 1))
    south_in = pltpu.roll(a, BLOCK_SIDE, 1)
    from_south = jnp.concatenate(
        [jnp.where(lane < BLOCK_SIDE, pltpu.roll(g, 2 * BLOCK_SIDE, 1), south_in[:, :tile]),
         south_in[:, tile:]],
        axis=1,
    )
    north_in = pltpu.roll(a, BLOCK_CELLS - BLOCK_SIDE, 1)
    from_north = jnp.concatenate(
        [north_in[:, : BLOCK_CELLS - tile],
         jnp.where(lane >= 3 * BLOCK_SIDE, g, north_in[:, BLOCK_CELLS - tile :])],
        axis=1,
    )
    x_plus = c_ref[0]
    x_minus = c_ref[1]
    y_plus = c_ref[2]
    y_minus = c_ref[3]
    new = (
        a
        - (x_plus * (a - from_west) + x_minus * (from_east - a))
        - (y_plus * (a - from_south) + y_minus * (from_north - a))
    )
    if e_ref is None:
        chunk = o_ref.shape[-1]
        for k in range(o_ref.shape[0]):
            o_ref[k, 0] = new[:, k * chunk : (k + 1) * chunk]
    else:
        o_ref[0] = new
        e_ref[0] = _edges_of(new, we_hit)


def last_step_call(action, ghosts, coefs, parts):
    blocks, comps, cells = action.shape
    chunk = cells // parts
    return pl.pallas_call(
        _step_kernel,
        grid=(blocks,),
        in_specs=[
            pl.BlockSpec((1, comps, cells), lambda b: (b, 0, 0)),
            pl.BlockSpec((1, comps, 4 * BLOCK_SIDE), lambda b: (b, 0, 0)),
            pl.BlockSpec((4, comps, 1), lambda b: (0, 0, 0)),
        ],
        out_specs=pl.BlockSpec((parts, 1, comps, chunk), lambda b: (0, b, 0, 0)),
        out_shape=jax.ShapeDtypeStruct((parts, blocks, comps, chunk), jnp.float32),
        interpret=INTERPRET,
    )(action, ghosts, coefs)


def edges_call(action):
    blocks, comps, cells = action.shape
    return pl.pallas_call(
        _edge_kernel,
        grid=(blocks,),
        in_specs=[pl.BlockSpec((1, comps, cells), lambda b: (b, 0, 0))],
        out_specs=pl.BlockSpec((1, comps, 4 * BLOCK_SIDE), lambda b: (b, 0, 0)),
        out_shape=jax.ShapeDtypeStruct((blocks, comps, 4 * BLOCK_SIDE), jnp.float32),
        interpret=INTERPRET,
    )(action)


def step_call(action, ghosts, coefs):
    blocks, comps, cells = action.shape
    return pl.pallas_call(
        _step_kernel,
        grid=(blocks,),
        in_specs=[
            pl.BlockSpec((1, comps, cells), lambda b: (b, 0, 0)),
            pl.BlockSpec((1, comps, 4 * BLOCK_SIDE), lambda b: (b, 0, 0)),
            pl.BlockSpec((4, comps, 1), lambda b: (0, 0, 0)),
        ],
        out_specs=[
            pl.BlockSpec((1, comps, cells), lambda b: (b, 0, 0)),
            pl.BlockSpec((1, comps, 4 * BLOCK_SIDE), lambda b: (b, 0, 0)),
        ],
        out_shape=[
            jax.ShapeDtypeStruct((blocks, comps, cells), jnp.float32),
            jax.ShapeDtypeStruct((blocks, comps, 4 * BLOCK_SIDE), jnp.float32),
        ],
        interpret=INTERPRET,
    )(action, ghosts, coefs)


def _per_lane(table):
    return jnp.repeat(table, BLOCK_SIDE, axis=1)


def _select_matrix(rows, use, row_of, group_of):
    blocks = use.shape[0]
    shape = (rows, 4 * BLOCK_SIDE, blocks, 4 * BLOCK_SIDE)
    a = lax.broadcasted_iota(jnp.int32, shape, 0)
    i = lax.broadcasted_iota(jnp.int32, shape, 1)
    q = lax.broadcasted_iota(jnp.int32, shape, 3)
    hit = (
        _per_lane(use)[None, None]
        & (_per_lane(row_of)[None, None] == a)
        & (_per_lane(group_of)[None, None] == i // BLOCK_SIDE)
        & (i % BLOCK_SIDE == q % BLOCK_SIDE)
    )
    return hit.astype(jnp.float32)


def routing(neighbours, blocks, devices):
    me = lax.axis_index("space")
    opp = jnp.array([1, 0, 3, 2], jnp.int32)[None, :]
    nb = neighbours
    ok = nb >= 0
    other = jnp.where(ok, nb // blocks, -1)
    own_key = jnp.arange(blocks * 4, dtype=jnp.int32).reshape(blocks, 4)
    src_key = (nb % blocks) * 4 + opp

    def rank(key):
        same = (other.reshape(-1)[None, :] == other.reshape(-1)[:, None]) & ok.reshape(-1)[None, :]
        before = key.reshape(-1)[None, :] < key.reshape(-1)[:, None]
        return (same & before).sum(-1).astype(jnp.int32).reshape(blocks, 4)

    pos_send = rank(own_key)
    pos_recv = rank(src_key)
    remote = ok & (other != me)
    overflow = jnp.any(remote & (pos_send >= CAPACITY)) | jnp.any(remote & (pos_recv >= CAPACITY))

    shape = (devices, blocks, 4 * BLOCK_SIDE, CAPACITY * BLOCK_SIDE)
    b = lax.broadcasted_iota(jnp.int32, shape, 0)
    i = lax.broadcasted_iota(jnp.int32, shape, 2)
    q = lax.broadcasted_iota(jnp.int32, shape, 3)
    send_mat = (
        _per_lane(remote)[None, :, :, None]
        & (_per_lane(other)[None, :, :, None] == b)
        & (_per_lane(pos_send)[None, :, :, None] == q // BLOCK_SIDE)
        & (i % BLOCK_SIDE == q % BLOCK_SIDE)
    ).astype(jnp.float32)

    local = ok & (other == me)
    recv_mat = _select_matrix(
        devices + blocks,
        ok & (local | (pos_recv < CAPACITY)),
        jnp.where(local, devices + nb % blocks, other),
        jnp.where(local, jnp.broadcast_to(opp, nb.shape), pos_recv),
    )
    return overflow, send_mat, recv_mat, (nb, ok, jnp.broadcast_to(opp, nb.shape))


def _split_einsum(spec, x, sel):
    sel = sel.astype(jnp.bfloat16)
    run = lambda part: jnp.einsum(spec, part, sel, preferred_element_type=jnp.float32)
    hi, mid, lo = _split3_xla(x)
    return (run(hi) + run(mid)) + run(lo)


def exchange(edges, tables, first):
    overflow, send_mat, recv_mat, fallback = tables
    comps = edges.shape[1]

    def fast(e, flag=None):
        send_buf = _split_einsum("lci,bliq->bcq", e, send_mat)
        if flag is not None:
            row = jnp.broadcast_to(flag.astype(jnp.float32), (send_buf.shape[0], 1, send_buf.shape[2]))
            send_buf = jnp.concatenate([send_buf, row], axis=1)
        recv = lax.all_to_all(send_buf, "space", 0, 0, tiled=True)
        srcs = jnp.concatenate([recv[:, :comps], e], axis=0)
        ghosts = jnp.einsum("aci,aiLq->Lcq", srcs, recv_mat, precision=lax.Precision.HIGHEST)
        return ghosts, recv

    def slow(e):
        nb, ok, opp = fallback
        gathered = lax.all_gather(e, "space", axis=0, tiled=True)
        fmat = _select_matrix(gathered.shape[0], ok, nb, opp)
        return _split_einsum("aci,aiLq->Lcq", gathered, fmat)

    if first:
        ghosts, recv = fast(edges, overflow)
        anywhere = jnp.any(recv[:, comps, 0] > 0.5)
        return lax.cond(anywhere, slow, lambda e: ghosts, edges), anywhere
    return lax.cond(overflow, slow, lambda e: fast(e)[0], edges), overflow


def interaction_of(spectra, pairs, coupling):
    plus_vals = jnp.take(spectra, pairs[:, 0], axis=1)
    minus_vals = jnp.take(spectra, pairs[:, 1], axis=1)
    return coupling[None, :, None] * (
        spectra * spectra * (plus_vals + minus_vals) - 2.0 * spectra * plus_vals * minus_vals
    )


def shards(devices, parts, action, coupling, active, neighbours, pairs):
    blocks, comp_dev, cell_count = action.shape
    spec_rank = lax.axis_index("spec")
    comp_ids = spec_rank * comp_dev + jnp.arange(comp_dev, dtype=jnp.int32)
    courant_x, courant_y = courant(comp_ids)
    coefs = jnp.stack(
        [
            jnp.maximum(courant_x, 0.0),
            jnp.minimum(courant_x, 0.0),
            jnp.maximum(courant_y, 0.0),
            jnp.minimum(courant_y, 0.0),
        ]
    )[:, :, None]
    tables = routing(neighbours, blocks, devices)
    current_action = action
    edges = edges_call(action)
    for substep_idx in range(SUBSTEPS):
        ghosts, anywhere = exchange(edges, tables, substep_idx == 0)
        tables = (anywhere,) + tables[1:]
        if substep_idx < SUBSTEPS - 1:
            current_action, edges = step_call(current_action, ghosts, coefs)
        else:
            chunked = last_step_call(current_action, ghosts, coefs, parts)
    mixing = (
        jax.nn.one_hot(pairs[:, 0], SPECTRAL_COUNT, dtype=jnp.float32)
        + jax.nn.one_hot(pairs[:, 1], SPECTRAL_COUNT, dtype=jnp.float32)
        - 2.0 * jnp.eye(SPECTRAL_COUNT, dtype=jnp.float32)
    ).astype(jnp.bfloat16)
    arrived = lax.all_to_all(chunked, "spec", split_axis=0, concat_axis=0, tiled=True)
    points = jnp.transpose(arrived, (1, 0, 2, 3)).reshape(blocks, parts * comp_dev, -1)
    interaction = interaction_of(points, pairs, coupling)
    hi, mid, lo = _split3_xla(interaction)
    mix = lambda part: jnp.einsum("cj,bcx->bjx", mixing, part, preferred_element_type=jnp.float32)
    change = (mix(hi) + mix(mid)) + mix(lo)
    evolved = (points + change).reshape(blocks, parts, comp_dev, -1)
    back = lax.all_to_all(jnp.transpose(evolved, (1, 0, 2, 3)), "spec", 0, 0, tiled=True)
    result = jnp.transpose(back, (1, 2, 0, 3)).reshape(blocks, comp_dev, cell_count)
    return jnp.where(active[:, None, None] > 0, result, 0.0)


def solution(mesh):
    placed = (P("space", "spec", None), P(), P("space"), P("space", None), P())
    return jax.shard_map(
        functools.partial(shards, mesh.shape["space"], mesh.shape["spec"]), mesh=mesh, in_specs=placed, out_specs=P("space", "spec", None), check_vma=False
    )
```

```python
import functools
import math

import jax
import jax.numpy as jnp
from jax import lax
from jax.experimental import pallas as pl
from jax.experimental.pallas import tpu as pltpu
from jax.sharding import PartitionSpec as P

NDIR = 36
BLOCK_SIDE = 32
BLOCK_CELLS = BLOCK_SIDE * BLOCK_SIDE
SUBSTEPS = 3
SPECTRAL_COUNT = 1296
CAPACITY = 4
INTERPRET = False

CFL = 0.68


def courant(comp_ids):
    frequency = (comp_ids // NDIR).astype(jnp.float32)
    direction = comp_ids % NDIR
    half_dirs = NDIR // 2
    angles = (
        2.0
        * math.pi
        / NDIR
        * ((2 * (direction % half_dirs) + direction // half_dirs).astype(jnp.float32) + 0.5)
    )
    speeds = CFL * jnp.exp(-frequency * math.log(1.1))
    return (speeds * jnp.cos(angles), speeds * jnp.sin(angles))


def _split3(x):
    hi = x.astype(jnp.bfloat16)
    rest = x - hi.astype(jnp.float32)
    mid = rest.astype(jnp.bfloat16)
    lo = (rest - mid.astype(jnp.float32)).astype(jnp.bfloat16)
    return hi, mid, lo


def _split3_xla(x):
    hi = lax.reduce_precision(x, exponent_bits=8, mantissa_bits=7)
    rest = x - hi
    mid = lax.reduce_precision(rest, exponent_bits=8, mantissa_bits=7)
    lo = rest - mid
    return tuple(p.astype(jnp.bfloat16) for p in (hi, mid, lo))


def _select_dot(x, sel, dims):
    hi, mid, lo = _split3(x)
    run = lambda part: lax.dot_general(part, sel, (dims, ((), ())), preferred_element_type=jnp.float32)
    return (run(hi) + run(mid)) + run(lo)


def _we_hits():
    row = lax.broadcasted_iota(jnp.int32, (4 * BLOCK_SIDE, BLOCK_CELLS), 0)
    cell = lax.broadcasted_iota(jnp.int32, (4 * BLOCK_SIDE, BLOCK_CELLS), 1)
    side = row // BLOCK_SIDE
    t = row % BLOCK_SIDE
    target = jnp.where(side == 0, t * BLOCK_SIDE, t * BLOCK_SIDE + BLOCK_SIDE - 1)
    return ((cell == target) & (side < 2)).astype(jnp.bfloat16)


def _edges_of(field, we_hit):
    we = _select_dot(field, we_hit, ((1,), (1,)))
    lane = lax.broadcasted_iota(jnp.int32, (1, 4 * BLOCK_SIDE), 1)
    south = pltpu.roll(field[:, : 4 * BLOCK_SIDE], 2 * BLOCK_SIDE, 1)
    north = field[:, BLOCK_CELLS - 4 * BLOCK_SIDE :]
    return jnp.where(lane < 2 * BLOCK_SIDE, we, jnp.where(lane < 3 * BLOCK_SIDE, south, north))


def _edge_kernel(a_ref, e_ref):
    e_ref[0] = _edges_of(a_ref[0], _we_hits())


def _step_kernel(a_ref, g_ref, c_ref, o_ref, e_ref=None):
    a = a_ref[0]
    g = g_ref[0]
    we_hit = _we_hits()
    g_we = _select_dot(g, we_hit, ((1,), (0,)))
    cell = lax.broadcasted_iota(jnp.int32, (1, BLOCK_CELLS), 1)
    lane = lax.broadcasted_iota(jnp.int32, (1, 4 * BLOCK_SIDE), 1)
    x = cell % BLOCK_SIDE
    tile = 4 * BLOCK_SIDE
    from_west = jnp.where(x == 0, g_we, pltpu.roll(a, 1, 1))
    from_east = jnp.where(x == BLOCK_SIDE - 1, g_we, pltpu.roll(a, BLOCK_CELLS - 1, 1))
    south_in = pltpu.roll(a, BLOCK_SIDE, 1)
    from_south = jnp.concatenate(
        [jnp.where(lane < BLOCK_SIDE, pltpu.roll(g, 2 * BLOCK_SIDE, 1), south_in[:, :tile]),
         south_in[:, tile:]],
        axis=1,
    )
    north_in = pltpu.roll(a, BLOCK_CELLS - BLOCK_SIDE, 1)
    from_north = jnp.concatenate(
        [north_in[:, : BLOCK_CELLS - tile],
         jnp.where(lane >= 3 * BLOCK_SIDE, g, north_in[:, BLOCK_CELLS - tile :])],
        axis=1,
    )
    x_plus = c_ref[0]
    x_minus = c_ref[1]
    y_plus = c_ref[2]
    y_minus = c_ref[3]
    new = (
        a
        - (x_plus * (a - from_west) + x_minus * (from_east - a))
        - (y_plus * (a - from_south) + y_minus * (from_north - a))
    )
    if e_ref is None:
        chunk = o_ref.shape[-1]
        for k in range(o_ref.shape[0]):
            o_ref[k, 0] = new[:, k * chunk : (k + 1) * chunk]
    else:
        o_ref[0] = new
        e_ref[0] = _edges_of(new, we_hit)


def last_step_call(action, ghosts, coefs, parts):
    blocks, comps, cells = action.shape
    chunk = cells // parts
    return pl.pallas_call(
        _step_kernel,
        grid=(blocks,),
        in_specs=[
            pl.BlockSpec((1, comps, cells), lambda b: (b, 0, 0)),
            pl.BlockSpec((1, comps, 4 * BLOCK_SIDE), lambda b: (b, 0, 0)),
            pl.BlockSpec((4, comps, 1), lambda b: (0, 0, 0)),
        ],
        out_specs=pl.BlockSpec((parts, 1, comps, chunk), lambda b: (0, b, 0, 0)),
        out_shape=jax.ShapeDtypeStruct((parts, blocks, comps, chunk), jnp.float32),
        interpret=INTERPRET,
    )(action, ghosts, coefs)


def edges_call(action):
    blocks, comps, cells = action.shape
    return pl.pallas_call(
        _edge_kernel,
        grid=(blocks,),
        in_specs=[pl.BlockSpec((1, comps, cells), lambda b: (b, 0, 0))],
        out_specs=pl.BlockSpec((1, comps, 4 * BLOCK_SIDE), lambda b: (b, 0, 0)),
        out_shape=jax.ShapeDtypeStruct((blocks, comps, 4 * BLOCK_SIDE), jnp.float32),
        interpret=INTERPRET,
    )(action)


def step_call(action, ghosts, coefs):
    blocks, comps, cells = action.shape
    return pl.pallas_call(
        _step_kernel,
        grid=(blocks,),
        in_specs=[
            pl.BlockSpec((1, comps, cells), lambda b: (b, 0, 0)),
            pl.BlockSpec((1, comps, 4 * BLOCK_SIDE), lambda b: (b, 0, 0)),
            pl.BlockSpec((4, comps, 1), lambda b: (0, 0, 0)),
        ],
        out_specs=[
            pl.BlockSpec((1, comps, cells), lambda b: (b, 0, 0)),
            pl.BlockSpec((1, comps, 4 * BLOCK_SIDE), lambda b: (b, 0, 0)),
        ],
        out_shape=[
            jax.ShapeDtypeStruct((blocks, comps, cells), jnp.float32),
            jax.ShapeDtypeStruct((blocks, comps, 4 * BLOCK_SIDE), jnp.float32),
        ],
        interpret=INTERPRET,
    )(action, ghosts, coefs)


def _per_lane(table):
    return jnp.repeat(table, BLOCK_SIDE, axis=1)


def _select_matrix(rows, use, row_of, group_of):
    blocks = use.shape[0]
    shape = (rows, 4 * BLOCK_SIDE, blocks, 4 * BLOCK_SIDE)
    a = lax.broadcasted_iota(jnp.int32, shape, 0)
    i = lax.broadcasted_iota(jnp.int32, shape, 1)
    q = lax.broadcasted_iota(jnp.int32, shape, 3)
    hit = (
        _per_lane(use)[None, None]
        & (_per_lane(row_of)[None, None] == a)
        & (_per_lane(group_of)[None, None] == i // BLOCK_SIDE)
        & (i % BLOCK_SIDE == q % BLOCK_SIDE)
    )
    return hit.astype(jnp.float32)


def routing(neighbours, blocks, devices):
    me = lax.axis_index("space")
    opp = jnp.array([1, 0, 3, 2], jnp.int32)[None, :]
    nb = neighbours
    ok = nb >= 0
    other = jnp.where(ok, nb // blocks, -1)
    own_key = jnp.arange(blocks * 4, dtype=jnp.int32).reshape(blocks, 4)
    src_key = (nb % blocks) * 4 + opp

    def rank(key):
        same = (other.reshape(-1)[None, :] == other.reshape(-1)[:, None]) & ok.reshape(-1)[None, :]
        before = key.reshape(-1)[None, :] < key.reshape(-1)[:, None]
        return (same & before).sum(-1).astype(jnp.int32).reshape(blocks, 4)

    pos_send = rank(own_key)
    pos_recv = rank(src_key)
    remote = ok & (other != me)
    overflow = jnp.any(remote & (pos_send >= CAPACITY)) | jnp.any(remote & (pos_recv >= CAPACITY))

    shape = (devices, blocks, 4 * BLOCK_SIDE, CAPACITY * BLOCK_SIDE)
    b = lax.broadcasted_iota(jnp.int32, shape, 0)
    i = lax.broadcasted_iota(jnp.int32, shape, 2)
    q = lax.broadcasted_iota(jnp.int32, shape, 3)
    send_mat = (
        _per_lane(remote)[None, :, :, None]
        & (_per_lane(other)[None, :, :, None] == b)
        & (_per_lane(pos_send)[None, :, :, None] == q // BLOCK_SIDE)
        & (i % BLOCK_SIDE == q % BLOCK_SIDE)
    ).astype(jnp.float32)

    local = ok & (other == me)
    recv_mat = _select_matrix(
        devices + blocks,
        ok & (local | (pos_recv < CAPACITY)),
        jnp.where(local, devices + nb % blocks, other),
        jnp.where(local, jnp.broadcast_to(opp, nb.shape), pos_recv),
    )
    return overflow, send_mat, recv_mat, (nb, ok, jnp.broadcast_to(opp, nb.shape))


def _split_einsum(spec, x, sel):
    sel = sel.astype(jnp.bfloat16)
    run = lambda part: jnp.einsum(spec, part, sel, preferred_element_type=jnp.float32)
    hi, mid, lo = _split3_xla(x)
    return (run(hi) + run(mid)) + run(lo)


def exchange_fast(edges, tables, flag=None):
    _, send_mat, recv_mat, _ = tables
    comps = edges.shape[1]
    send_buf = _split_einsum("lci,bliq->bcq", edges, send_mat)
    if flag is not None:
        row = jnp.broadcast_to(flag.astype(jnp.float32), (send_buf.shape[0], 1, send_buf.shape[2]))
        send_buf = jnp.concatenate([send_buf, row], axis=1)
    recv = lax.all_to_all(send_buf, "space", 0, 0, tiled=True)
    srcs = jnp.concatenate([recv[:, :comps], edges], axis=0)
    ghosts = jnp.einsum("aci,aiLq->Lcq", srcs, recv_mat, precision=lax.Precision.HIGHEST)
    if flag is None:
        return ghosts
    return ghosts, jnp.any(recv[:, comps, 0] > 0.5)


def exchange_slow(edges, tables):
    nb, ok, opp = tables[3]
    gathered = lax.all_gather(edges, "space", axis=0, tiled=True)
    fmat = _select_matrix(gathered.shape[0], ok, nb, opp)
    return _split_einsum("aci,aiLq->Lcq", gathered, fmat)


def interaction_of(spectra, pairs, coupling):
    plus_vals = jnp.take(spectra, pairs[:, 0], axis=1)
    minus_vals = jnp.take(spectra, pairs[:, 1], axis=1)
    return coupling[None, :, None] * (
        spectra * spectra * (plus_vals + minus_vals) - 2.0 * spectra * plus_vals * minus_vals
    )


def shards(devices, parts, action, coupling, active, neighbours, pairs):
    blocks, comp_dev, cell_count = action.shape
    spec_rank = lax.axis_index("spec")
    comp_ids = spec_rank * comp_dev + jnp.arange(comp_dev, dtype=jnp.int32)
    courant_x, courant_y = courant(comp_ids)
    coefs = jnp.stack(
        [
            jnp.maximum(courant_x, 0.0),
            jnp.minimum(courant_x, 0.0),
            jnp.maximum(courant_y, 0.0),
            jnp.minimum(courant_y, 0.0),
        ]
    )[:, :, None]
    tables = routing(neighbours, blocks, devices)
    edges = edges_call(action)
    ghosts, anywhere = exchange_fast(edges, tables, tables[0])

    def substeps(first_ghosts, exchange):
        current_action, next_edges = step_call(action, first_ghosts, coefs)
        for substep_idx in range(1, SUBSTEPS - 1):
            current_action, next_edges = step_call(
                current_action, exchange(next_edges, tables), coefs
            )
        return last_step_call(current_action, exchange(next_edges, tables), coefs, parts)

    chunked = lax.cond(
        anywhere,
        lambda g, e: substeps(exchange_slow(e, tables), exchange_slow),
        lambda g, e: substeps(g, exchange_fast),
        ghosts,
        edges,
    )
    mixing = (
        jax.nn.one_hot(pairs[:, 0], SPECTRAL_COUNT, dtype=jnp.float32)
        + jax.nn.one_hot(pairs[:, 1], SPECTRAL_COUNT, dtype=jnp.float32)
        - 2.0 * jnp.eye(SPECTRAL_COUNT, dtype=jnp.float32)
    ).astype(jnp.bfloat16)
    arrived = lax.all_to_all(chunked, "spec", split_axis=0, concat_axis=0, tiled=True)
    points = jnp.transpose(arrived, (1, 0, 2, 3)).reshape(blocks, parts * comp_dev, -1)
    interaction = interaction_of(points, pairs, coupling)
    hi, mid, lo = _split3_xla(interaction)
    mix = lambda part: jnp.einsum("cj,bcx->bjx", mixing, part, preferred_element_type=jnp.float32)
    change = (mix(hi) + mix(mid)) + mix(lo)
    evolved = (points + change).reshape(blocks, parts, comp_dev, -1)
    back = lax.all_to_all(jnp.transpose(evolved, (1, 0, 2, 3)), "spec", 0, 0, tiled=True)
    result = jnp.transpose(back, (1, 2, 0, 3)).reshape(blocks, comp_dev, cell_count)
    return jnp.where(active[:, None, None] > 0, result, 0.0)


def solution(mesh):
    placed = (P("space", "spec", None), P(), P("space"), P("space", None), P())
    return jax.shard_map(
        functools.partial(shards, mesh.shape["space"], mesh.shape["spec"]), mesh=mesh, in_specs=placed, out_specs=P("space", "spec", None), check_vma=False
    )
```

```python
import functools
import math

import jax
import jax.numpy as jnp
from jax import lax
from jax.experimental import pallas as pl
from jax.experimental.pallas import tpu as pltpu
from jax.sharding import PartitionSpec as P

NDIR = 36
BLOCK_SIDE = 32
BLOCK_CELLS = BLOCK_SIDE * BLOCK_SIDE
SUBSTEPS = 3
SPECTRAL_COUNT = 1296
CAPACITY = 4
INTERPRET = False

CFL = 0.68


def courant(comp_ids):
    frequency = (comp_ids // NDIR).astype(jnp.float32)
    direction = comp_ids % NDIR
    half_dirs = NDIR // 2
    angles = (
        2.0
        * math.pi
        / NDIR
        * ((2 * (direction % half_dirs) + direction // half_dirs).astype(jnp.float32) + 0.5)
    )
    speeds = CFL * jnp.exp(-frequency * math.log(1.1))
    return (speeds * jnp.cos(angles), speeds * jnp.sin(angles))


def _split3(x):
    hi = x.astype(jnp.bfloat16)
    rest = x - hi.astype(jnp.float32)
    mid = rest.astype(jnp.bfloat16)
    lo = (rest - mid.astype(jnp.float32)).astype(jnp.bfloat16)
    return hi, mid, lo


def _split3_xla(x):
    hi = lax.reduce_precision(x, exponent_bits=8, mantissa_bits=7)
    rest = x - hi
    mid = lax.reduce_precision(rest, exponent_bits=8, mantissa_bits=7)
    lo = rest - mid
    return tuple(p.astype(jnp.bfloat16) for p in (hi, mid, lo))


def _select_dot(x, sel, dims):
    hi, mid, lo = _split3(x)
    run = lambda part: lax.dot_general(part, sel, (dims, ((), ())), preferred_element_type=jnp.float32)
    return (run(hi) + run(mid)) + run(lo)


def _we_hits():
    row = lax.broadcasted_iota(jnp.int32, (4 * BLOCK_SIDE, BLOCK_CELLS), 0)
    cell = lax.broadcasted_iota(jnp.int32, (4 * BLOCK_SIDE, BLOCK_CELLS), 1)
    side = row // BLOCK_SIDE
    t = row % BLOCK_SIDE
    target = jnp.where(side == 0, t * BLOCK_SIDE, t * BLOCK_SIDE + BLOCK_SIDE - 1)
    return ((cell == target) & (side < 2)).astype(jnp.bfloat16)


def _edges_of(field, we_hit):
    we = _select_dot(field, we_hit, ((1,), (1,)))
    lane = lax.broadcasted_iota(jnp.int32, (1, 4 * BLOCK_SIDE), 1)
    south = pltpu.roll(field[:, : 4 * BLOCK_SIDE], 2 * BLOCK_SIDE, 1)
    north = field[:, BLOCK_CELLS - 4 * BLOCK_SIDE :]
    return jnp.where(lane < 2 * BLOCK_SIDE, we, jnp.where(lane < 3 * BLOCK_SIDE, south, north))


def _edge_kernel(a_ref, e_ref):
    e_ref[0] = _edges_of(a_ref[0], _we_hits())


def _step_kernel(a_ref, g_ref, c_ref, o_ref, e_ref=None):
    a = a_ref[0]
    g = g_ref[0]
    we_hit = _we_hits()
    g_we = _select_dot(g, we_hit, ((1,), (0,)))
    cell = lax.broadcasted_iota(jnp.int32, (1, BLOCK_CELLS), 1)
    lane = lax.broadcasted_iota(jnp.int32, (1, 4 * BLOCK_SIDE), 1)
    x = cell % BLOCK_SIDE
    tile = 4 * BLOCK_SIDE
    from_west = jnp.where(x == 0, g_we, pltpu.roll(a, 1, 1))
    from_east = jnp.where(x == BLOCK_SIDE - 1, g_we, pltpu.roll(a, BLOCK_CELLS - 1, 1))
    south_in = pltpu.roll(a, BLOCK_SIDE, 1)
    from_south = jnp.concatenate(
        [jnp.where(lane < BLOCK_SIDE, pltpu.roll(g, 2 * BLOCK_SIDE, 1), south_in[:, :tile]),
         south_in[:, tile:]],
        axis=1,
    )
    north_in = pltpu.roll(a, BLOCK_CELLS - BLOCK_SIDE, 1)
    from_north = jnp.concatenate(
        [north_in[:, : BLOCK_CELLS - tile],
         jnp.where(lane >= 3 * BLOCK_SIDE, g, north_in[:, BLOCK_CELLS - tile :])],
        axis=1,
    )
    x_plus = c_ref[0]
    x_minus = c_ref[1]
    y_plus = c_ref[2]
    y_minus = c_ref[3]
    new = (
        a
        - (x_plus * (a - from_west) + x_minus * (from_east - a))
        - (y_plus * (a - from_south) + y_minus * (from_north - a))
    )
    if e_ref is None:
        chunk = o_ref.shape[-1]
        for k in range(o_ref.shape[0]):
            o_ref[k, 0] = new[:, k * chunk : (k + 1) * chunk]
    else:
        o_ref[0] = new
        e_ref[0] = _edges_of(new, we_hit)


def last_step_call(action, ghosts, coefs, parts):
    blocks, comps, cells = action.shape
    chunk = cells // parts
    return pl.pallas_call(
        _step_kernel,
        grid=(blocks,),
        in_specs=[
            pl.BlockSpec((1, comps, cells), lambda b: (b, 0, 0)),
            pl.BlockSpec((1, comps, 4 * BLOCK_SIDE), lambda b: (b, 0, 0)),
            pl.BlockSpec((4, comps, 1), lambda b: (0, 0, 0)),
        ],
        out_specs=pl.BlockSpec((parts, 1, comps, chunk), lambda b: (0, b, 0, 0)),
        out_shape=jax.ShapeDtypeStruct((parts, blocks, comps, chunk), jnp.float32),
        interpret=INTERPRET,
    )(action, ghosts, coefs)


def edges_call(action):
    blocks, comps, cells = action.shape
    return pl.pallas_call(
        _edge_kernel,
        grid=(blocks,),
        in_specs=[pl.BlockSpec((1, comps, cells), lambda b: (b, 0, 0))],
        out_specs=pl.BlockSpec((1, comps, 4 * BLOCK_SIDE), lambda b: (b, 0, 0)),
        out_shape=jax.ShapeDtypeStruct((blocks, comps, 4 * BLOCK_SIDE), jnp.float32),
        interpret=INTERPRET,
    )(action)


def step_call(action, ghosts, coefs):
    blocks, comps, cells = action.shape
    return pl.pallas_call(
        _step_kernel,
        grid=(blocks,),
        in_specs=[
            pl.BlockSpec((1, comps, cells), lambda b: (b, 0, 0)),
            pl.BlockSpec((1, comps, 4 * BLOCK_SIDE), lambda b: (b, 0, 0)),
            pl.BlockSpec((4, comps, 1), lambda b: (0, 0, 0)),
        ],
        out_specs=[
            pl.BlockSpec((1, comps, cells), lambda b: (b, 0, 0)),
            pl.BlockSpec((1, comps, 4 * BLOCK_SIDE), lambda b: (b, 0, 0)),
        ],
        out_shape=[
            jax.ShapeDtypeStruct((blocks, comps, cells), jnp.float32),
            jax.ShapeDtypeStruct((blocks, comps, 4 * BLOCK_SIDE), jnp.float32),
        ],
        interpret=INTERPRET,
    )(action, ghosts, coefs)


def _per_lane(table):
    return jnp.repeat(table, BLOCK_SIDE, axis=1)


def _select_matrix(rows, use, row_of, group_of):
    blocks = use.shape[0]
    shape = (rows, 4 * BLOCK_SIDE, blocks, 4 * BLOCK_SIDE)
    a = lax.broadcasted_iota(jnp.int32, shape, 0)
    i = lax.broadcasted_iota(jnp.int32, shape, 1)
    q = lax.broadcasted_iota(jnp.int32, shape, 3)
    hit = (
        _per_lane(use)[None, None]
        & (_per_lane(row_of)[None, None] == a)
        & (_per_lane(group_of)[None, None] == i // BLOCK_SIDE)
        & (i % BLOCK_SIDE == q % BLOCK_SIDE)
    )
    return hit.astype(jnp.float32)


def routing(neighbours, blocks, devices):
    me = lax.axis_index("space")
    opp = jnp.array([1, 0, 3, 2], jnp.int32)[None, :]
    nb = neighbours
    ok = nb >= 0
    other = jnp.where(ok, nb // blocks, -1)
    own_key = jnp.arange(blocks * 4, dtype=jnp.int32).reshape(blocks, 4)
    src_key = (nb % blocks) * 4 + opp

    def rank(key):
        same = (other.reshape(-1)[None, :] == other.reshape(-1)[:, None]) & ok.reshape(-1)[None, :]
        before = key.reshape(-1)[None, :] < key.reshape(-1)[:, None]
        return (same & before).sum(-1).astype(jnp.int32).reshape(blocks, 4)

    pos_send = rank(own_key)
    pos_recv = rank(src_key)
    remote = ok & (other != me)
    overflow = jnp.any(remote & (pos_send >= CAPACITY)) | jnp.any(remote & (pos_recv >= CAPACITY))

    shape = (devices, blocks, 4 * BLOCK_SIDE, CAPACITY * BLOCK_SIDE)
    b = lax.broadcasted_iota(jnp.int32, shape, 0)
    i = lax.broadcasted_iota(jnp.int32, shape, 2)
    q = lax.broadcasted_iota(jnp.int32, shape, 3)
    send_mat = (
        _per_lane(remote)[None, :, :, None]
        & (_per_lane(other)[None, :, :, None] == b)
        & (_per_lane(pos_send)[None, :, :, None] == q // BLOCK_SIDE)
        & (i % BLOCK_SIDE == q % BLOCK_SIDE)
    ).astype(jnp.float32)

    local = ok & (other == me)
    recv_mat = _select_matrix(
        devices + blocks,
        ok & (local | (pos_recv < CAPACITY)),
        jnp.where(local, devices + nb % blocks, other),
        jnp.where(local, jnp.broadcast_to(opp, nb.shape), pos_recv),
    )
    return overflow, send_mat, recv_mat, (nb, ok, jnp.broadcast_to(opp, nb.shape))


def _split_einsum(spec, x, sel):
    sel = sel.astype(jnp.bfloat16)
    run = lambda part: jnp.einsum(spec, part, sel, preferred_element_type=jnp.float32)
    hi, mid, lo = _split3_xla(x)
    return (run(hi) + run(mid)) + run(lo)


def exchange_fast(edges, tables, flag=None):
    _, send_mat, recv_mat, _ = tables
    comps = edges.shape[1]
    send_buf = _split_einsum("lci,bliq->bcq", edges, send_mat)
    if flag is not None:
        row = jnp.broadcast_to(flag.astype(jnp.float32), (send_buf.shape[0], 1, send_buf.shape[2]))
        send_buf = jnp.concatenate([send_buf, row], axis=1)
    recv = lax.all_to_all(send_buf, "space", 0, 0, tiled=True)
    srcs = jnp.concatenate([recv[:, :comps], edges], axis=0)
    ghosts = jnp.einsum("aci,aiLq->Lcq", srcs, recv_mat, precision=lax.Precision.HIGHEST)
    if flag is None:
        return ghosts
    return ghosts, jnp.any(recv[:, comps, 0] > 0.5)


def exchange_slow(edges, tables):
    nb, ok, opp = tables[3]
    gathered = lax.all_gather(edges, "space", axis=0, tiled=True)
    fmat = _select_matrix(gathered.shape[0], ok, nb, opp)
    return _split_einsum("aci,aiLq->Lcq", gathered, fmat)


def interaction_of(spectra, pairs, coupling):
    plus_vals = jnp.take(spectra, pairs[:, 0], axis=1)
    minus_vals = jnp.take(spectra, pairs[:, 1], axis=1)
    return coupling[None, :, None] * (
        spectra * spectra * (plus_vals + minus_vals) - 2.0 * spectra * plus_vals * minus_vals
    )


def shards(devices, parts, action, coupling, active, neighbours, pairs):
    blocks, comp_dev, cell_count = action.shape
    spec_rank = lax.axis_index("spec")
    comp_ids = spec_rank * comp_dev + jnp.arange(comp_dev, dtype=jnp.int32)
    courant_x, courant_y = courant(comp_ids)
    coefs = jnp.stack(
        [
            jnp.maximum(courant_x, 0.0),
            jnp.minimum(courant_x, 0.0),
            jnp.maximum(courant_y, 0.0),
            jnp.minimum(courant_y, 0.0),
        ]
    )[:, :, None]
    tables = routing(neighbours, blocks, devices)

    def propagate(exchange, first=None):
        current_action = action
        edges = edges_call(action)
        for substep_idx in range(SUBSTEPS):
            if first is not None and substep_idx == 0:
                ghosts = first
            else:
                ghosts = exchange(edges)
            if substep_idx < SUBSTEPS - 1:
                current_action, edges = step_call(current_action, ghosts, coefs)
            else:
                return last_step_call(current_action, ghosts, coefs, parts)

    edges0 = edges_call(action)
    ghosts, anywhere = exchange_fast(edges0, tables, tables[0])
    chunked = propagate(lambda e: exchange_fast(e, tables), ghosts)
    chunked = lax.cond(
        anywhere, lambda c: propagate(lambda e: exchange_slow(e, tables)), lambda c: c, chunked
    )
    mixing = (
        jax.nn.one_hot(pairs[:, 0], SPECTRAL_COUNT, dtype=jnp.float32)
        + jax.nn.one_hot(pairs[:, 1], SPECTRAL_COUNT, dtype=jnp.float32)
        - 2.0 * jnp.eye(SPECTRAL_COUNT, dtype=jnp.float32)
    ).astype(jnp.bfloat16)
    arrived = lax.all_to_all(chunked, "spec", split_axis=0, concat_axis=0, tiled=True)
    points = jnp.transpose(arrived, (1, 0, 2, 3)).reshape(blocks, parts * comp_dev, -1)
    interaction = interaction_of(points, pairs, coupling)
    hi, mid, lo = _split3_xla(interaction)
    mix = lambda part: jnp.einsum("cj,bcx->bjx", mixing, part, preferred_element_type=jnp.float32)
    change = (mix(hi) + mix(mid)) + mix(lo)
    evolved = (points + change).reshape(blocks, parts, comp_dev, -1)
    back = lax.all_to_all(jnp.transpose(evolved, (1, 0, 2, 3)), "spec", 0, 0, tiled=True)
    result = jnp.transpose(back, (1, 2, 0, 3)).reshape(blocks, comp_dev, cell_count)
    return jnp.where(active[:, None, None] > 0, result, 0.0)


def solution(mesh):
    placed = (P("space", "spec", None), P(), P("space"), P("space", None), P())
    return jax.shard_map(
        functools.partial(shards, mesh.shape["space"], mesh.shape["spec"]), mesh=mesh, in_specs=placed, out_specs=P("space", "spec", None), check_vma=False
    )
```

```python
import functools
import math

import jax
import jax.numpy as jnp
from jax import lax
from jax.experimental import pallas as pl
from jax.experimental.pallas import tpu as pltpu
from jax.sharding import PartitionSpec as P

NDIR = 36
BLOCK_SIDE = 32
BLOCK_CELLS = BLOCK_SIDE * BLOCK_SIDE
SUBSTEPS = 3
SPECTRAL_COUNT = 1296
CAPACITY = 4
INTERPRET = False

CFL = 0.68


def courant(comp_ids):
    frequency = (comp_ids // NDIR).astype(jnp.float32)
    direction = comp_ids % NDIR
    half_dirs = NDIR // 2
    angles = (
        2.0
        * math.pi
        / NDIR
        * ((2 * (direction % half_dirs) + direction // half_dirs).astype(jnp.float32) + 0.5)
    )
    speeds = CFL * jnp.exp(-frequency * math.log(1.1))
    return (speeds * jnp.cos(angles), speeds * jnp.sin(angles))


def _split3(x):
    hi = x.astype(jnp.bfloat16)
    rest = x - hi.astype(jnp.float32)
    mid = rest.astype(jnp.bfloat16)
    lo = (rest - mid.astype(jnp.float32)).astype(jnp.bfloat16)
    return hi, mid, lo


def _split3_xla(x):
    hi = lax.reduce_precision(x, exponent_bits=8, mantissa_bits=7)
    rest = x - hi
    mid = lax.reduce_precision(rest, exponent_bits=8, mantissa_bits=7)
    lo = rest - mid
    return tuple(p.astype(jnp.bfloat16) for p in (hi, mid, lo))


def _select_dot(x, sel, dims):
    hi, mid, lo = _split3(x)
    run = lambda part: lax.dot_general(part, sel, (dims, ((), ())), preferred_element_type=jnp.float32)
    return (run(hi) + run(mid)) + run(lo)


def _we_hits():
    row = lax.broadcasted_iota(jnp.int32, (4 * BLOCK_SIDE, BLOCK_CELLS), 0)
    cell = lax.broadcasted_iota(jnp.int32, (4 * BLOCK_SIDE, BLOCK_CELLS), 1)
    side = row // BLOCK_SIDE
    t = row % BLOCK_SIDE
    target = jnp.where(side == 0, t * BLOCK_SIDE, t * BLOCK_SIDE + BLOCK_SIDE - 1)
    return ((cell == target) & (side < 2)).astype(jnp.bfloat16)


def _edges_of(field, we_hit):
    we = _select_dot(field, we_hit, ((1,), (1,)))
    lane = lax.broadcasted_iota(jnp.int32, (1, 4 * BLOCK_SIDE), 1)
    south = pltpu.roll(field[:, : 4 * BLOCK_SIDE], 2 * BLOCK_SIDE, 1)
    north = field[:, BLOCK_CELLS - 4 * BLOCK_SIDE :]
    return jnp.where(lane < 2 * BLOCK_SIDE, we, jnp.where(lane < 3 * BLOCK_SIDE, south, north))


def _edge_kernel(a_ref, e_ref):
    e_ref[0] = _edges_of(a_ref[0], _we_hits())


def _step_kernel(a_ref, g_ref, c_ref, o_ref, e_ref=None):
    a = a_ref[0]
    g = g_ref[0]
    we_hit = _we_hits()
    g_we = _select_dot(g, we_hit, ((1,), (0,)))
    cell = lax.broadcasted_iota(jnp.int32, (1, BLOCK_CELLS), 1)
    lane = lax.broadcasted_iota(jnp.int32, (1, 4 * BLOCK_SIDE), 1)
    x = cell % BLOCK_SIDE
    tile = 4 * BLOCK_SIDE
    from_west = jnp.where(x == 0, g_we, pltpu.roll(a, 1, 1))
    from_east = jnp.where(x == BLOCK_SIDE - 1, g_we, pltpu.roll(a, BLOCK_CELLS - 1, 1))
    south_in = pltpu.roll(a, BLOCK_SIDE, 1)
    from_south = jnp.concatenate(
        [jnp.where(lane < BLOCK_SIDE, pltpu.roll(g, 2 * BLOCK_SIDE, 1), south_in[:, :tile]),
         south_in[:, tile:]],
        axis=1,
    )
    north_in = pltpu.roll(a, BLOCK_CELLS - BLOCK_SIDE, 1)
    from_north = jnp.concatenate(
        [north_in[:, : BLOCK_CELLS - tile],
         jnp.where(lane >= 3 * BLOCK_SIDE, g, north_in[:, BLOCK_CELLS - tile :])],
        axis=1,
    )
    x_plus = c_ref[0]
    x_minus = c_ref[1]
    y_plus = c_ref[2]
    y_minus = c_ref[3]
    new = (
        a
        - (x_plus * (a - from_west) + x_minus * (from_east - a))
        - (y_plus * (a - from_south) + y_minus * (from_north - a))
    )
    if e_ref is None:
        chunk = o_ref.shape[-1]
        for k in range(o_ref.shape[0]):
            o_ref[k, 0] = new[:, k * chunk : (k + 1) * chunk]
    else:
        o_ref[0] = new
        e_ref[0] = _edges_of(new, we_hit)


def last_step_call(action, ghosts, coefs, parts):
    blocks, comps, cells = action.shape
    chunk = cells // parts
    return pl.pallas_call(
        _step_kernel,
        grid=(blocks,),
        in_specs=[
            pl.BlockSpec((1, comps, cells), lambda b: (b, 0, 0)),
            pl.BlockSpec((1, comps, 4 * BLOCK_SIDE), lambda b: (b, 0, 0)),
            pl.BlockSpec((4, comps, 1), lambda b: (0, 0, 0)),
        ],
        out_specs=pl.BlockSpec((parts, 1, comps, chunk), lambda b: (0, b, 0, 0)),
        out_shape=jax.ShapeDtypeStruct((parts, blocks, comps, chunk), jnp.float32),
        interpret=INTERPRET,
    )(action, ghosts, coefs)


def edges_call(action):
    blocks, comps, cells = action.shape
    return pl.pallas_call(
        _edge_kernel,
        grid=(blocks,),
        in_specs=[pl.BlockSpec((1, comps, cells), lambda b: (b, 0, 0))],
        out_specs=pl.BlockSpec((1, comps, 4 * BLOCK_SIDE), lambda b: (b, 0, 0)),
        out_shape=jax.ShapeDtypeStruct((blocks, comps, 4 * BLOCK_SIDE), jnp.float32),
        interpret=INTERPRET,
    )(action)


def step_call(action, ghosts, coefs):
    blocks, comps, cells = action.shape
    return pl.pallas_call(
        _step_kernel,
        grid=(blocks,),
        in_specs=[
            pl.BlockSpec((1, comps, cells), lambda b: (b, 0, 0)),
            pl.BlockSpec((1, comps, 4 * BLOCK_SIDE), lambda b: (b, 0, 0)),
            pl.BlockSpec((4, comps, 1), lambda b: (0, 0, 0)),
        ],
        out_specs=[
            pl.BlockSpec((1, comps, cells), lambda b: (b, 0, 0)),
            pl.BlockSpec((1, comps, 4 * BLOCK_SIDE), lambda b: (b, 0, 0)),
        ],
        out_shape=[
            jax.ShapeDtypeStruct((blocks, comps, cells), jnp.float32),
            jax.ShapeDtypeStruct((blocks, comps, 4 * BLOCK_SIDE), jnp.float32),
        ],
        interpret=INTERPRET,
    )(action, ghosts, coefs)


def _per_lane(table):
    return jnp.repeat(table, BLOCK_SIDE, axis=1)


def _select_matrix(rows, use, row_of, group_of):
    blocks = use.shape[0]
    shape = (rows, 4 * BLOCK_SIDE, blocks, 4 * BLOCK_SIDE)
    a = lax.broadcasted_iota(jnp.int32, shape, 0)
    i = lax.broadcasted_iota(jnp.int32, shape, 1)
    q = lax.broadcasted_iota(jnp.int32, shape, 3)
    hit = (
        _per_lane(use)[None, None]
        & (_per_lane(row_of)[None, None] == a)
        & (_per_lane(group_of)[None, None] == i // BLOCK_SIDE)
        & (i % BLOCK_SIDE == q % BLOCK_SIDE)
    )
    return hit.astype(jnp.float32)


def routing(neighbours, blocks, devices):
    me = lax.axis_index("space")
    opp = jnp.array([1, 0, 3, 2], jnp.int32)[None, :]
    nb = neighbours
    ok = nb >= 0
    other = jnp.where(ok, nb // blocks, -1)
    own_key = jnp.arange(blocks * 4, dtype=jnp.int32).reshape(blocks, 4)
    src_key = (nb % blocks) * 4 + opp

    def rank(key):
        same = (other.reshape(-1)[None, :] == other.reshape(-1)[:, None]) & ok.reshape(-1)[None, :]
        before = key.reshape(-1)[None, :] < key.reshape(-1)[:, None]
        return (same & before).sum(-1).astype(jnp.int32).reshape(blocks, 4)

    pos_send = rank(own_key)
    pos_recv = rank(src_key)
    remote = ok & (other != me)
    overflow = jnp.any(remote & (pos_send >= CAPACITY)) | jnp.any(remote & (pos_recv >= CAPACITY))

    shape = (devices, blocks, 4 * BLOCK_SIDE, CAPACITY * BLOCK_SIDE)
    b = lax.broadcasted_iota(jnp.int32, shape, 0)
    i = lax.broadcasted_iota(jnp.int32, shape, 2)
    q = lax.broadcasted_iota(jnp.int32, shape, 3)
    send_mat = (
        _per_lane(remote)[None, :, :, None]
        & (_per_lane(other)[None, :, :, None] == b)
        & (_per_lane(pos_send)[None, :, :, None] == q // BLOCK_SIDE)
        & (i % BLOCK_SIDE == q % BLOCK_SIDE)
    ).astype(jnp.float32)

    local = ok & (other == me)
    recv_mat = _select_matrix(
        devices + blocks,
        ok & (local | (pos_recv < CAPACITY)),
        jnp.where(local, devices + nb % blocks, other),
        jnp.where(local, jnp.broadcast_to(opp, nb.shape), pos_recv),
    )
    return overflow, send_mat, recv_mat, (nb, ok, jnp.broadcast_to(opp, nb.shape))


def _split_einsum(spec, x, sel):
    sel = sel.astype(jnp.bfloat16)
    run = lambda part: jnp.einsum(spec, part, sel, preferred_element_type=jnp.float32)
    hi, mid, lo = _split3_xla(x)
    return (run(hi) + run(mid)) + run(lo)


def exchange_fast(edges, tables, flag=None):
    _, send_mat, recv_mat, _ = tables
    comps = edges.shape[1]
    send_buf = _split_einsum("lci,bliq->bcq", edges, send_mat)
    if flag is not None:
        row = jnp.broadcast_to(flag.astype(jnp.float32), (send_buf.shape[0], 1, send_buf.shape[2]))
        send_buf = jnp.concatenate([send_buf, row], axis=1)
    recv = lax.all_to_all(send_buf, "space", 0, 0, tiled=True)
    srcs = jnp.concatenate([recv[:, :comps], edges], axis=0)
    ghosts = jnp.einsum("aci,aiLq->Lcq", srcs, recv_mat, precision=lax.Precision.HIGHEST)
    if flag is None:
        return ghosts
    return ghosts, jnp.any(recv[:, comps, 0] > 0.5)


def exchange_slow(edges, tables):
    nb, ok, opp = tables[3]
    gathered = lax.all_gather(edges, "space", axis=0, tiled=True)
    fmat = _select_matrix(gathered.shape[0], ok, nb, opp)
    return _split_einsum("aci,aiLq->Lcq", gathered, fmat)


def interaction_of(spectra, pairs, coupling):
    plus_vals = jnp.take(spectra, pairs[:, 0], axis=1)
    minus_vals = jnp.take(spectra, pairs[:, 1], axis=1)
    return coupling[None, :, None] * (
        spectra * spectra * (plus_vals + minus_vals) - 2.0 * spectra * plus_vals * minus_vals
    )


def shards(devices, parts, action, coupling, active, neighbours, pairs):
    blocks, comp_dev, cell_count = action.shape
    spec_rank = lax.axis_index("spec")
    comp_ids = spec_rank * comp_dev + jnp.arange(comp_dev, dtype=jnp.int32)
    courant_x, courant_y = courant(comp_ids)
    coefs = jnp.stack(
        [
            jnp.maximum(courant_x, 0.0),
            jnp.minimum(courant_x, 0.0),
            jnp.maximum(courant_y, 0.0),
            jnp.minimum(courant_y, 0.0),
        ]
    )[:, :, None]
    tables = routing(neighbours, blocks, devices)

    def propagate(exchange, first=None):
        current_action = action
        edges = edges_call(action)
        for substep_idx in range(SUBSTEPS):
            if first is not None and substep_idx == 0:
                ghosts = first
            else:
                ghosts = exchange(edges)
            if substep_idx < SUBSTEPS - 1:
                current_action, edges = step_call(current_action, ghosts, coefs)
            else:
                return last_step_call(current_action, ghosts, coefs, parts)

    edges0 = edges_call(action)
    ghosts, anywhere = exchange_fast(edges0, tables, tables[0])
    chunked = propagate(lambda e: exchange_fast(e, tables), ghosts)
    mixing = (
        jax.nn.one_hot(pairs[:, 0], SPECTRAL_COUNT, dtype=jnp.float32)
        + jax.nn.one_hot(pairs[:, 1], SPECTRAL_COUNT, dtype=jnp.float32)
        - 2.0 * jnp.eye(SPECTRAL_COUNT, dtype=jnp.float32)
    ).astype(jnp.bfloat16)

    def interact(chunked):
        arrived = lax.all_to_all(chunked, "spec", split_axis=0, concat_axis=0, tiled=True)
        points = jnp.transpose(arrived, (1, 0, 2, 3)).reshape(blocks, parts * comp_dev, -1)
        interaction = interaction_of(points, pairs, coupling)
        hi, mid, lo = _split3_xla(interaction)
        mix = lambda part: jnp.einsum("cj,bcx->bjx", mixing, part, preferred_element_type=jnp.float32)
        change = (mix(hi) + mix(mid)) + mix(lo)
        evolved = (points + change).reshape(blocks, parts, comp_dev, -1)
        back = lax.all_to_all(jnp.transpose(evolved, (1, 0, 2, 3)), "spec", 0, 0, tiled=True)
        return jnp.transpose(back, (1, 2, 0, 3)).reshape(blocks, comp_dev, cell_count)

    result = lax.cond(
        anywhere,
        lambda c: interact(propagate(lambda e: exchange_slow(e, tables))),
        interact,
        chunked,
    )
    return jnp.where(active[:, None, None] > 0, result, 0.0)


def solution(mesh):
    placed = (P("space", "spec", None), P(), P("space"), P("space", None), P())
    return jax.shard_map(
        functools.partial(shards, mesh.shape["space"], mesh.shape["spec"]), mesh=mesh, in_specs=placed, out_specs=P("space", "spec", None), check_vma=False
    )
```

```python
import functools
import math

import jax
import jax.numpy as jnp
from jax import lax
from jax.experimental import pallas as pl
from jax.experimental.pallas import tpu as pltpu
from jax.sharding import PartitionSpec as P

NDIR = 36
BLOCK_SIDE = 32
BLOCK_CELLS = BLOCK_SIDE * BLOCK_SIDE
SUBSTEPS = 3
SPECTRAL_COUNT = 1296
CAPACITY = 4
INTERPRET = False

CFL = 0.68


def courant(comp_ids):
    frequency = (comp_ids // NDIR).astype(jnp.float32)
    direction = comp_ids % NDIR
    half_dirs = NDIR // 2
    angles = (
        2.0
        * math.pi
        / NDIR
        * ((2 * (direction % half_dirs) + direction // half_dirs).astype(jnp.float32) + 0.5)
    )
    speeds = CFL * jnp.exp(-frequency * math.log(1.1))
    return (speeds * jnp.cos(angles), speeds * jnp.sin(angles))


def _split3(x):
    hi = x.astype(jnp.bfloat16)
    rest = x - hi.astype(jnp.float32)
    mid = rest.astype(jnp.bfloat16)
    lo = (rest - mid.astype(jnp.float32)).astype(jnp.bfloat16)
    return hi, mid, lo


def _split3_xla(x):
    hi = lax.reduce_precision(x, exponent_bits=8, mantissa_bits=7)
    rest = x - hi
    mid = lax.reduce_precision(rest, exponent_bits=8, mantissa_bits=7)
    lo = rest - mid
    return tuple(p.astype(jnp.bfloat16) for p in (hi, mid, lo))


def _select_dot(x, sel, dims):
    hi, mid, lo = _split3(x)
    run = lambda part: lax.dot_general(part, sel, (dims, ((), ())), preferred_element_type=jnp.float32)
    return (run(hi) + run(mid)) + run(lo)


def _we_hits():
    row = lax.broadcasted_iota(jnp.int32, (4 * BLOCK_SIDE, BLOCK_CELLS), 0)
    cell = lax.broadcasted_iota(jnp.int32, (4 * BLOCK_SIDE, BLOCK_CELLS), 1)
    side = row // BLOCK_SIDE
    t = row % BLOCK_SIDE
    target = jnp.where(side == 0, t * BLOCK_SIDE, t * BLOCK_SIDE + BLOCK_SIDE - 1)
    return ((cell == target) & (side < 2)).astype(jnp.bfloat16)


def _edges_of(field, we_hit):
    we = _select_dot(field, we_hit, ((1,), (1,)))
    lane = lax.broadcasted_iota(jnp.int32, (1, 4 * BLOCK_SIDE), 1)
    south = pltpu.roll(field[:, : 4 * BLOCK_SIDE], 2 * BLOCK_SIDE, 1)
    north = field[:, BLOCK_CELLS - 4 * BLOCK_SIDE :]
    return jnp.where(lane < 2 * BLOCK_SIDE, we, jnp.where(lane < 3 * BLOCK_SIDE, south, north))


def _edge_kernel(a_ref, e_ref):
    e_ref[0] = _edges_of(a_ref[0], _we_hits())


def _step_kernel(a_ref, g_ref, c_ref, o_ref, e_ref=None):
    a = a_ref[0]
    g = g_ref[0]
    we_hit = _we_hits()
    g_we = _select_dot(g, we_hit, ((1,), (0,)))
    cell = lax.broadcasted_iota(jnp.int32, (1, BLOCK_CELLS), 1)
    lane = lax.broadcasted_iota(jnp.int32, (1, 4 * BLOCK_SIDE), 1)
    x = cell % BLOCK_SIDE
    tile = 4 * BLOCK_SIDE
    from_west = jnp.where(x == 0, g_we, pltpu.roll(a, 1, 1))
    from_east = jnp.where(x == BLOCK_SIDE - 1, g_we, pltpu.roll(a, BLOCK_CELLS - 1, 1))
    south_in = pltpu.roll(a, BLOCK_SIDE, 1)
    from_south = jnp.concatenate(
        [jnp.where(lane < BLOCK_SIDE, pltpu.roll(g, 2 * BLOCK_SIDE, 1), south_in[:, :tile]),
         south_in[:, tile:]],
        axis=1,
    )
    north_in = pltpu.roll(a, BLOCK_CELLS - BLOCK_SIDE, 1)
    from_north = jnp.concatenate(
        [north_in[:, : BLOCK_CELLS - tile],
         jnp.where(lane >= 3 * BLOCK_SIDE, g, north_in[:, BLOCK_CELLS - tile :])],
        axis=1,
    )
    x_plus = c_ref[0]
    x_minus = c_ref[1]
    y_plus = c_ref[2]
    y_minus = c_ref[3]
    new = (
        a
        - (x_plus * (a - from_west) + x_minus * (from_east - a))
        - (y_plus * (a - from_south) + y_minus * (from_north - a))
    )
    if e_ref is None:
        chunk = o_ref.shape[-1]
        for k in range(o_ref.shape[0]):
            o_ref[k, 0] = new[:, k * chunk : (k + 1) * chunk]
    else:
        o_ref[0] = new
        e_ref[0] = _edges_of(new, we_hit)


def last_step_call(action, ghosts, coefs, parts):
    blocks, comps, cells = action.shape
    chunk = cells // parts
    return pl.pallas_call(
        _step_kernel,
        grid=(blocks,),
        in_specs=[
            pl.BlockSpec((1, comps, cells), lambda b: (b, 0, 0)),
            pl.BlockSpec((1, comps, 4 * BLOCK_SIDE), lambda b: (b, 0, 0)),
            pl.BlockSpec((4, comps, 1), lambda b: (0, 0, 0)),
        ],
        out_specs=pl.BlockSpec((parts, 1, comps, chunk), lambda b: (0, b, 0, 0)),
        out_shape=jax.ShapeDtypeStruct((parts, blocks, comps, chunk), jnp.float32),
        interpret=INTERPRET,
    )(action, ghosts, coefs)


def edges_call(action):
    blocks, comps, cells = action.shape
    return pl.pallas_call(
        _edge_kernel,
        grid=(blocks,),
        in_specs=[pl.BlockSpec((1, comps, cells), lambda b: (b, 0, 0))],
        out_specs=pl.BlockSpec((1, comps, 4 * BLOCK_SIDE), lambda b: (b, 0, 0)),
        out_shape=jax.ShapeDtypeStruct((blocks, comps, 4 * BLOCK_SIDE), jnp.float32),
        interpret=INTERPRET,
    )(action)


def step_call(action, ghosts, coefs):
    blocks, comps, cells = action.shape
    return pl.pallas_call(
        _step_kernel,
        grid=(blocks,),
        in_specs=[
            pl.BlockSpec((1, comps, cells), lambda b: (b, 0, 0)),
            pl.BlockSpec((1, comps, 4 * BLOCK_SIDE), lambda b: (b, 0, 0)),
            pl.BlockSpec((4, comps, 1), lambda b: (0, 0, 0)),
        ],
        out_specs=[
            pl.BlockSpec((1, comps, cells), lambda b: (b, 0, 0)),
            pl.BlockSpec((1, comps, 4 * BLOCK_SIDE), lambda b: (b, 0, 0)),
        ],
        out_shape=[
            jax.ShapeDtypeStruct((blocks, comps, cells), jnp.float32),
            jax.ShapeDtypeStruct((blocks, comps, 4 * BLOCK_SIDE), jnp.float32),
        ],
        interpret=INTERPRET,
    )(action, ghosts, coefs)


def _per_lane(table):
    return jnp.repeat(table, BLOCK_SIDE, axis=1)


def _select_matrix(rows, use, row_of, group_of):
    blocks = use.shape[0]
    shape = (rows, 4 * BLOCK_SIDE, blocks, 4 * BLOCK_SIDE)
    a = lax.broadcasted_iota(jnp.int32, shape, 0)
    i = lax.broadcasted_iota(jnp.int32, shape, 1)
    q = lax.broadcasted_iota(jnp.int32, shape, 3)
    hit = (
        _per_lane(use)[None, None]
        & (_per_lane(row_of)[None, None] == a)
        & (_per_lane(group_of)[None, None] == i // BLOCK_SIDE)
        & (i % BLOCK_SIDE == q % BLOCK_SIDE)
    )
    return hit.astype(jnp.float32)


def routing(neighbours, blocks, devices):
    me = lax.axis_index("space")
    opp = jnp.array([1, 0, 3, 2], jnp.int32)[None, :]
    nb = neighbours
    ok = nb >= 0
    other = jnp.where(ok, nb // blocks, -1)
    own_key = jnp.arange(blocks * 4, dtype=jnp.int32).reshape(blocks, 4)
    src_key = (nb % blocks) * 4 + opp

    def rank(key):
        same = (other.reshape(-1)[None, :] == other.reshape(-1)[:, None]) & ok.reshape(-1)[None, :]
        before = key.reshape(-1)[None, :] < key.reshape(-1)[:, None]
        return (same & before).sum(-1).astype(jnp.int32).reshape(blocks, 4)

    pos_send = rank(own_key)
    pos_recv = rank(src_key)
    remote = ok & (other != me)
    overflow = jnp.any(remote & (pos_send >= CAPACITY)) | jnp.any(remote & (pos_recv >= CAPACITY))

    shape = (devices, blocks, 4 * BLOCK_SIDE, CAPACITY * BLOCK_SIDE)
    b = lax.broadcasted_iota(jnp.int32, shape, 0)
    i = lax.broadcasted_iota(jnp.int32, shape, 2)
    q = lax.broadcasted_iota(jnp.int32, shape, 3)
    send_mat = (
        _per_lane(remote)[None, :, :, None]
        & (_per_lane(other)[None, :, :, None] == b)
        & (_per_lane(pos_send)[None, :, :, None] == q // BLOCK_SIDE)
        & (i % BLOCK_SIDE == q % BLOCK_SIDE)
    ).astype(jnp.float32)

    local = ok & (other == me)
    recv_mat = _select_matrix(
        devices + blocks,
        ok & (local | (pos_recv < CAPACITY)),
        jnp.where(local, devices + nb % blocks, other),
        jnp.where(local, jnp.broadcast_to(opp, nb.shape), pos_recv),
    )
    return overflow, send_mat, recv_mat, (nb, ok, jnp.broadcast_to(opp, nb.shape))


def _split_einsum(spec, x, sel):
    sel = sel.astype(jnp.bfloat16)
    run = lambda part: jnp.einsum(spec, part, sel, preferred_element_type=jnp.float32)
    hi, mid, lo = _split3_xla(x)
    return (run(hi) + run(mid)) + run(lo)


def exchange_fast(edges, tables, flag=None):
    _, send_mat, recv_mat, _ = tables
    comps = edges.shape[1]
    send_buf = _split_einsum("lci,bliq->bcq", edges, send_mat)
    if flag is not None:
        row = jnp.broadcast_to(flag.astype(jnp.float32), (send_buf.shape[0], 1, send_buf.shape[2]))
        send_buf = jnp.concatenate([send_buf, row], axis=1)
    recv = lax.all_to_all(send_buf, "space", 0, 0, tiled=True)
    srcs = jnp.concatenate([recv[:, :comps], edges], axis=0)
    ghosts = jnp.einsum("aci,aiLq->Lcq", srcs, recv_mat, precision=lax.Precision.HIGHEST)
    if flag is None:
        return ghosts
    return ghosts, jnp.any(recv[:, comps, 0] > 0.5)


def exchange_slow(edges, tables):
    nb, ok, opp = tables[3]
    gathered = lax.all_gather(edges, "space", axis=0, tiled=True)
    fmat = _select_matrix(gathered.shape[0], ok, nb, opp)
    return _split_einsum("aci,aiLq->Lcq", gathered, fmat)


def interaction_of(spectra, pairs, coupling):
    comps = pairs.shape[0]
    both = jnp.take(spectra, jnp.concatenate([pairs[:, 0], pairs[:, 1]]), axis=1)
    plus_vals = both[:, :comps]
    minus_vals = both[:, comps:]
    return coupling[None, :, None] * (
        spectra * spectra * (plus_vals + minus_vals) - 2.0 * spectra * plus_vals * minus_vals
    )


def shards(devices, parts, action, coupling, active, neighbours, pairs):
    blocks, comp_dev, cell_count = action.shape
    spec_rank = lax.axis_index("spec")
    comp_ids = spec_rank * comp_dev + jnp.arange(comp_dev, dtype=jnp.int32)
    courant_x, courant_y = courant(comp_ids)
    coefs = jnp.stack(
        [
            jnp.maximum(courant_x, 0.0),
            jnp.minimum(courant_x, 0.0),
            jnp.maximum(courant_y, 0.0),
            jnp.minimum(courant_y, 0.0),
        ]
    )[:, :, None]
    tables = routing(neighbours, blocks, devices)

    def propagate(exchange, first=None):
        current_action = action
        edges = edges_call(action)
        for substep_idx in range(SUBSTEPS):
            if first is not None and substep_idx == 0:
                ghosts = first
            else:
                ghosts = exchange(edges)
            if substep_idx < SUBSTEPS - 1:
                current_action, edges = step_call(current_action, ghosts, coefs)
            else:
                return last_step_call(current_action, ghosts, coefs, parts)

    edges0 = edges_call(action)
    ghosts, anywhere = exchange_fast(edges0, tables, tables[0])
    chunked = propagate(lambda e: exchange_fast(e, tables), ghosts)
    chunked = lax.cond(
        anywhere, lambda c: propagate(lambda e: exchange_slow(e, tables)), lambda c: c, chunked
    )
    mixing = (
        jax.nn.one_hot(pairs[:, 0], SPECTRAL_COUNT, dtype=jnp.float32)
        + jax.nn.one_hot(pairs[:, 1], SPECTRAL_COUNT, dtype=jnp.float32)
        - 2.0 * jnp.eye(SPECTRAL_COUNT, dtype=jnp.float32)
    ).astype(jnp.bfloat16)
    arrived = lax.all_to_all(chunked, "spec", split_axis=0, concat_axis=0, tiled=True)
    points = jnp.transpose(arrived, (1, 0, 2, 3)).reshape(blocks, parts * comp_dev, -1)
    interaction = interaction_of(points, pairs, coupling)
    parts3 = jnp.stack(_split3_xla(interaction))
    mixed = jnp.einsum("cj,sbcx->sbjx", mixing, parts3, preferred_element_type=jnp.float32)
    change = (mixed[0] + mixed[1]) + mixed[2]
    evolved = (points + change).reshape(blocks, parts, comp_dev, -1)
    back = lax.all_to_all(jnp.transpose(evolved, (1, 0, 2, 3)), "spec", 0, 0, tiled=True)
    result = jnp.transpose(back, (1, 2, 0, 3)).reshape(blocks, comp_dev, cell_count)
    return jnp.where(active[:, None, None] > 0, result, 0.0)


def solution(mesh):
    placed = (P("space", "spec", None), P(), P("space"), P("space", None), P())
    return jax.shard_map(
        functools.partial(shards, mesh.shape["space"], mesh.shape["spec"]), mesh=mesh, in_specs=placed, out_specs=P("space", "spec", None), check_vma=False
    )
```

```python
import functools
import math

import jax
import jax.numpy as jnp
from jax import lax
from jax.experimental import pallas as pl
from jax.experimental.pallas import tpu as pltpu
from jax.sharding import PartitionSpec as P

NDIR = 36
BLOCK_SIDE = 32
BLOCK_CELLS = BLOCK_SIDE * BLOCK_SIDE
SUBSTEPS = 3
SPECTRAL_COUNT = 1296
CAPACITY = 4
INTERPRET = False

CFL = 0.68


def courant(comp_ids):
    frequency = (comp_ids // NDIR).astype(jnp.float32)
    direction = comp_ids % NDIR
    half_dirs = NDIR // 2
    angles = (
        2.0
        * math.pi
        / NDIR
        * ((2 * (direction % half_dirs) + direction // half_dirs).astype(jnp.float32) + 0.5)
    )
    speeds = CFL * jnp.exp(-frequency * math.log(1.1))
    return (speeds * jnp.cos(angles), speeds * jnp.sin(angles))


def _split3(x):
    hi = x.astype(jnp.bfloat16)
    rest = x - hi.astype(jnp.float32)
    mid = rest.astype(jnp.bfloat16)
    lo = (rest - mid.astype(jnp.float32)).astype(jnp.bfloat16)
    return hi, mid, lo


def _split3_xla(x):
    hi = lax.reduce_precision(x, exponent_bits=8, mantissa_bits=7)
    rest = x - hi
    mid = lax.reduce_precision(rest, exponent_bits=8, mantissa_bits=7)
    lo = rest - mid
    return tuple(p.astype(jnp.bfloat16) for p in (hi, mid, lo))


def _select_dot(x, sel, dims):
    hi, mid, lo = _split3(x)
    run = lambda part: lax.dot_general(part, sel, (dims, ((), ())), preferred_element_type=jnp.float32)
    return (run(hi) + run(mid)) + run(lo)


def _we_hits():
    row = lax.broadcasted_iota(jnp.int32, (4 * BLOCK_SIDE, BLOCK_CELLS), 0)
    cell = lax.broadcasted_iota(jnp.int32, (4 * BLOCK_SIDE, BLOCK_CELLS), 1)
    side = row // BLOCK_SIDE
    t = row % BLOCK_SIDE
    target = jnp.where(side == 0, t * BLOCK_SIDE, t * BLOCK_SIDE + BLOCK_SIDE - 1)
    return ((cell == target) & (side < 2)).astype(jnp.bfloat16)


def _edges_of(field, we_hit):
    we = _select_dot(field, we_hit, ((1,), (1,)))
    lane = lax.broadcasted_iota(jnp.int32, (1, 4 * BLOCK_SIDE), 1)
    south = pltpu.roll(field[:, : 4 * BLOCK_SIDE], 2 * BLOCK_SIDE, 1)
    north = field[:, BLOCK_CELLS - 4 * BLOCK_SIDE :]
    return jnp.where(lane < 2 * BLOCK_SIDE, we, jnp.where(lane < 3 * BLOCK_SIDE, south, north))


def _edge_kernel(a_ref, e_ref):
    e_ref[0] = _edges_of(a_ref[0], _we_hits())


def _step_kernel(a_ref, g_ref, c_ref, o_ref, e_ref=None):
    a = a_ref[0]
    g = g_ref[0]
    we_hit = _we_hits()
    g_we = _select_dot(g, we_hit, ((1,), (0,)))
    cell = lax.broadcasted_iota(jnp.int32, (1, BLOCK_CELLS), 1)
    lane = lax.broadcasted_iota(jnp.int32, (1, 4 * BLOCK_SIDE), 1)
    x = cell % BLOCK_SIDE
    tile = 4 * BLOCK_SIDE
    from_west = jnp.where(x == 0, g_we, pltpu.roll(a, 1, 1))
    from_east = jnp.where(x == BLOCK_SIDE - 1, g_we, pltpu.roll(a, BLOCK_CELLS - 1, 1))
    south_in = pltpu.roll(a, BLOCK_SIDE, 1)
    from_south = jnp.concatenate(
        [jnp.where(lane < BLOCK_SIDE, pltpu.roll(g, 2 * BLOCK_SIDE, 1), south_in[:, :tile]),
         south_in[:, tile:]],
        axis=1,
    )
    north_in = pltpu.roll(a, BLOCK_CELLS - BLOCK_SIDE, 1)
    from_north = jnp.concatenate(
        [north_in[:, : BLOCK_CELLS - tile],
         jnp.where(lane >= 3 * BLOCK_SIDE, g, north_in[:, BLOCK_CELLS - tile :])],
        axis=1,
    )
    x_plus = c_ref[0]
    x_minus = c_ref[1]
    y_plus = c_ref[2]
    y_minus = c_ref[3]
    new = (
        a
        - (x_plus * (a - from_west) + x_minus * (from_east - a))
        - (y_plus * (a - from_south) + y_minus * (from_north - a))
    )
    if e_ref is None:
        chunk = o_ref.shape[-1]
        for k in range(o_ref.shape[0]):
            o_ref[k, 0] = new[:, k * chunk : (k + 1) * chunk]
    else:
        o_ref[0] = new
        e_ref[0] = _edges_of(new, we_hit)


def last_step_call(action, ghosts, coefs, parts):
    blocks, comps, cells = action.shape
    chunk = cells // parts
    return pl.pallas_call(
        _step_kernel,
        grid=(blocks,),
        in_specs=[
            pl.BlockSpec((1, comps, cells), lambda b: (b, 0, 0)),
            pl.BlockSpec((1, comps, 4 * BLOCK_SIDE), lambda b: (b, 0, 0)),
            pl.BlockSpec((4, comps, 1), lambda b: (0, 0, 0)),
        ],
        out_specs=pl.BlockSpec((parts, 1, comps, chunk), lambda b: (0, b, 0, 0)),
        out_shape=jax.ShapeDtypeStruct((parts, blocks, comps, chunk), jnp.float32),
        interpret=INTERPRET,
    )(action, ghosts, coefs)


def edges_call(action):
    blocks, comps, cells = action.shape
    return pl.pallas_call(
        _edge_kernel,
        grid=(blocks,),
        in_specs=[pl.BlockSpec((1, comps, cells), lambda b: (b, 0, 0))],
        out_specs=pl.BlockSpec((1, comps, 4 * BLOCK_SIDE), lambda b: (b, 0, 0)),
        out_shape=jax.ShapeDtypeStruct((blocks, comps, 4 * BLOCK_SIDE), jnp.float32),
        interpret=INTERPRET,
    )(action)


def step_call(action, ghosts, coefs):
    blocks, comps, cells = action.shape
    return pl.pallas_call(
        _step_kernel,
        grid=(blocks,),
        in_specs=[
            pl.BlockSpec((1, comps, cells), lambda b: (b, 0, 0)),
            pl.BlockSpec((1, comps, 4 * BLOCK_SIDE), lambda b: (b, 0, 0)),
            pl.BlockSpec((4, comps, 1), lambda b: (0, 0, 0)),
        ],
        out_specs=[
            pl.BlockSpec((1, comps, cells), lambda b: (b, 0, 0)),
            pl.BlockSpec((1, comps, 4 * BLOCK_SIDE), lambda b: (b, 0, 0)),
        ],
        out_shape=[
            jax.ShapeDtypeStruct((blocks, comps, cells), jnp.float32),
            jax.ShapeDtypeStruct((blocks, comps, 4 * BLOCK_SIDE), jnp.float32),
        ],
        interpret=INTERPRET,
    )(action, ghosts, coefs)


def _per_lane(table):
    return jnp.repeat(table, BLOCK_SIDE, axis=1)


def _select_matrix(rows, use, row_of, group_of):
    blocks = use.shape[0]
    shape = (rows, 4 * BLOCK_SIDE, blocks, 4 * BLOCK_SIDE)
    a = lax.broadcasted_iota(jnp.int32, shape, 0)
    i = lax.broadcasted_iota(jnp.int32, shape, 1)
    q = lax.broadcasted_iota(jnp.int32, shape, 3)
    hit = (
        _per_lane(use)[None, None]
        & (_per_lane(row_of)[None, None] == a)
        & (_per_lane(group_of)[None, None] == i // BLOCK_SIDE)
        & (i % BLOCK_SIDE == q % BLOCK_SIDE)
    )
    return hit.astype(jnp.float32)


def routing(neighbours, blocks, devices):
    me = lax.axis_index("space")
    opp = jnp.array([1, 0, 3, 2], jnp.int32)[None, :]
    nb = neighbours
    ok = nb >= 0
    other = jnp.where(ok, nb // blocks, -1)
    own_key = jnp.arange(blocks * 4, dtype=jnp.int32).reshape(blocks, 4)
    src_key = (nb % blocks) * 4 + opp

    def rank(key):
        same = (other.reshape(-1)[None, :] == other.reshape(-1)[:, None]) & ok.reshape(-1)[None, :]
        before = key.reshape(-1)[None, :] < key.reshape(-1)[:, None]
        return (same & before).sum(-1).astype(jnp.int32).reshape(blocks, 4)

    pos_send = rank(own_key)
    pos_recv = rank(src_key)
    remote = ok & (other != me)
    overflow = jnp.any(remote & (pos_send >= CAPACITY)) | jnp.any(remote & (pos_recv >= CAPACITY))

    shape = (devices, blocks, 4 * BLOCK_SIDE, CAPACITY * BLOCK_SIDE)
    b = lax.broadcasted_iota(jnp.int32, shape, 0)
    i = lax.broadcasted_iota(jnp.int32, shape, 2)
    q = lax.broadcasted_iota(jnp.int32, shape, 3)
    send_mat = (
        _per_lane(remote)[None, :, :, None]
        & (_per_lane(other)[None, :, :, None] == b)
        & (_per_lane(pos_send)[None, :, :, None] == q // BLOCK_SIDE)
        & (i % BLOCK_SIDE == q % BLOCK_SIDE)
    ).astype(jnp.float32)

    local = ok & (other == me)
    recv_mat = _select_matrix(
        devices + blocks,
        ok & (local | (pos_recv < CAPACITY)),
        jnp.where(local, devices + nb % blocks, other),
        jnp.where(local, jnp.broadcast_to(opp, nb.shape), pos_recv),
    )
    return overflow, send_mat, recv_mat, (nb, ok, jnp.broadcast_to(opp, nb.shape))


def _split_einsum(spec, x, sel):
    sel = sel.astype(jnp.bfloat16)
    run = lambda part: jnp.einsum(spec, part, sel, preferred_element_type=jnp.float32)
    hi, mid, lo = _split3_xla(x)
    return (run(hi) + run(mid)) + run(lo)


def exchange_fast(edges, tables, flag=None):
    _, send_mat, recv_mat, _ = tables
    comps = edges.shape[1]
    send_buf = _split_einsum("lci,bliq->bcq", edges, send_mat)
    if flag is not None:
        row = jnp.broadcast_to(flag.astype(jnp.float32), (send_buf.shape[0], 1, send_buf.shape[2]))
        send_buf = jnp.concatenate([send_buf, row], axis=1)
    recv = lax.all_to_all(send_buf, "space", 0, 0, tiled=True)
    srcs = jnp.concatenate([recv[:, :comps], edges], axis=0)
    ghosts = jnp.einsum("aci,aiLq->Lcq", srcs, recv_mat, precision=lax.Precision.HIGHEST)
    if flag is None:
        return ghosts
    return ghosts, jnp.any(recv[:, comps, 0] > 0.5)


def exchange_slow(edges, tables):
    nb, ok, opp = tables[3]
    gathered = lax.all_gather(edges, "space", axis=0, tiled=True)
    fmat = _select_matrix(gathered.shape[0], ok, nb, opp)
    return _split_einsum("aci,aiLq->Lcq", gathered, fmat)


def interaction_of(spectra, pairs, coupling):
    plus_vals = jnp.take(spectra, pairs[:, 0], axis=1)
    minus_vals = jnp.take(spectra, pairs[:, 1], axis=1)
    return coupling[None, :, None] * (
        spectra * spectra * (plus_vals + minus_vals) - 2.0 * spectra * plus_vals * minus_vals
    )


def shards(devices, parts, action, coupling, active, neighbours, pairs):
    blocks, comp_dev, cell_count = action.shape
    spec_rank = lax.axis_index("spec")
    comp_ids = spec_rank * comp_dev + jnp.arange(comp_dev, dtype=jnp.int32)
    courant_x, courant_y = courant(comp_ids)
    coefs = jnp.stack(
        [
            jnp.maximum(courant_x, 0.0),
            jnp.minimum(courant_x, 0.0),
            jnp.maximum(courant_y, 0.0),
            jnp.minimum(courant_y, 0.0),
        ]
    )[:, :, None]
    tables = routing(neighbours, blocks, devices)

    def propagate(exchange, first=None):
        current_action = action
        edges = edges_call(action)
        for substep_idx in range(SUBSTEPS):
            if first is not None and substep_idx == 0:
                ghosts = first
            else:
                ghosts = exchange(edges)
            if substep_idx == SUBSTEPS - 1:
                return current_action, ghosts
            current_action, edges = step_call(current_action, ghosts, coefs)

    edges0 = edges_call(action)
    ghosts, anywhere = exchange_fast(edges0, tables, tables[0])
    state = propagate(lambda e: exchange_fast(e, tables), ghosts)
    state = lax.cond(
        anywhere, lambda a, g: propagate(lambda e: exchange_slow(e, tables)), lambda a, g: (a, g), *state
    )
    chunked = last_step_call(*state, coefs, parts)
    mixing = (
        jax.nn.one_hot(pairs[:, 0], SPECTRAL_COUNT, dtype=jnp.float32)
        + jax.nn.one_hot(pairs[:, 1], SPECTRAL_COUNT, dtype=jnp.float32)
        - 2.0 * jnp.eye(SPECTRAL_COUNT, dtype=jnp.float32)
    ).astype(jnp.bfloat16)
    arrived = lax.all_to_all(chunked, "spec", split_axis=0, concat_axis=0, tiled=True)
    points = jnp.transpose(arrived, (1, 0, 2, 3)).reshape(blocks, parts * comp_dev, -1)
    interaction = interaction_of(points, pairs, coupling)
    hi, mid, lo = _split3_xla(interaction)
    mix = lambda part: jnp.einsum("cj,bcx->bjx", mixing, part, preferred_element_type=jnp.float32)
    change = (mix(hi) + mix(mid)) + mix(lo)
    evolved = (points + change).reshape(blocks, parts, comp_dev, -1)
    back = lax.all_to_all(jnp.transpose(evolved, (1, 0, 2, 3)), "spec", 0, 0, tiled=True)
    result = jnp.transpose(back, (1, 2, 0, 3)).reshape(blocks, comp_dev, cell_count)
    return jnp.where(active[:, None, None] > 0, result, 0.0)


def solution(mesh):
    placed = (P("space", "spec", None), P(), P("space"), P("space", None), P())
    return jax.shard_map(
        functools.partial(shards, mesh.shape["space"], mesh.shape["spec"]), mesh=mesh, in_specs=placed, out_specs=P("space", "spec", None), check_vma=False
    )
```

```python
import functools
import math

import jax
import jax.numpy as jnp
from jax import lax
from jax.experimental import pallas as pl
from jax.experimental.pallas import tpu as pltpu
from jax.sharding import PartitionSpec as P

NDIR = 36
BLOCK_SIDE = 32
BLOCK_CELLS = BLOCK_SIDE * BLOCK_SIDE
SUBSTEPS = 3
SPECTRAL_COUNT = 1296
CAPACITY = 4
INTERPRET = False
KERNEL_PARAMS = pltpu.CompilerParams()

CFL = 0.68


def courant(comp_ids):
    frequency = (comp_ids // NDIR).astype(jnp.float32)
    direction = comp_ids % NDIR
    half_dirs = NDIR // 2
    angles = (
        2.0
        * math.pi
        / NDIR
        * ((2 * (direction % half_dirs) + direction // half_dirs).astype(jnp.float32) + 0.5)
    )
    speeds = CFL * jnp.exp(-frequency * math.log(1.1))
    return (speeds * jnp.cos(angles), speeds * jnp.sin(angles))


def _split3(x):
    hi = x.astype(jnp.bfloat16)
    rest = x - hi.astype(jnp.float32)
    mid = rest.astype(jnp.bfloat16)
    lo = (rest - mid.astype(jnp.float32)).astype(jnp.bfloat16)
    return hi, mid, lo


def _split3_xla(x):
    hi = lax.reduce_precision(x, exponent_bits=8, mantissa_bits=7)
    rest = x - hi
    mid = lax.reduce_precision(rest, exponent_bits=8, mantissa_bits=7)
    lo = rest - mid
    return tuple(p.astype(jnp.bfloat16) for p in (hi, mid, lo))


def _select_dot(x, sel, dims):
    hi, mid, lo = _split3(x)
    run = lambda part: lax.dot_general(part, sel, (dims, ((), ())), preferred_element_type=jnp.float32)
    return (run(hi) + run(mid)) + run(lo)


def _we_hits():
    row = lax.broadcasted_iota(jnp.int32, (4 * BLOCK_SIDE, BLOCK_CELLS), 0)
    cell = lax.broadcasted_iota(jnp.int32, (4 * BLOCK_SIDE, BLOCK_CELLS), 1)
    side = row // BLOCK_SIDE
    t = row % BLOCK_SIDE
    target = jnp.where(side == 0, t * BLOCK_SIDE, t * BLOCK_SIDE + BLOCK_SIDE - 1)
    return ((cell == target) & (side < 2)).astype(jnp.bfloat16)


def _edges_of(field, we_hit):
    we = _select_dot(field, we_hit, ((1,), (1,)))
    lane = lax.broadcasted_iota(jnp.int32, (1, 4 * BLOCK_SIDE), 1)
    south = pltpu.roll(field[:, : 4 * BLOCK_SIDE], 2 * BLOCK_SIDE, 1)
    north = field[:, BLOCK_CELLS - 4 * BLOCK_SIDE :]
    return jnp.where(lane < 2 * BLOCK_SIDE, we, jnp.where(lane < 3 * BLOCK_SIDE, south, north))


def _edge_kernel(a_ref, e_ref):
    e_ref[0] = _edges_of(a_ref[0], _we_hits())


def _step_kernel(a_ref, g_ref, c_ref, o_ref, e_ref=None):
    a = a_ref[0]
    g = g_ref[0]
    we_hit = _we_hits()
    g_we = _select_dot(g, we_hit, ((1,), (0,)))
    cell = lax.broadcasted_iota(jnp.int32, (1, BLOCK_CELLS), 1)
    lane = lax.broadcasted_iota(jnp.int32, (1, 4 * BLOCK_SIDE), 1)
    x = cell % BLOCK_SIDE
    tile = 4 * BLOCK_SIDE
    from_west = jnp.where(x == 0, g_we, pltpu.roll(a, 1, 1))
    from_east = jnp.where(x == BLOCK_SIDE - 1, g_we, pltpu.roll(a, BLOCK_CELLS - 1, 1))
    south_in = pltpu.roll(a, BLOCK_SIDE, 1)
    from_south = jnp.concatenate(
        [jnp.where(lane < BLOCK_SIDE, pltpu.roll(g, 2 * BLOCK_SIDE, 1), south_in[:, :tile]),
         south_in[:, tile:]],
        axis=1,
    )
    north_in = pltpu.roll(a, BLOCK_CELLS - BLOCK_SIDE, 1)
    from_north = jnp.concatenate(
        [north_in[:, : BLOCK_CELLS - tile],
         jnp.where(lane >= 3 * BLOCK_SIDE, g, north_in[:, BLOCK_CELLS - tile :])],
        axis=1,
    )
    x_plus = c_ref[0]
    x_minus = c_ref[1]
    y_plus = c_ref[2]
    y_minus = c_ref[3]
    new = (
        a
        - (x_plus * (a - from_west) + x_minus * (from_east - a))
        - (y_plus * (a - from_south) + y_minus * (from_north - a))
    )
    if e_ref is None:
        chunk = o_ref.shape[-1]
        for k in range(o_ref.shape[0]):
            o_ref[k, 0] = new[:, k * chunk : (k + 1) * chunk]
    else:
        o_ref[0] = new
        e_ref[0] = _edges_of(new, we_hit)


def last_step_call(action, ghosts, coefs, parts):
    blocks, comps, cells = action.shape
    chunk = cells // parts
    return pl.pallas_call(
        _step_kernel,
        grid=(blocks,),
        in_specs=[
            pl.BlockSpec((1, comps, cells), lambda b: (b, 0, 0)),
            pl.BlockSpec((1, comps, 4 * BLOCK_SIDE), lambda b: (b, 0, 0)),
            pl.BlockSpec((4, comps, 1), lambda b: (0, 0, 0)),
        ],
        out_specs=pl.BlockSpec((parts, 1, comps, chunk), lambda b: (0, b, 0, 0)),
        out_shape=jax.ShapeDtypeStruct((parts, blocks, comps, chunk), jnp.float32),
        compiler_params=KERNEL_PARAMS,
        interpret=INTERPRET,
    )(action, ghosts, coefs)


def edges_call(action):
    blocks, comps, cells = action.shape
    return pl.pallas_call(
        _edge_kernel,
        grid=(blocks,),
        in_specs=[pl.BlockSpec((1, comps, cells), lambda b: (b, 0, 0))],
        out_specs=pl.BlockSpec((1, comps, 4 * BLOCK_SIDE), lambda b: (b, 0, 0)),
        out_shape=jax.ShapeDtypeStruct((blocks, comps, 4 * BLOCK_SIDE), jnp.float32),
        compiler_params=KERNEL_PARAMS,
        interpret=INTERPRET,
    )(action)


def step_call(action, ghosts, coefs):
    blocks, comps, cells = action.shape
    return pl.pallas_call(
        _step_kernel,
        grid=(blocks,),
        in_specs=[
            pl.BlockSpec((1, comps, cells), lambda b: (b, 0, 0)),
            pl.BlockSpec((1, comps, 4 * BLOCK_SIDE), lambda b: (b, 0, 0)),
            pl.BlockSpec((4, comps, 1), lambda b: (0, 0, 0)),
        ],
        out_specs=[
            pl.BlockSpec((1, comps, cells), lambda b: (b, 0, 0)),
            pl.BlockSpec((1, comps, 4 * BLOCK_SIDE), lambda b: (b, 0, 0)),
        ],
        out_shape=[
            jax.ShapeDtypeStruct((blocks, comps, cells), jnp.float32),
            jax.ShapeDtypeStruct((blocks, comps, 4 * BLOCK_SIDE), jnp.float32),
        ],
        compiler_params=KERNEL_PARAMS,
        interpret=INTERPRET,
    )(action, ghosts, coefs)


def _per_lane(table):
    return jnp.repeat(table, BLOCK_SIDE, axis=1)


def _select_matrix(rows, use, row_of, group_of):
    blocks = use.shape[0]
    shape = (rows, 4 * BLOCK_SIDE, blocks, 4 * BLOCK_SIDE)
    a = lax.broadcasted_iota(jnp.int32, shape, 0)
    i = lax.broadcasted_iota(jnp.int32, shape, 1)
    q = lax.broadcasted_iota(jnp.int32, shape, 3)
    hit = (
        _per_lane(use)[None, None]
        & (_per_lane(row_of)[None, None] == a)
        & (_per_lane(group_of)[None, None] == i // BLOCK_SIDE)
        & (i % BLOCK_SIDE == q % BLOCK_SIDE)
    )
    return hit.astype(jnp.float32)


def routing(neighbours, blocks, devices):
    me = lax.axis_index("space")
    opp = jnp.array([1, 0, 3, 2], jnp.int32)[None, :]
    nb = neighbours
    ok = nb >= 0
    other = jnp.where(ok, nb // blocks, -1)
    own_key = jnp.arange(blocks * 4, dtype=jnp.int32).reshape(blocks, 4)
    src_key = (nb % blocks) * 4 + opp

    def rank(key):
        same = (other.reshape(-1)[None, :] == other.reshape(-1)[:, None]) & ok.reshape(-1)[None, :]
        before = key.reshape(-1)[None, :] < key.reshape(-1)[:, None]
        return (same & before).sum(-1).astype(jnp.int32).reshape(blocks, 4)

    pos_send = rank(own_key)
    pos_recv = rank(src_key)
    remote = ok & (other != me)
    overflow = jnp.any(remote & (pos_send >= CAPACITY)) | jnp.any(remote & (pos_recv >= CAPACITY))

    shape = (devices, blocks, 4 * BLOCK_SIDE, CAPACITY * BLOCK_SIDE)
    b = lax.broadcasted_iota(jnp.int32, shape, 0)
    i = lax.broadcasted_iota(jnp.int32, shape, 2)
    q = lax.broadcasted_iota(jnp.int32, shape, 3)
    send_mat = (
        _per_lane(remote)[None, :, :, None]
        & (_per_lane(other)[None, :, :, None] == b)
        & (_per_lane(pos_send)[None, :, :, None] == q // BLOCK_SIDE)
        & (i % BLOCK_SIDE == q % BLOCK_SIDE)
    ).astype(jnp.float32)

    local = ok & (other == me)
    recv_mat = _select_matrix(
        devices + blocks,
        ok & (local | (pos_recv < CAPACITY)),
        jnp.where(local, devices + nb % blocks, other),
        jnp.where(local, jnp.broadcast_to(opp, nb.shape), pos_recv),
    )
    return overflow, send_mat, recv_mat, (nb, ok, jnp.broadcast_to(opp, nb.shape))


def _split_einsum(spec, x, sel):
    sel = sel.astype(jnp.bfloat16)
    run = lambda part: jnp.einsum(spec, part, sel, preferred_element_type=jnp.float32)
    hi, mid, lo = _split3_xla(x)
    return (run(hi) + run(mid)) + run(lo)


def exchange_fast(edges, tables, flag=None):
    _, send_mat, recv_mat, _ = tables
    comps = edges.shape[1]
    send_buf = _split_einsum("lci,bliq->bcq", edges, send_mat)
    if flag is not None:
        row = jnp.broadcast_to(flag.astype(jnp.float32), (send_buf.shape[0], 1, send_buf.shape[2]))
        send_buf = jnp.concatenate([send_buf, row], axis=1)
    recv = lax.all_to_all(send_buf, "space", 0, 0, tiled=True)
    srcs = jnp.concatenate([recv[:, :comps], edges], axis=0)
    ghosts = jnp.einsum("aci,aiLq->Lcq", srcs, recv_mat, precision=lax.Precision.HIGHEST)
    if flag is None:
        return ghosts
    return ghosts, jnp.any(recv[:, comps, 0] > 0.5)


def exchange_slow(edges, tables):
    nb, ok, opp = tables[3]
    gathered = lax.all_gather(edges, "space", axis=0, tiled=True)
    fmat = _select_matrix(gathered.shape[0], ok, nb, opp)
    return _split_einsum("aci,aiLq->Lcq", gathered, fmat)


def interaction_of(spectra, pairs, coupling):
    plus_vals = jnp.take(spectra, pairs[:, 0], axis=1)
    minus_vals = jnp.take(spectra, pairs[:, 1], axis=1)
    return coupling[None, :, None] * (
        spectra * spectra * (plus_vals + minus_vals) - 2.0 * spectra * plus_vals * minus_vals
    )


def shards(devices, parts, action, coupling, active, neighbours, pairs):
    blocks, comp_dev, cell_count = action.shape
    spec_rank = lax.axis_index("spec")
    comp_ids = spec_rank * comp_dev + jnp.arange(comp_dev, dtype=jnp.int32)
    courant_x, courant_y = courant(comp_ids)
    coefs = jnp.stack(
        [
            jnp.maximum(courant_x, 0.0),
            jnp.minimum(courant_x, 0.0),
            jnp.maximum(courant_y, 0.0),
            jnp.minimum(courant_y, 0.0),
        ]
    )[:, :, None]
    tables = routing(neighbours, blocks, devices)

    def propagate(exchange, first=None):
        current_action = action
        edges = edges_call(action)
        for substep_idx in range(SUBSTEPS):
            if first is not None and substep_idx == 0:
                ghosts = first
            else:
                ghosts = exchange(edges)
            if substep_idx < SUBSTEPS - 1:
                current_action, edges = step_call(current_action, ghosts, coefs)
            else:
                return last_step_call(current_action, ghosts, coefs, parts)

    edges0 = edges_call(action)
    ghosts, anywhere = exchange_fast(edges0, tables, tables[0])
    chunked = propagate(lambda e: exchange_fast(e, tables), ghosts)
    chunked = lax.cond(
        anywhere, lambda c: propagate(lambda e: exchange_slow(e, tables)), lambda c: c, chunked
    )
    mixing = (
        jax.nn.one_hot(pairs[:, 0], SPECTRAL_COUNT, dtype=jnp.float32)
        + jax.nn.one_hot(pairs[:, 1], SPECTRAL_COUNT, dtype=jnp.float32)
        - 2.0 * jnp.eye(SPECTRAL_COUNT, dtype=jnp.float32)
    ).astype(jnp.bfloat16)
    arrived = lax.all_to_all(chunked, "spec", split_axis=0, concat_axis=0, tiled=True)
    points = jnp.transpose(arrived, (1, 0, 2, 3)).reshape(blocks, parts * comp_dev, -1)
    interaction = interaction_of(points, pairs, coupling)
    hi, mid, lo = _split3_xla(interaction)
    mix = lambda part: jnp.einsum("cj,bcx->bjx", mixing, part, preferred_element_type=jnp.float32)
    change = (mix(hi) + mix(mid)) + mix(lo)
    evolved = (points + change).reshape(blocks, parts, comp_dev, -1)
    back = lax.all_to_all(jnp.transpose(evolved, (1, 0, 2, 3)), "spec", 0, 0, tiled=True)
    result = jnp.transpose(back, (1, 2, 0, 3)).reshape(blocks, comp_dev, cell_count)
    return jnp.where(active[:, None, None] > 0, result, 0.0)


def solution(mesh):
    placed = (P("space", "spec", None), P(), P("space"), P("space", None), P())
    return jax.shard_map(
        functools.partial(shards, mesh.shape["space"], mesh.shape["spec"]), mesh=mesh, in_specs=placed, out_specs=P("space", "spec", None), check_vma=False
    )
```

```python
import functools
import math

import jax
import jax.numpy as jnp
from jax import lax
from jax.experimental import pallas as pl
from jax.experimental.pallas import tpu as pltpu
from jax.sharding import PartitionSpec as P

NDIR = 36
BLOCK_SIDE = 32
BLOCK_CELLS = BLOCK_SIDE * BLOCK_SIDE
SUBSTEPS = 3
SPECTRAL_COUNT = 1296
CAPACITY = 4
INTERPRET = False

CFL = 0.68


def courant(comp_ids):
    frequency = (comp_ids // NDIR).astype(jnp.float32)
    direction = comp_ids % NDIR
    half_dirs = NDIR // 2
    angles = (
        2.0
        * math.pi
        / NDIR
        * ((2 * (direction % half_dirs) + direction // half_dirs).astype(jnp.float32) + 0.5)
    )
    speeds = CFL * jnp.exp(-frequency * math.log(1.1))
    return (speeds * jnp.cos(angles), speeds * jnp.sin(angles))


def _split3(x):
    hi = x.astype(jnp.bfloat16)
    rest = x - hi.astype(jnp.float32)
    mid = rest.astype(jnp.bfloat16)
    lo = (rest - mid.astype(jnp.float32)).astype(jnp.bfloat16)
    return hi, mid, lo


def _split3_xla(x):
    hi = lax.reduce_precision(x, exponent_bits=8, mantissa_bits=7)
    rest = x - hi
    mid = lax.reduce_precision(rest, exponent_bits=8, mantissa_bits=7)
    lo = rest - mid
    return tuple(p.astype(jnp.bfloat16) for p in (hi, mid, lo))


def _select_dot(x, sel, dims):
    hi, mid, lo = _split3(x)
    run = lambda part: lax.dot_general(part, sel, (dims, ((), ())), preferred_element_type=jnp.float32)
    return (run(hi) + run(mid)) + run(lo)


def _we_hits():
    row = lax.broadcasted_iota(jnp.int32, (4 * BLOCK_SIDE, BLOCK_CELLS), 0)
    cell = lax.broadcasted_iota(jnp.int32, (4 * BLOCK_SIDE, BLOCK_CELLS), 1)
    side = row // BLOCK_SIDE
    t = row % BLOCK_SIDE
    target = jnp.where(side == 0, t * BLOCK_SIDE, t * BLOCK_SIDE + BLOCK_SIDE - 1)
    return ((cell == target) & (side < 2)).astype(jnp.bfloat16)


def _edges_of(field, we_hit):
    we = _select_dot(field, we_hit, ((1,), (1,)))
    lane = lax.broadcasted_iota(jnp.int32, (1, 4 * BLOCK_SIDE), 1)
    south = pltpu.roll(field[:, : 4 * BLOCK_SIDE], 2 * BLOCK_SIDE, 1)
    north = field[:, BLOCK_CELLS - 4 * BLOCK_SIDE :]
    return jnp.where(lane < 2 * BLOCK_SIDE, we, jnp.where(lane < 3 * BLOCK_SIDE, south, north))


def _edge_kernel(a_ref, e_ref):
    e_ref[0] = _edges_of(a_ref[0], _we_hits())


def _step_kernel(a_ref, g_ref, c_ref, o_ref, e_ref=None):
    a = a_ref[0]
    g = g_ref[0]
    we_hit = _we_hits()
    g_we = _select_dot(g, we_hit, ((1,), (0,)))
    cell = lax.broadcasted_iota(jnp.int32, (1, BLOCK_CELLS), 1)
    lane = lax.broadcasted_iota(jnp.int32, (1, 4 * BLOCK_SIDE), 1)
    x = cell % BLOCK_SIDE
    tile = 4 * BLOCK_SIDE
    from_west = jnp.where(x == 0, g_we, pltpu.roll(a, 1, 1))
    from_east = jnp.where(x == BLOCK_SIDE - 1, g_we, pltpu.roll(a, BLOCK_CELLS - 1, 1))
    south_in = pltpu.roll(a, BLOCK_SIDE, 1)
    from_south = jnp.concatenate(
        [jnp.where(lane < BLOCK_SIDE, pltpu.roll(g, 2 * BLOCK_SIDE, 1), south_in[:, :tile]),
         south_in[:, tile:]],
        axis=1,
    )
    north_in = pltpu.roll(a, BLOCK_CELLS - BLOCK_SIDE, 1)
    from_north = jnp.concatenate(
        [north_in[:, : BLOCK_CELLS - tile],
         jnp.where(lane >= 3 * BLOCK_SIDE, g, north_in[:, BLOCK_CELLS - tile :])],
        axis=1,
    )
    x_plus = c_ref[0]
    x_minus = c_ref[1]
    y_plus = c_ref[2]
    y_minus = c_ref[3]
    new = (
        a
        - (x_plus * (a - from_west) + x_minus * (from_east - a))
        - (y_plus * (a - from_south) + y_minus * (from_north - a))
    )
    if e_ref is None:
        chunk = o_ref.shape[-1]
        for k in range(o_ref.shape[0]):
            o_ref[k, 0] = new[:, k * chunk : (k + 1) * chunk]
    else:
        o_ref[0] = new
        e_ref[0] = _edges_of(new, we_hit)


def last_step_call(action, ghosts, coefs, parts):
    blocks, comps, cells = action.shape
    chunk = cells // parts
    return pl.pallas_call(
        _step_kernel,
        grid=(blocks,),
        in_specs=[
            pl.BlockSpec((1, comps, cells), lambda b: (b, 0, 0)),
            pl.BlockSpec((1, comps, 4 * BLOCK_SIDE), lambda b: (b, 0, 0)),
            pl.BlockSpec((4, comps, 1), lambda b: (0, 0, 0)),
        ],
        out_specs=pl.BlockSpec((parts, 1, comps, chunk), lambda b: (0, b, 0, 0)),
        out_shape=jax.ShapeDtypeStruct((parts, blocks, comps, chunk), jnp.float32),
        interpret=INTERPRET,
    )(action, ghosts, coefs)


def edges_call(action):
    blocks, comps, cells = action.shape
    return pl.pallas_call(
        _edge_kernel,
        grid=(blocks,),
        in_specs=[pl.BlockSpec((1, comps, cells), lambda b: (b, 0, 0))],
        out_specs=pl.BlockSpec((1, comps, 4 * BLOCK_SIDE), lambda b: (b, 0, 0)),
        out_shape=jax.ShapeDtypeStruct((blocks, comps, 4 * BLOCK_SIDE), jnp.float32),
        interpret=INTERPRET,
    )(action)


def step_call(action, ghosts, coefs):
    blocks, comps, cells = action.shape
    return pl.pallas_call(
        _step_kernel,
        grid=(blocks,),
        in_specs=[
            pl.BlockSpec((1, comps, cells), lambda b: (b, 0, 0)),
            pl.BlockSpec((1, comps, 4 * BLOCK_SIDE), lambda b: (b, 0, 0)),
            pl.BlockSpec((4, comps, 1), lambda b: (0, 0, 0)),
        ],
        out_specs=[
            pl.BlockSpec((1, comps, cells), lambda b: (b, 0, 0)),
            pl.BlockSpec((1, comps, 4 * BLOCK_SIDE), lambda b: (b, 0, 0)),
        ],
        out_shape=[
            jax.ShapeDtypeStruct((blocks, comps, cells), jnp.float32),
            jax.ShapeDtypeStruct((blocks, comps, 4 * BLOCK_SIDE), jnp.float32),
        ],
        interpret=INTERPRET,
    )(action, ghosts, coefs)


def _per_lane(table):
    return jnp.repeat(table, BLOCK_SIDE, axis=1)


def _select_matrix(rows, use, row_of, group_of):
    blocks = use.shape[0]
    shape = (rows, 4 * BLOCK_SIDE, blocks, 4 * BLOCK_SIDE)
    a = lax.broadcasted_iota(jnp.int32, shape, 0)
    i = lax.broadcasted_iota(jnp.int32, shape, 1)
    q = lax.broadcasted_iota(jnp.int32, shape, 3)
    hit = (
        _per_lane(use)[None, None]
        & (_per_lane(row_of)[None, None] == a)
        & (_per_lane(group_of)[None, None] == i // BLOCK_SIDE)
        & (i % BLOCK_SIDE == q % BLOCK_SIDE)
    )
    return hit.astype(jnp.bfloat16)


def routing(neighbours, blocks, devices):
    me = lax.axis_index("space")
    opp = jnp.array([1, 0, 3, 2], jnp.int32)[None, :]
    nb = neighbours
    ok = nb >= 0
    other = jnp.where(ok, nb // blocks, -1)
    own_key = jnp.arange(blocks * 4, dtype=jnp.int32).reshape(blocks, 4)
    src_key = (nb % blocks) * 4 + opp

    def rank(key):
        same = (other.reshape(-1)[None, :] == other.reshape(-1)[:, None]) & ok.reshape(-1)[None, :]
        before = key.reshape(-1)[None, :] < key.reshape(-1)[:, None]
        return (same & before).sum(-1).astype(jnp.int32).reshape(blocks, 4)

    pos_send = rank(own_key)
    pos_recv = rank(src_key)
    remote = ok & (other != me)
    overflow = jnp.any(remote & (pos_send >= CAPACITY)) | jnp.any(remote & (pos_recv >= CAPACITY))

    shape = (devices, blocks, 4 * BLOCK_SIDE, CAPACITY * BLOCK_SIDE)
    b = lax.broadcasted_iota(jnp.int32, shape, 0)
    i = lax.broadcasted_iota(jnp.int32, shape, 2)
    q = lax.broadcasted_iota(jnp.int32, shape, 3)
    send_mat = (
        _per_lane(remote)[None, :, :, None]
        & (_per_lane(other)[None, :, :, None] == b)
        & (_per_lane(pos_send)[None, :, :, None] == q // BLOCK_SIDE)
        & (i % BLOCK_SIDE == q % BLOCK_SIDE)
    ).astype(jnp.bfloat16)

    local = ok & (other == me)
    recv_mat = _select_matrix(
        devices + blocks,
        ok & (local | (pos_recv < CAPACITY)),
        jnp.where(local, devices + nb % blocks, other),
        jnp.where(local, jnp.broadcast_to(opp, nb.shape), pos_recv),
    )
    return overflow, send_mat, recv_mat, (nb, ok, jnp.broadcast_to(opp, nb.shape))


def _split_einsum(spec, x, sel):
    ins, out = spec.split("->")
    lhs, rhs = ins.split(",")
    parts = jnp.stack(_split3_xla(x))
    res = jnp.einsum(
        "s" + lhs + "," + rhs + "->s" + out, parts, sel.astype(jnp.bfloat16),
        preferred_element_type=jnp.float32,
    )
    return (res[0] + res[1]) + res[2]


def exchange_fast(edges, tables, flag=None):
    _, send_mat, recv_mat, _ = tables
    comps = edges.shape[1]
    send_buf = _split_einsum("lci,bliq->bcq", edges, send_mat)
    if flag is not None:
        row = jnp.broadcast_to(flag.astype(jnp.float32), (send_buf.shape[0], 1, send_buf.shape[2]))
        send_buf = jnp.concatenate([send_buf, row], axis=1)
    recv = lax.all_to_all(send_buf, "space", 0, 0, tiled=True)
    srcs = jnp.concatenate([recv[:, :comps], edges], axis=0)
    ghosts = _split_einsum("aci,aiLq->Lcq", srcs, recv_mat)
    if flag is None:
        return ghosts
    return ghosts, jnp.any(recv[:, comps, 0] > 0.5)


def exchange_slow(edges, tables):
    nb, ok, opp = tables[3]
    gathered = lax.all_gather(edges, "space", axis=0, tiled=True)
    fmat = _select_matrix(gathered.shape[0], ok, nb, opp)
    return _split_einsum("aci,aiLq->Lcq", gathered, fmat)


def interaction_of(spectra, pairs, coupling):
    plus_vals = jnp.take(spectra, pairs[:, 0], axis=1)
    minus_vals = jnp.take(spectra, pairs[:, 1], axis=1)
    return coupling[None, :, None] * (
        spectra * spectra * (plus_vals + minus_vals) - 2.0 * spectra * plus_vals * minus_vals
    )


def shards(devices, parts, action, coupling, active, neighbours, pairs):
    blocks, comp_dev, cell_count = action.shape
    spec_rank = lax.axis_index("spec")
    comp_ids = spec_rank * comp_dev + jnp.arange(comp_dev, dtype=jnp.int32)
    courant_x, courant_y = courant(comp_ids)
    coefs = jnp.stack(
        [
            jnp.maximum(courant_x, 0.0),
            jnp.minimum(courant_x, 0.0),
            jnp.maximum(courant_y, 0.0),
            jnp.minimum(courant_y, 0.0),
        ]
    )[:, :, None]
    tables = routing(neighbours, blocks, devices)

    def propagate(exchange, first=None):
        current_action = action
        edges = edges_call(action)
        for substep_idx in range(SUBSTEPS):
            if first is not None and substep_idx == 0:
                ghosts = first
            else:
                ghosts = exchange(edges)
            if substep_idx < SUBSTEPS - 1:
                current_action, edges = step_call(current_action, ghosts, coefs)
            else:
                return last_step_call(current_action, ghosts, coefs, parts)

    edges0 = edges_call(action)
    ghosts, anywhere = exchange_fast(edges0, tables, tables[0])
    chunked = propagate(lambda e: exchange_fast(e, tables), ghosts)
    chunked = lax.cond(
        anywhere, lambda c: propagate(lambda e: exchange_slow(e, tables)), lambda c: c, chunked
    )
    mixing = (
        jax.nn.one_hot(pairs[:, 0], SPECTRAL_COUNT, dtype=jnp.float32)
        + jax.nn.one_hot(pairs[:, 1], SPECTRAL_COUNT, dtype=jnp.float32)
        - 2.0 * jnp.eye(SPECTRAL_COUNT, dtype=jnp.float32)
    ).astype(jnp.bfloat16)
    arrived = lax.all_to_all(chunked, "spec", split_axis=0, concat_axis=0, tiled=True)
    points = jnp.transpose(arrived, (1, 0, 2, 3)).reshape(blocks, parts * comp_dev, -1)
    interaction = interaction_of(points, pairs, coupling)
    hi, mid, lo = _split3_xla(interaction)
    mix = lambda part: jnp.einsum("cj,bcx->bjx", mixing, part, preferred_element_type=jnp.float32)
    change = (mix(hi) + mix(mid)) + mix(lo)
    evolved = (points + change).reshape(blocks, parts, comp_dev, -1)
    back = lax.all_to_all(jnp.transpose(evolved, (1, 0, 2, 3)), "spec", 0, 0, tiled=True)
    result = jnp.transpose(back, (1, 2, 0, 3)).reshape(blocks, comp_dev, cell_count)
    return jnp.where(active[:, None, None] > 0, result, 0.0)


def solution(mesh):
    placed = (P("space", "spec", None), P(), P("space"), P("space", None), P())
    return jax.shard_map(
        functools.partial(shards, mesh.shape["space"], mesh.shape["spec"]), mesh=mesh, in_specs=placed, out_specs=P("space", "spec", None), check_vma=False
    )
```

```python
import functools
import math

import jax
import jax.numpy as jnp
from jax import lax
from jax.experimental import pallas as pl
from jax.experimental.pallas import tpu as pltpu
from jax.sharding import PartitionSpec as P

NDIR = 36
BLOCK_SIDE = 32
BLOCK_CELLS = BLOCK_SIDE * BLOCK_SIDE
SUBSTEPS = 3
SPECTRAL_COUNT = 1296
CAPACITY = 4
INTERPRET = False
KERNEL_PARAMS = pltpu.CompilerParams()

CFL = 0.68


def courant(comp_ids):
    frequency = (comp_ids // NDIR).astype(jnp.float32)
    direction = comp_ids % NDIR
    half_dirs = NDIR // 2
    angles = (
        2.0
        * math.pi
        / NDIR
        * ((2 * (direction % half_dirs) + direction // half_dirs).astype(jnp.float32) + 0.5)
    )
    speeds = CFL * jnp.exp(-frequency * math.log(1.1))
    return (speeds * jnp.cos(angles), speeds * jnp.sin(angles))


def _split3(x):
    hi = x.astype(jnp.bfloat16)
    rest = x - hi.astype(jnp.float32)
    mid = rest.astype(jnp.bfloat16)
    lo = (rest - mid.astype(jnp.float32)).astype(jnp.bfloat16)
    return hi, mid, lo


def _split3_xla(x):
    hi = lax.reduce_precision(x, exponent_bits=8, mantissa_bits=7)
    rest = x - hi
    mid = lax.reduce_precision(rest, exponent_bits=8, mantissa_bits=7)
    lo = rest - mid
    return tuple(p.astype(jnp.bfloat16) for p in (hi, mid, lo))


def _select_dot(x, sel, dims):
    hi, mid, lo = _split3(x)
    run = lambda part: lax.dot_general(part, sel, (dims, ((), ())), preferred_element_type=jnp.float32)
    return (run(hi) + run(mid)) + run(lo)


def _we_hits():
    row = lax.broadcasted_iota(jnp.int32, (4 * BLOCK_SIDE, BLOCK_CELLS), 0)
    cell = lax.broadcasted_iota(jnp.int32, (4 * BLOCK_SIDE, BLOCK_CELLS), 1)
    side = row // BLOCK_SIDE
    t = row % BLOCK_SIDE
    target = jnp.where(side == 0, t * BLOCK_SIDE, t * BLOCK_SIDE + BLOCK_SIDE - 1)
    return ((cell == target) & (side < 2)).astype(jnp.bfloat16)


def _edges_of(field, we_hit):
    we = _select_dot(field, we_hit, ((1,), (1,)))
    lane = lax.broadcasted_iota(jnp.int32, (1, 4 * BLOCK_SIDE), 1)
    south = pltpu.roll(field[:, : 4 * BLOCK_SIDE], 2 * BLOCK_SIDE, 1)
    north = field[:, BLOCK_CELLS - 4 * BLOCK_SIDE :]
    return jnp.where(lane < 2 * BLOCK_SIDE, we, jnp.where(lane < 3 * BLOCK_SIDE, south, north))


def _edge_kernel(a_ref, e_ref):
    e_ref[0] = _edges_of(a_ref[0], _we_hits())


def _step_kernel(a_ref, g_ref, c_ref, o_ref, e_ref=None):
    a = a_ref[0]
    g = g_ref[0]
    we_hit = _we_hits()
    g_we = _select_dot(g, we_hit, ((1,), (0,)))
    cell = lax.broadcasted_iota(jnp.int32, (1, BLOCK_CELLS), 1)
    lane = lax.broadcasted_iota(jnp.int32, (1, 4 * BLOCK_SIDE), 1)
    x = cell % BLOCK_SIDE
    tile = 4 * BLOCK_SIDE
    from_west = jnp.where(x == 0, g_we, pltpu.roll(a, 1, 1))
    from_east = jnp.where(x == BLOCK_SIDE - 1, g_we, pltpu.roll(a, BLOCK_CELLS - 1, 1))
    south_in = pltpu.roll(a, BLOCK_SIDE, 1)
    from_south = jnp.concatenate(
        [jnp.where(lane < BLOCK_SIDE, pltpu.roll(g, 2 * BLOCK_SIDE, 1), south_in[:, :tile]),
         south_in[:, tile:]],
        axis=1,
    )
    north_in = pltpu.roll(a, BLOCK_CELLS - BLOCK_SIDE, 1)
    from_north = jnp.concatenate(
        [north_in[:, : BLOCK_CELLS - tile],
         jnp.where(lane >= 3 * BLOCK_SIDE, g, north_in[:, BLOCK_CELLS - tile :])],
        axis=1,
    )
    x_plus = c_ref[0]
    x_minus = c_ref[1]
    y_plus = c_ref[2]
    y_minus = c_ref[3]
    new = (
        a
        - (x_plus * (a - from_west) + x_minus * (from_east - a))
        - (y_plus * (a - from_south) + y_minus * (from_north - a))
    )
    if e_ref is None:
        chunk = o_ref.shape[-1]
        for k in range(o_ref.shape[0]):
            o_ref[k, 0] = new[:, k * chunk : (k + 1) * chunk]
    else:
        o_ref[0] = new
        e_ref[0] = _edges_of(new, we_hit)


def last_step_call(action, ghosts, coefs, parts):
    blocks, comps, cells = action.shape
    chunk = cells // parts
    return pl.pallas_call(
        _step_kernel,
        grid=(blocks,),
        in_specs=[
            pl.BlockSpec((1, comps, cells), lambda b: (b, 0, 0)),
            pl.BlockSpec((1, comps, 4 * BLOCK_SIDE), lambda b: (b, 0, 0)),
            pl.BlockSpec((4, comps, 1), lambda b: (0, 0, 0)),
        ],
        out_specs=pl.BlockSpec((parts, 1, comps, chunk), lambda b: (0, b, 0, 0)),
        out_shape=jax.ShapeDtypeStruct((parts, blocks, comps, chunk), jnp.float32),
        compiler_params=KERNEL_PARAMS,
        interpret=INTERPRET,
    )(action, ghosts, coefs)


def edges_call(action):
    blocks, comps, cells = action.shape
    return pl.pallas_call(
        _edge_kernel,
        grid=(blocks,),
        in_specs=[pl.BlockSpec((1, comps, cells), lambda b: (b, 0, 0))],
        out_specs=pl.BlockSpec((1, comps, 4 * BLOCK_SIDE), lambda b: (b, 0, 0)),
        out_shape=jax.ShapeDtypeStruct((blocks, comps, 4 * BLOCK_SIDE), jnp.float32),
        compiler_params=KERNEL_PARAMS,
        interpret=INTERPRET,
    )(action)


def step_call(action, ghosts, coefs):
    blocks, comps, cells = action.shape
    return pl.pallas_call(
        _step_kernel,
        grid=(blocks,),
        in_specs=[
            pl.BlockSpec((1, comps, cells), lambda b: (b, 0, 0)),
            pl.BlockSpec((1, comps, 4 * BLOCK_SIDE), lambda b: (b, 0, 0)),
            pl.BlockSpec((4, comps, 1), lambda b: (0, 0, 0)),
        ],
        out_specs=[
            pl.BlockSpec((1, comps, cells), lambda b: (b, 0, 0)),
            pl.BlockSpec((1, comps, 4 * BLOCK_SIDE), lambda b: (b, 0, 0)),
        ],
        out_shape=[
            jax.ShapeDtypeStruct((blocks, comps, cells), jnp.float32),
            jax.ShapeDtypeStruct((blocks, comps, 4 * BLOCK_SIDE), jnp.float32),
        ],
        compiler_params=KERNEL_PARAMS,
        interpret=INTERPRET,
    )(action, ghosts, coefs)


def _per_lane(table):
    return jnp.repeat(table, BLOCK_SIDE, axis=1)


def _select_matrix(rows, use, row_of, group_of):
    blocks = use.shape[0]
    shape = (rows, 4 * BLOCK_SIDE, blocks, 4 * BLOCK_SIDE)
    a = lax.broadcasted_iota(jnp.int32, shape, 0)
    i = lax.broadcasted_iota(jnp.int32, shape, 1)
    q = lax.broadcasted_iota(jnp.int32, shape, 3)
    hit = (
        _per_lane(use)[None, None]
        & (_per_lane(row_of)[None, None] == a)
        & (_per_lane(group_of)[None, None] == i // BLOCK_SIDE)
        & (i % BLOCK_SIDE == q % BLOCK_SIDE)
    )
    return hit.astype(jnp.float32)


def routing(neighbours, blocks, devices):
    me = lax.axis_index("space")
    opp = jnp.array([1, 0, 3, 2], jnp.int32)[None, :]
    nb = neighbours
    ok = nb >= 0
    other = jnp.where(ok, nb // blocks, -1)
    own_key = jnp.arange(blocks * 4, dtype=jnp.int32).reshape(blocks, 4)
    src_key = (nb % blocks) * 4 + opp

    def rank(key):
        same = (other.reshape(-1)[None, :] == other.reshape(-1)[:, None]) & ok.reshape(-1)[None, :]
        before = key.reshape(-1)[None, :] < key.reshape(-1)[:, None]
        return (same & before).sum(-1).astype(jnp.int32).reshape(blocks, 4)

    pos_send = rank(own_key)
    pos_recv = rank(src_key)
    remote = ok & (other != me)
    overflow = jnp.any(remote & (pos_send >= CAPACITY)) | jnp.any(remote & (pos_recv >= CAPACITY))

    shape = (devices, blocks, 4 * BLOCK_SIDE, CAPACITY * BLOCK_SIDE)
    b = lax.broadcasted_iota(jnp.int32, shape, 0)
    i = lax.broadcasted_iota(jnp.int32, shape, 2)
    q = lax.broadcasted_iota(jnp.int32, shape, 3)
    send_mat = (
        _per_lane(remote)[None, :, :, None]
        & (_per_lane(other)[None, :, :, None] == b)
        & (_per_lane(pos_send)[None, :, :, None] == q // BLOCK_SIDE)
        & (i % BLOCK_SIDE == q % BLOCK_SIDE)
    ).astype(jnp.bfloat16)

    local = ok & (other == me)
    recv_mat = _select_matrix(
        devices + blocks,
        ok & (local | (pos_recv < CAPACITY)),
        jnp.where(local, devices + nb % blocks, other),
        jnp.where(local, jnp.broadcast_to(opp, nb.shape), pos_recv),
    )
    return overflow, send_mat, recv_mat, (nb, ok, jnp.broadcast_to(opp, nb.shape))


def _split_einsum(spec, x, sel):
    sel = sel.astype(jnp.bfloat16)
    run = lambda part: jnp.einsum(spec, part, sel, preferred_element_type=jnp.float32)
    hi, mid, lo = _split3_xla(x)
    return (run(hi) + run(mid)) + run(lo)


def exchange_fast(edges, tables, flag=None):
    _, send_mat, recv_mat, _ = tables
    comps = edges.shape[1]
    send_buf = _split_einsum("lci,bliq->bcq", edges, send_mat)
    if flag is not None:
        row = jnp.broadcast_to(flag.astype(jnp.float32), (send_buf.shape[0], 1, send_buf.shape[2]))
        send_buf = jnp.concatenate([send_buf, row], axis=1)
    recv = lax.all_to_all(send_buf, "space", 0, 0, tiled=True)
    srcs = jnp.concatenate([recv[:, :comps], edges], axis=0)
    ghosts = jnp.einsum("aci,aiLq->Lcq", srcs, recv_mat, precision=lax.Precision.HIGHEST)
    if flag is None:
        return ghosts
    return ghosts, jnp.any(recv[:, comps, 0] > 0.5)


def exchange_slow(edges, tables):
    nb, ok, opp = tables[3]
    gathered = lax.all_gather(edges, "space", axis=0, tiled=True)
    fmat = _select_matrix(gathered.shape[0], ok, nb, opp)
    return _split_einsum("aci,aiLq->Lcq", gathered, fmat)


def interaction_of(spectra, pairs, coupling):
    plus_vals = jnp.take(spectra, pairs[:, 0], axis=1)
    minus_vals = jnp.take(spectra, pairs[:, 1], axis=1)
    return coupling[None, :, None] * (
        spectra * spectra * (plus_vals + minus_vals) - 2.0 * spectra * plus_vals * minus_vals
    )


def shards(devices, parts, action, coupling, active, neighbours, pairs):
    blocks, comp_dev, cell_count = action.shape
    spec_rank = lax.axis_index("spec")
    comp_ids = spec_rank * comp_dev + jnp.arange(comp_dev, dtype=jnp.int32)
    courant_x, courant_y = courant(comp_ids)
    coefs = jnp.stack(
        [
            jnp.maximum(courant_x, 0.0),
            jnp.minimum(courant_x, 0.0),
            jnp.maximum(courant_y, 0.0),
            jnp.minimum(courant_y, 0.0),
        ]
    )[:, :, None]
    tables = routing(neighbours, blocks, devices)

    def propagate(exchange, first=None):
        current_action = action
        edges = edges_call(action)
        for substep_idx in range(SUBSTEPS):
            if first is not None and substep_idx == 0:
                ghosts = first
            else:
                ghosts = exchange(edges)
            if substep_idx < SUBSTEPS - 1:
                current_action, edges = step_call(current_action, ghosts, coefs)
            else:
                return last_step_call(current_action, ghosts, coefs, parts)

    edges0 = edges_call(action)
    ghosts, anywhere = exchange_fast(edges0, tables, tables[0])
    chunked = propagate(lambda e: exchange_fast(e, tables), ghosts)
    chunked = lax.cond(
        anywhere, lambda c: propagate(lambda e: exchange_slow(e, tables)), lambda c: c, chunked
    )
    mixing = (
        jax.nn.one_hot(pairs[:, 0], SPECTRAL_COUNT, dtype=jnp.float32)
        + jax.nn.one_hot(pairs[:, 1], SPECTRAL_COUNT, dtype=jnp.float32)
        - 2.0 * jnp.eye(SPECTRAL_COUNT, dtype=jnp.float32)
    ).astype(jnp.bfloat16)
    arrived = lax.all_to_all(chunked, "spec", split_axis=0, concat_axis=0, tiled=True)
    points = jnp.transpose(arrived, (1, 0, 2, 3)).reshape(blocks, parts * comp_dev, -1)
    interaction = interaction_of(points, pairs, coupling)
    hi, mid, lo = _split3_xla(interaction)
    mix = lambda part: jnp.einsum("cj,bcx->bjx", mixing, part, preferred_element_type=jnp.float32)
    change = (mix(hi) + mix(mid)) + mix(lo)
    evolved = (points + change).reshape(blocks, parts, comp_dev, -1)
    back = lax.all_to_all(jnp.transpose(evolved, (1, 0, 2, 3)), "spec", 0, 0, tiled=True)
    result = jnp.transpose(back, (1, 2, 0, 3)).reshape(blocks, comp_dev, cell_count)
    return jnp.where(active[:, None, None] > 0, result, 0.0)


def solution(mesh):
    placed = (P("space", "spec", None), P(), P("space"), P("space", None), P())
    return jax.shard_map(
        functools.partial(shards, mesh.shape["space"], mesh.shape["spec"]), mesh=mesh, in_specs=placed, out_specs=P("space", "spec", None), check_vma=False
    )
```

```python
import functools
import math

import jax
import jax.numpy as jnp
from jax import lax
from jax.experimental import pallas as pl
from jax.experimental.pallas import tpu as pltpu
from jax.sharding import PartitionSpec as P

NDIR = 36
BLOCK_SIDE = 32
BLOCK_CELLS = BLOCK_SIDE * BLOCK_SIDE
SUBSTEPS = 3
SPECTRAL_COUNT = 1296
CAPACITY = 4
INTERPRET = False
SLOTS_PER_STEP = 2
KERNEL_PARAMS = pltpu.CompilerParams()

CFL = 0.68


def courant(comp_ids):
    frequency = (comp_ids // NDIR).astype(jnp.float32)
    direction = comp_ids % NDIR
    half_dirs = NDIR // 2
    angles = (
        2.0
        * math.pi
        / NDIR
        * ((2 * (direction % half_dirs) + direction // half_dirs).astype(jnp.float32) + 0.5)
    )
    speeds = CFL * jnp.exp(-frequency * math.log(1.1))
    return (speeds * jnp.cos(angles), speeds * jnp.sin(angles))


def _split3(x):
    hi = x.astype(jnp.bfloat16)
    rest = x - hi.astype(jnp.float32)
    mid = rest.astype(jnp.bfloat16)
    lo = (rest - mid.astype(jnp.float32)).astype(jnp.bfloat16)
    return hi, mid, lo


def _split3_xla(x):
    hi = lax.reduce_precision(x, exponent_bits=8, mantissa_bits=7)
    rest = x - hi
    mid = lax.reduce_precision(rest, exponent_bits=8, mantissa_bits=7)
    lo = rest - mid
    return tuple(p.astype(jnp.bfloat16) for p in (hi, mid, lo))


def _select_dot(x, sel, dims):
    hi, mid, lo = _split3(x)
    run = lambda part: lax.dot_general(part, sel, (dims, ((), ())), preferred_element_type=jnp.float32)
    return (run(hi) + run(mid)) + run(lo)


def _we_hits():
    row = lax.broadcasted_iota(jnp.int32, (4 * BLOCK_SIDE, BLOCK_CELLS), 0)
    cell = lax.broadcasted_iota(jnp.int32, (4 * BLOCK_SIDE, BLOCK_CELLS), 1)
    side = row // BLOCK_SIDE
    t = row % BLOCK_SIDE
    target = jnp.where(side == 0, t * BLOCK_SIDE, t * BLOCK_SIDE + BLOCK_SIDE - 1)
    return ((cell == target) & (side < 2)).astype(jnp.bfloat16)


def _edges_of(field, we_hit):
    we = _select_dot(field, we_hit, ((1,), (1,)))
    lane = lax.broadcasted_iota(jnp.int32, (1, 4 * BLOCK_SIDE), 1)
    south = pltpu.roll(field[:, : 4 * BLOCK_SIDE], 2 * BLOCK_SIDE, 1)
    north = field[:, BLOCK_CELLS - 4 * BLOCK_SIDE :]
    return jnp.where(lane < 2 * BLOCK_SIDE, we, jnp.where(lane < 3 * BLOCK_SIDE, south, north))


def _edge_kernel(a_ref, e_ref):
    for s in range(a_ref.shape[0]):
        e_ref[s] = _edges_of(a_ref[s], _we_hits())


def _step_kernel(a_ref, g_ref, c_ref, o_ref, e_ref=None):
    for s in range(a_ref.shape[0]):
        _step_slot(s, a_ref, g_ref, c_ref, o_ref, e_ref)


def _step_slot(s, a_ref, g_ref, c_ref, o_ref, e_ref):
    a = a_ref[s]
    g = g_ref[s]
    we_hit = _we_hits()
    g_we = _select_dot(g, we_hit, ((1,), (0,)))
    cell = lax.broadcasted_iota(jnp.int32, (1, BLOCK_CELLS), 1)
    lane = lax.broadcasted_iota(jnp.int32, (1, 4 * BLOCK_SIDE), 1)
    x = cell % BLOCK_SIDE
    tile = 4 * BLOCK_SIDE
    from_west = jnp.where(x == 0, g_we, pltpu.roll(a, 1, 1))
    from_east = jnp.where(x == BLOCK_SIDE - 1, g_we, pltpu.roll(a, BLOCK_CELLS - 1, 1))
    south_in = pltpu.roll(a, BLOCK_SIDE, 1)
    from_south = jnp.concatenate(
        [jnp.where(lane < BLOCK_SIDE, pltpu.roll(g, 2 * BLOCK_SIDE, 1), south_in[:, :tile]),
         south_in[:, tile:]],
        axis=1,
    )
    north_in = pltpu.roll(a, BLOCK_CELLS - BLOCK_SIDE, 1)
    from_north = jnp.concatenate(
        [north_in[:, : BLOCK_CELLS - tile],
         jnp.where(lane >= 3 * BLOCK_SIDE, g, north_in[:, BLOCK_CELLS - tile :])],
        axis=1,
    )
    x_plus = c_ref[0]
    x_minus = c_ref[1]
    y_plus = c_ref[2]
    y_minus = c_ref[3]
    new = (
        a
        - (x_plus * (a - from_west) + x_minus * (from_east - a))
        - (y_plus * (a - from_south) + y_minus * (from_north - a))
    )
    if e_ref is None:
        chunk = o_ref.shape[-1]
        for k in range(o_ref.shape[0]):
            o_ref[k, s] = new[:, k * chunk : (k + 1) * chunk]
    else:
        o_ref[s] = new
        e_ref[s] = _edges_of(new, we_hit)


def last_step_call(action, ghosts, coefs, parts):
    blocks, comps, cells = action.shape
    chunk = cells // parts
    return pl.pallas_call(
        _step_kernel,
        grid=(blocks // SLOTS_PER_STEP,),
        in_specs=[
            pl.BlockSpec((SLOTS_PER_STEP, comps, cells), lambda b: (b, 0, 0)),
            pl.BlockSpec((SLOTS_PER_STEP, comps, 4 * BLOCK_SIDE), lambda b: (b, 0, 0)),
            pl.BlockSpec((4, comps, 1), lambda b: (0, 0, 0)),
        ],
        out_specs=pl.BlockSpec((parts, SLOTS_PER_STEP, comps, chunk), lambda b: (0, b, 0, 0)),
        out_shape=jax.ShapeDtypeStruct((parts, blocks, comps, chunk), jnp.float32),
        compiler_params=KERNEL_PARAMS,
        interpret=INTERPRET,
    )(action, ghosts, coefs)


def edges_call(action):
    blocks, comps, cells = action.shape
    return pl.pallas_call(
        _edge_kernel,
        grid=(blocks // SLOTS_PER_STEP,),
        in_specs=[pl.BlockSpec((SLOTS_PER_STEP, comps, cells), lambda b: (b, 0, 0))],
        out_specs=pl.BlockSpec((SLOTS_PER_STEP, comps, 4 * BLOCK_SIDE), lambda b: (b, 0, 0)),
        out_shape=jax.ShapeDtypeStruct((blocks, comps, 4 * BLOCK_SIDE), jnp.float32),
        compiler_params=KERNEL_PARAMS,
        interpret=INTERPRET,
    )(action)


def step_call(action, ghosts, coefs):
    blocks, comps, cells = action.shape
    return pl.pallas_call(
        _step_kernel,
        grid=(blocks // SLOTS_PER_STEP,),
        in_specs=[
            pl.BlockSpec((SLOTS_PER_STEP, comps, cells), lambda b: (b, 0, 0)),
            pl.BlockSpec((SLOTS_PER_STEP, comps, 4 * BLOCK_SIDE), lambda b: (b, 0, 0)),
            pl.BlockSpec((4, comps, 1), lambda b: (0, 0, 0)),
        ],
        out_specs=[
            pl.BlockSpec((SLOTS_PER_STEP, comps, cells), lambda b: (b, 0, 0)),
            pl.BlockSpec((SLOTS_PER_STEP, comps, 4 * BLOCK_SIDE), lambda b: (b, 0, 0)),
        ],
        out_shape=[
            jax.ShapeDtypeStruct((blocks, comps, cells), jnp.float32),
            jax.ShapeDtypeStruct((blocks, comps, 4 * BLOCK_SIDE), jnp.float32),
        ],
        compiler_params=KERNEL_PARAMS,
        interpret=INTERPRET,
    )(action, ghosts, coefs)


def _per_lane(table):
    return jnp.repeat(table, BLOCK_SIDE, axis=1)


def _select_matrix(rows, use, row_of, group_of):
    blocks = use.shape[0]
    shape = (rows, 4 * BLOCK_SIDE, blocks, 4 * BLOCK_SIDE)
    a = lax.broadcasted_iota(jnp.int32, shape, 0)
    i = lax.broadcasted_iota(jnp.int32, shape, 1)
    q = lax.broadcasted_iota(jnp.int32, shape, 3)
    hit = (
        _per_lane(use)[None, None]
        & (_per_lane(row_of)[None, None] == a)
        & (_per_lane(group_of)[None, None] == i // BLOCK_SIDE)
        & (i % BLOCK_SIDE == q % BLOCK_SIDE)
    )
    return hit.astype(jnp.float32)


def routing(neighbours, blocks, devices):
    me = lax.axis_index("space")
    opp = jnp.array([1, 0, 3, 2], jnp.int32)[None, :]
    nb = neighbours
    ok = nb >= 0
    other = jnp.where(ok, nb // blocks, -1)
    own_key = jnp.arange(blocks * 4, dtype=jnp.int32).reshape(blocks, 4)
    src_key = (nb % blocks) * 4 + opp

    def rank(key):
        same = (other.reshape(-1)[None, :] == other.reshape(-1)[:, None]) & ok.reshape(-1)[None, :]
        before = key.reshape(-1)[None, :] < key.reshape(-1)[:, None]
        return (same & before).sum(-1).astype(jnp.int32).reshape(blocks, 4)

    pos_send = rank(own_key)
    pos_recv = rank(src_key)
    remote = ok & (other != me)
    overflow = jnp.any(remote & (pos_send >= CAPACITY)) | jnp.any(remote & (pos_recv >= CAPACITY))

    shape = (devices, blocks, 4 * BLOCK_SIDE, CAPACITY * BLOCK_SIDE)
    b = lax.broadcasted_iota(jnp.int32, shape, 0)
    i = lax.broadcasted_iota(jnp.int32, shape, 2)
    q = lax.broadcasted_iota(jnp.int32, shape, 3)
    send_mat = (
        _per_lane(remote)[None, :, :, None]
        & (_per_lane(other)[None, :, :, None] == b)
        & (_per_lane(pos_send)[None, :, :, None] == q // BLOCK_SIDE)
        & (i % BLOCK_SIDE == q % BLOCK_SIDE)
    ).astype(jnp.float32)

    local = ok & (other == me)
    recv_mat = _select_matrix(
        devices + blocks,
        ok & (local | (pos_recv < CAPACITY)),
        jnp.where(local, devices + nb % blocks, other),
        jnp.where(local, jnp.broadcast_to(opp, nb.shape), pos_recv),
    )
    return overflow, send_mat, recv_mat, (nb, ok, jnp.broadcast_to(opp, nb.shape))


def _split_einsum(spec, x, sel):
    sel = sel.astype(jnp.bfloat16)
    run = lambda part: jnp.einsum(spec, part, sel, preferred_element_type=jnp.float32)
    hi, mid, lo = _split3_xla(x)
    return (run(hi) + run(mid)) + run(lo)


def exchange_fast(edges, tables, flag=None):
    _, send_mat, recv_mat, _ = tables
    comps = edges.shape[1]
    send_buf = _split_einsum("lci,bliq->bcq", edges, send_mat)
    if flag is not None:
        row = jnp.broadcast_to(flag.astype(jnp.float32), (send_buf.shape[0], 1, send_buf.shape[2]))
        send_buf = jnp.concatenate([send_buf, row], axis=1)
    recv = lax.all_to_all(send_buf, "space", 0, 0, tiled=True)
    srcs = jnp.concatenate([recv[:, :comps], edges], axis=0)
    ghosts = jnp.einsum("aci,aiLq->Lcq", srcs, recv_mat, precision=lax.Precision.HIGHEST)
    if flag is None:
        return ghosts
    return ghosts, jnp.any(recv[:, comps, 0] > 0.5)


def exchange_slow(edges, tables):
    nb, ok, opp = tables[3]
    gathered = lax.all_gather(edges, "space", axis=0, tiled=True)
    fmat = _select_matrix(gathered.shape[0], ok, nb, opp)
    return _split_einsum("aci,aiLq->Lcq", gathered, fmat)


def interaction_of(spectra, pairs, coupling):
    plus_vals = jnp.take(spectra, pairs[:, 0], axis=1)
    minus_vals = jnp.take(spectra, pairs[:, 1], axis=1)
    return coupling[None, :, None] * (
        spectra * spectra * (plus_vals + minus_vals) - 2.0 * spectra * plus_vals * minus_vals
    )


def shards(devices, parts, action, coupling, active, neighbours, pairs):
    blocks, comp_dev, cell_count = action.shape
    spec_rank = lax.axis_index("spec")
    comp_ids = spec_rank * comp_dev + jnp.arange(comp_dev, dtype=jnp.int32)
    courant_x, courant_y = courant(comp_ids)
    coefs = jnp.stack(
        [
            jnp.maximum(courant_x, 0.0),
            jnp.minimum(courant_x, 0.0),
            jnp.maximum(courant_y, 0.0),
            jnp.minimum(courant_y, 0.0),
        ]
    )[:, :, None]
    tables = routing(neighbours, blocks, devices)

    def propagate(exchange, first=None):
        current_action = action
        edges = edges_call(action)
        for substep_idx in range(SUBSTEPS):
            if first is not None and substep_idx == 0:
                ghosts = first
            else:
                ghosts = exchange(edges)
            if substep_idx < SUBSTEPS - 1:
                current_action, edges = step_call(current_action, ghosts, coefs)
            else:
                return last_step_call(current_action, ghosts, coefs, parts)

    edges0 = edges_call(action)
    ghosts, anywhere = exchange_fast(edges0, tables, tables[0])
    chunked = propagate(lambda e: exchange_fast(e, tables), ghosts)
    chunked = lax.cond(
        anywhere, lambda c: propagate(lambda e: exchange_slow(e, tables)), lambda c: c, chunked
    )
    mixing = (
        jax.nn.one_hot(pairs[:, 0], SPECTRAL_COUNT, dtype=jnp.float32)
        + jax.nn.one_hot(pairs[:, 1], SPECTRAL_COUNT, dtype=jnp.float32)
        - 2.0 * jnp.eye(SPECTRAL_COUNT, dtype=jnp.float32)
    ).astype(jnp.bfloat16)
    arrived = lax.all_to_all(chunked, "spec", split_axis=0, concat_axis=0, tiled=True)
    points = jnp.transpose(arrived, (1, 0, 2, 3)).reshape(blocks, parts * comp_dev, -1)
    interaction = interaction_of(points, pairs, coupling)
    hi, mid, lo = _split3_xla(interaction)
    mix = lambda part: jnp.einsum("cj,bcx->bjx", mixing, part, preferred_element_type=jnp.float32)
    change = (mix(hi) + mix(mid)) + mix(lo)
    evolved = (points + change).reshape(blocks, parts, comp_dev, -1)
    back = lax.all_to_all(jnp.transpose(evolved, (1, 0, 2, 3)), "spec", 0, 0, tiled=True)
    result = jnp.transpose(back, (1, 2, 0, 3)).reshape(blocks, comp_dev, cell_count)
    return jnp.where(active[:, None, None] > 0, result, 0.0)


def solution(mesh):
    placed = (P("space", "spec", None), P(), P("space"), P("space", None), P())
    return jax.shard_map(
        functools.partial(shards, mesh.shape["space"], mesh.shape["spec"]), mesh=mesh, in_specs=placed, out_specs=P("space", "spec", None), check_vma=False
    )
```

```python
import functools
import math

import jax
import jax.numpy as jnp
from jax import lax
from jax.experimental import pallas as pl
from jax.experimental.pallas import tpu as pltpu
from jax.sharding import PartitionSpec as P

NDIR = 36
BLOCK_SIDE = 32
BLOCK_CELLS = BLOCK_SIDE * BLOCK_SIDE
SUBSTEPS = 3
SPECTRAL_COUNT = 1296
CAPACITY = 4
INTERPRET = False
SLOTS_PER_STEP = 4
KERNEL_PARAMS = pltpu.CompilerParams()

CFL = 0.68


def courant(comp_ids):
    frequency = (comp_ids // NDIR).astype(jnp.float32)
    direction = comp_ids % NDIR
    half_dirs = NDIR // 2
    angles = (
        2.0
        * math.pi
        / NDIR
        * ((2 * (direction % half_dirs) + direction // half_dirs).astype(jnp.float32) + 0.5)
    )
    speeds = CFL * jnp.exp(-frequency * math.log(1.1))
    return (speeds * jnp.cos(angles), speeds * jnp.sin(angles))


def _split3(x):
    hi = x.astype(jnp.bfloat16)
    rest = x - hi.astype(jnp.float32)
    mid = rest.astype(jnp.bfloat16)
    lo = (rest - mid.astype(jnp.float32)).astype(jnp.bfloat16)
    return hi, mid, lo


def _split3_xla(x):
    hi = lax.reduce_precision(x, exponent_bits=8, mantissa_bits=7)
    rest = x - hi
    mid = lax.reduce_precision(rest, exponent_bits=8, mantissa_bits=7)
    lo = rest - mid
    return tuple(p.astype(jnp.bfloat16) for p in (hi, mid, lo))


def _select_dot(x, sel, dims):
    hi, mid, lo = _split3(x)
    run = lambda part: lax.dot_general(part, sel, (dims, ((), ())), preferred_element_type=jnp.float32)
    return (run(hi) + run(mid)) + run(lo)


def _we_hits():
    row = lax.broadcasted_iota(jnp.int32, (4 * BLOCK_SIDE, BLOCK_CELLS), 0)
    cell = lax.broadcasted_iota(jnp.int32, (4 * BLOCK_SIDE, BLOCK_CELLS), 1)
    side = row // BLOCK_SIDE
    t = row % BLOCK_SIDE
    target = jnp.where(side == 0, t * BLOCK_SIDE, t * BLOCK_SIDE + BLOCK_SIDE - 1)
    return ((cell == target) & (side < 2)).astype(jnp.bfloat16)


def _edges_of(field, we_hit):
    we = _select_dot(field, we_hit, ((1,), (1,)))
    lane = lax.broadcasted_iota(jnp.int32, (1, 4 * BLOCK_SIDE), 1)
    south = pltpu.roll(field[:, : 4 * BLOCK_SIDE], 2 * BLOCK_SIDE, 1)
    north = field[:, BLOCK_CELLS - 4 * BLOCK_SIDE :]
    return jnp.where(lane < 2 * BLOCK_SIDE, we, jnp.where(lane < 3 * BLOCK_SIDE, south, north))


def _edge_kernel(a_ref, e_ref):
    for s in range(a_ref.shape[0]):
        e_ref[s] = _edges_of(a_ref[s], _we_hits())


def _step_kernel(a_ref, g_ref, c_ref, o_ref, e_ref=None):
    for s in range(a_ref.shape[0]):
        _step_slot(s, a_ref, g_ref, c_ref, o_ref, e_ref)


def _step_slot(s, a_ref, g_ref, c_ref, o_ref, e_ref):
    a = a_ref[s]
    g = g_ref[s]
    we_hit = _we_hits()
    g_we = _select_dot(g, we_hit, ((1,), (0,)))
    cell = lax.broadcasted_iota(jnp.int32, (1, BLOCK_CELLS), 1)
    lane = lax.broadcasted_iota(jnp.int32, (1, 4 * BLOCK_SIDE), 1)
    x = cell % BLOCK_SIDE
    tile = 4 * BLOCK_SIDE
    from_west = jnp.where(x == 0, g_we, pltpu.roll(a, 1, 1))
    from_east = jnp.where(x == BLOCK_SIDE - 1, g_we, pltpu.roll(a, BLOCK_CELLS - 1, 1))
    south_in = pltpu.roll(a, BLOCK_SIDE, 1)
    from_south = jnp.concatenate(
        [jnp.where(lane < BLOCK_SIDE, pltpu.roll(g, 2 * BLOCK_SIDE, 1), south_in[:, :tile]),
         south_in[:, tile:]],
        axis=1,
    )
    north_in = pltpu.roll(a, BLOCK_CELLS - BLOCK_SIDE, 1)
    from_north = jnp.concatenate(
        [north_in[:, : BLOCK_CELLS - tile],
         jnp.where(lane >= 3 * BLOCK_SIDE, g, north_in[:, BLOCK_CELLS - tile :])],
        axis=1,
    )
    x_plus = c_ref[0]
    x_minus = c_ref[1]
    y_plus = c_ref[2]
    y_minus = c_ref[3]
    new = (
        a
        - (x_plus * (a - from_west) + x_minus * (from_east - a))
        - (y_plus * (a - from_south) + y_minus * (from_north - a))
    )
    if e_ref is None:
        chunk = o_ref.shape[-1]
        for k in range(o_ref.shape[0]):
            o_ref[k, s] = new[:, k * chunk : (k + 1) * chunk]
    else:
        o_ref[s] = new
        e_ref[s] = _edges_of(new, we_hit)


def last_step_call(action, ghosts, coefs, parts):
    blocks, comps, cells = action.shape
    chunk = cells // parts
    return pl.pallas_call(
        _step_kernel,
        grid=(blocks // SLOTS_PER_STEP,),
        in_specs=[
            pl.BlockSpec((SLOTS_PER_STEP, comps, cells), lambda b: (b, 0, 0)),
            pl.BlockSpec((SLOTS_PER_STEP, comps, 4 * BLOCK_SIDE), lambda b: (b, 0, 0)),
            pl.BlockSpec((4, comps, 1), lambda b: (0, 0, 0)),
        ],
        out_specs=pl.BlockSpec((parts, SLOTS_PER_STEP, comps, chunk), lambda b: (0, b, 0, 0)),
        out_shape=jax.ShapeDtypeStruct((parts, blocks, comps, chunk), jnp.float32),
        compiler_params=KERNEL_PARAMS,
        interpret=INTERPRET,
    )(action, ghosts, coefs)


def edges_call(action):
    blocks, comps, cells = action.shape
    return pl.pallas_call(
        _edge_kernel,
        grid=(blocks // SLOTS_PER_STEP,),
        in_specs=[pl.BlockSpec((SLOTS_PER_STEP, comps, cells), lambda b: (b, 0, 0))],
        out_specs=pl.BlockSpec((SLOTS_PER_STEP, comps, 4 * BLOCK_SIDE), lambda b: (b, 0, 0)),
        out_shape=jax.ShapeDtypeStruct((blocks, comps, 4 * BLOCK_SIDE), jnp.float32),
        compiler_params=KERNEL_PARAMS,
        interpret=INTERPRET,
    )(action)


def step_call(action, ghosts, coefs):
    blocks, comps, cells = action.shape
    return pl.pallas_call(
        _step_kernel,
        grid=(blocks // SLOTS_PER_STEP,),
        in_specs=[
            pl.BlockSpec((SLOTS_PER_STEP, comps, cells), lambda b: (b, 0, 0)),
            pl.BlockSpec((SLOTS_PER_STEP, comps, 4 * BLOCK_SIDE), lambda b: (b, 0, 0)),
            pl.BlockSpec((4, comps, 1), lambda b: (0, 0, 0)),
        ],
        out_specs=[
            pl.BlockSpec((SLOTS_PER_STEP, comps, cells), lambda b: (b, 0, 0)),
            pl.BlockSpec((SLOTS_PER_STEP, comps, 4 * BLOCK_SIDE), lambda b: (b, 0, 0)),
        ],
        out_shape=[
            jax.ShapeDtypeStruct((blocks, comps, cells), jnp.float32),
            jax.ShapeDtypeStruct((blocks, comps, 4 * BLOCK_SIDE), jnp.float32),
        ],
        compiler_params=KERNEL_PARAMS,
        interpret=INTERPRET,
    )(action, ghosts, coefs)


def _per_lane(table):
    return jnp.repeat(table, BLOCK_SIDE, axis=1)


def _select_matrix(rows, use, row_of, group_of):
    blocks = use.shape[0]
    shape = (rows, 4 * BLOCK_SIDE, blocks, 4 * BLOCK_SIDE)
    a = lax.broadcasted_iota(jnp.int32, shape, 0)
    i = lax.broadcasted_iota(jnp.int32, shape, 1)
    q = lax.broadcasted_iota(jnp.int32, shape, 3)
    hit = (
        _per_lane(use)[None, None]
        & (_per_lane(row_of)[None, None] == a)
        & (_per_lane(group_of)[None, None] == i // BLOCK_SIDE)
        & (i % BLOCK_SIDE == q % BLOCK_SIDE)
    )
    return hit.astype(jnp.float32)


def routing(neighbours, blocks, devices):
    me = lax.axis_index("space")
    opp = jnp.array([1, 0, 3, 2], jnp.int32)[None, :]
    nb = neighbours
    ok = nb >= 0
    other = jnp.where(ok, nb // blocks, -1)
    own_key = jnp.arange(blocks * 4, dtype=jnp.int32).reshape(blocks, 4)
    src_key = (nb % blocks) * 4 + opp

    def rank(key):
        same = (other.reshape(-1)[None, :] == other.reshape(-1)[:, None]) & ok.reshape(-1)[None, :]
        before = key.reshape(-1)[None, :] < key.reshape(-1)[:, None]
        return (same & before).sum(-1).astype(jnp.int32).reshape(blocks, 4)

    pos_send = rank(own_key)
    pos_recv = rank(src_key)
    remote = ok & (other != me)
    overflow = jnp.any(remote & (pos_send >= CAPACITY)) | jnp.any(remote & (pos_recv >= CAPACITY))

    shape = (devices, blocks, 4 * BLOCK_SIDE, CAPACITY * BLOCK_SIDE)
    b = lax.broadcasted_iota(jnp.int32, shape, 0)
    i = lax.broadcasted_iota(jnp.int32, shape, 2)
    q = lax.broadcasted_iota(jnp.int32, shape, 3)
    send_mat = (
        _per_lane(remote)[None, :, :, None]
        & (_per_lane(other)[None, :, :, None] == b)
        & (_per_lane(pos_send)[None, :, :, None] == q // BLOCK_SIDE)
        & (i % BLOCK_SIDE == q % BLOCK_SIDE)
    ).astype(jnp.float32)

    local = ok & (other == me)
    recv_mat = _select_matrix(
        devices + blocks,
        ok & (local | (pos_recv < CAPACITY)),
        jnp.where(local, devices + nb % blocks, other),
        jnp.where(local, jnp.broadcast_to(opp, nb.shape), pos_recv),
    )
    return overflow, send_mat, recv_mat, (nb, ok, jnp.broadcast_to(opp, nb.shape))


def _split_einsum(spec, x, sel):
    sel = sel.astype(jnp.bfloat16)
    run = lambda part: jnp.einsum(spec, part, sel, preferred_element_type=jnp.float32)
    hi, mid, lo = _split3_xla(x)
    return (run(hi) + run(mid)) + run(lo)


def exchange_fast(edges, tables, flag=None):
    _, send_mat, recv_mat, _ = tables
    comps = edges.shape[1]
    send_buf = _split_einsum("lci,bliq->bcq", edges, send_mat)
    if flag is not None:
        row = jnp.broadcast_to(flag.astype(jnp.float32), (send_buf.shape[0], 1, send_buf.shape[2]))
        send_buf = jnp.concatenate([send_buf, row], axis=1)
    recv = lax.all_to_all(send_buf, "space", 0, 0, tiled=True)
    srcs = jnp.concatenate([recv[:, :comps], edges], axis=0)
    ghosts = jnp.einsum("aci,aiLq->Lcq", srcs, recv_mat, precision=lax.Precision.HIGHEST)
    if flag is None:
        return ghosts
    return ghosts, jnp.any(recv[:, comps, 0] > 0.5)


def exchange_slow(edges, tables):
    nb, ok, opp = tables[3]
    gathered = lax.all_gather(edges, "space", axis=0, tiled=True)
    fmat = _select_matrix(gathered.shape[0], ok, nb, opp)
    return _split_einsum("aci,aiLq->Lcq", gathered, fmat)


def interaction_of(spectra, pairs, coupling):
    plus_vals = jnp.take(spectra, pairs[:, 0], axis=1)
    minus_vals = jnp.take(spectra, pairs[:, 1], axis=1)
    return coupling[None, :, None] * (
        spectra * spectra * (plus_vals + minus_vals) - 2.0 * spectra * plus_vals * minus_vals
    )


def shards(devices, parts, action, coupling, active, neighbours, pairs):
    blocks, comp_dev, cell_count = action.shape
    spec_rank = lax.axis_index("spec")
    comp_ids = spec_rank * comp_dev + jnp.arange(comp_dev, dtype=jnp.int32)
    courant_x, courant_y = courant(comp_ids)
    coefs = jnp.stack(
        [
            jnp.maximum(courant_x, 0.0),
            jnp.minimum(courant_x, 0.0),
            jnp.maximum(courant_y, 0.0),
            jnp.minimum(courant_y, 0.0),
        ]
    )[:, :, None]
    tables = routing(neighbours, blocks, devices)

    def propagate(exchange, first=None):
        current_action = action
        edges = edges_call(action)
        for substep_idx in range(SUBSTEPS):
            if first is not None and substep_idx == 0:
                ghosts = first
            else:
                ghosts = exchange(edges)
            if substep_idx < SUBSTEPS - 1:
                current_action, edges = step_call(current_action, ghosts, coefs)
            else:
                return last_step_call(current_action, ghosts, coefs, parts)

    edges0 = edges_call(action)
    ghosts, anywhere = exchange_fast(edges0, tables, tables[0])
    chunked = propagate(lambda e: exchange_fast(e, tables), ghosts)
    chunked = lax.cond(
        anywhere, lambda c: propagate(lambda e: exchange_slow(e, tables)), lambda c: c, chunked
    )
    mixing = (
        jax.nn.one_hot(pairs[:, 0], SPECTRAL_COUNT, dtype=jnp.float32)
        + jax.nn.one_hot(pairs[:, 1], SPECTRAL_COUNT, dtype=jnp.float32)
        - 2.0 * jnp.eye(SPECTRAL_COUNT, dtype=jnp.float32)
    ).astype(jnp.bfloat16)
    arrived = lax.all_to_all(chunked, "spec", split_axis=0, concat_axis=0, tiled=True)
    points = jnp.transpose(arrived, (1, 0, 2, 3)).reshape(blocks, parts * comp_dev, -1)
    interaction = interaction_of(points, pairs, coupling)
    hi, mid, lo = _split3_xla(interaction)
    mix = lambda part: jnp.einsum("cj,bcx->bjx", mixing, part, preferred_element_type=jnp.float32)
    change = (mix(hi) + mix(mid)) + mix(lo)
    evolved = (points + change).reshape(blocks, parts, comp_dev, -1)
    back = lax.all_to_all(jnp.transpose(evolved, (1, 0, 2, 3)), "spec", 0, 0, tiled=True)
    result = jnp.transpose(back, (1, 2, 0, 3)).reshape(blocks, comp_dev, cell_count)
    return jnp.where(active[:, None, None] > 0, result, 0.0)


def solution(mesh):
    placed = (P("space", "spec", None), P(), P("space"), P("space", None), P())
    return jax.shard_map(
        functools.partial(shards, mesh.shape["space"], mesh.shape["spec"]), mesh=mesh, in_specs=placed, out_specs=P("space", "spec", None), check_vma=False
    )
```

```python
import functools
import math

import jax
import jax.numpy as jnp
from jax import lax
from jax.experimental import pallas as pl
from jax.experimental.pallas import tpu as pltpu
from jax.sharding import PartitionSpec as P

NDIR = 36
BLOCK_SIDE = 32
BLOCK_CELLS = BLOCK_SIDE * BLOCK_SIDE
SUBSTEPS = 3
SPECTRAL_COUNT = 1296
CAPACITY = 4
INTERPRET = False
SLOTS_PER_STEP = 2
KERNEL_PARAMS = pltpu.CompilerParams()

CFL = 0.68


def courant(comp_ids):
    frequency = (comp_ids // NDIR).astype(jnp.float32)
    direction = comp_ids % NDIR
    half_dirs = NDIR // 2
    angles = (
        2.0
        * math.pi
        / NDIR
        * ((2 * (direction % half_dirs) + direction // half_dirs).astype(jnp.float32) + 0.5)
    )
    speeds = CFL * jnp.exp(-frequency * math.log(1.1))
    return (speeds * jnp.cos(angles), speeds * jnp.sin(angles))


def _split3(x):
    hi = x.astype(jnp.bfloat16)
    rest = x - hi.astype(jnp.float32)
    mid = rest.astype(jnp.bfloat16)
    lo = (rest - mid.astype(jnp.float32)).astype(jnp.bfloat16)
    return hi, mid, lo


def _split3_xla(x):
    hi = lax.reduce_precision(x, exponent_bits=8, mantissa_bits=7)
    rest = x - hi
    mid = lax.reduce_precision(rest, exponent_bits=8, mantissa_bits=7)
    lo = rest - mid
    return tuple(p.astype(jnp.bfloat16) for p in (hi, mid, lo))


def _select_dot(x, sel, dims):
    hi, mid, lo = _split3(x)
    run = lambda part: lax.dot_general(part, sel, (dims, ((), ())), preferred_element_type=jnp.float32)
    return (run(hi) + run(mid)) + run(lo)


def _we_hits():
    row = lax.broadcasted_iota(jnp.int32, (4 * BLOCK_SIDE, BLOCK_CELLS), 0)
    cell = lax.broadcasted_iota(jnp.int32, (4 * BLOCK_SIDE, BLOCK_CELLS), 1)
    side = row // BLOCK_SIDE
    t = row % BLOCK_SIDE
    target = jnp.where(side == 0, t * BLOCK_SIDE, t * BLOCK_SIDE + BLOCK_SIDE - 1)
    return ((cell == target) & (side < 2)).astype(jnp.bfloat16)


def _edges_of(field, we_hit):
    we = _select_dot(field, we_hit, ((1,), (1,)))
    lane = lax.broadcasted_iota(jnp.int32, (1, 4 * BLOCK_SIDE), 1)
    south = pltpu.roll(field[:, : 4 * BLOCK_SIDE], 2 * BLOCK_SIDE, 1)
    north = field[:, BLOCK_CELLS - 4 * BLOCK_SIDE :]
    return jnp.where(lane < 2 * BLOCK_SIDE, we, jnp.where(lane < 3 * BLOCK_SIDE, south, north))


def _edge_kernel(a_ref, e_ref):
    for s in range(a_ref.shape[0]):
        e_ref[s] = _edges_of(a_ref[s], _we_hits())


def _step_kernel(a_ref, g_ref, c_ref, o_ref, e_ref=None):
    for s in range(a_ref.shape[0]):
        _step_slot(s, a_ref, g_ref, c_ref, o_ref, e_ref)


def _step_slot(s, a_ref, g_ref, c_ref, o_ref, e_ref):
    a = a_ref[s]
    g = g_ref[s]
    we_hit = _we_hits()
    g_we = _select_dot(g, we_hit, ((1,), (0,)))
    cell = lax.broadcasted_iota(jnp.int32, (1, BLOCK_CELLS), 1)
    lane = lax.broadcasted_iota(jnp.int32, (1, 4 * BLOCK_SIDE), 1)
    x = cell % BLOCK_SIDE
    tile = 4 * BLOCK_SIDE
    from_west = jnp.where(x == 0, g_we, pltpu.roll(a, 1, 1))
    from_east = jnp.where(x == BLOCK_SIDE - 1, g_we, pltpu.roll(a, BLOCK_CELLS - 1, 1))
    south_in = pltpu.roll(a, BLOCK_SIDE, 1)
    from_south = jnp.concatenate(
        [jnp.where(lane < BLOCK_SIDE, pltpu.roll(g, 2 * BLOCK_SIDE, 1), south_in[:, :tile]),
         south_in[:, tile:]],
        axis=1,
    )
    north_in = pltpu.roll(a, BLOCK_CELLS - BLOCK_SIDE, 1)
    from_north = jnp.concatenate(
        [north_in[:, : BLOCK_CELLS - tile],
         jnp.where(lane >= 3 * BLOCK_SIDE, g, north_in[:, BLOCK_CELLS - tile :])],
        axis=1,
    )
    x_plus = c_ref[0]
    x_minus = c_ref[1]
    y_plus = c_ref[2]
    y_minus = c_ref[3]
    new = (
        a
        - (x_plus * (a - from_west) + x_minus * (from_east - a))
        - (y_plus * (a - from_south) + y_minus * (from_north - a))
    )
    if e_ref is None:
        chunk = o_ref.shape[-1]
        for k in range(o_ref.shape[0]):
            o_ref[k, s] = new[:, k * chunk : (k + 1) * chunk]
    else:
        o_ref[s] = new
        e_ref[s] = _edges_of(new, we_hit)


def last_step_call(action, ghosts, coefs, parts):
    blocks, comps, cells = action.shape
    chunk = cells // parts
    return pl.pallas_call(
        _step_kernel,
        grid=(blocks // SLOTS_PER_STEP,),
        in_specs=[
            pl.BlockSpec((SLOTS_PER_STEP, comps, cells), lambda b: (b, 0, 0)),
            pl.BlockSpec((SLOTS_PER_STEP, comps, 4 * BLOCK_SIDE), lambda b: (b, 0, 0)),
            pl.BlockSpec((4, comps, 1), lambda b: (0, 0, 0)),
        ],
        out_specs=pl.BlockSpec((parts, SLOTS_PER_STEP, comps, chunk), lambda b: (0, b, 0, 0)),
        out_shape=jax.ShapeDtypeStruct((parts, blocks, comps, chunk), jnp.float32),
        compiler_params=KERNEL_PARAMS,
        interpret=INTERPRET,
    )(action, ghosts, coefs)


def edges_call(action):
    blocks, comps, cells = action.shape
    return pl.pallas_call(
        _edge_kernel,
        grid=(blocks // SLOTS_PER_STEP,),
        in_specs=[pl.BlockSpec((SLOTS_PER_STEP, comps, cells), lambda b: (b, 0, 0))],
        out_specs=pl.BlockSpec((SLOTS_PER_STEP, comps, 4 * BLOCK_SIDE), lambda b: (b, 0, 0)),
        out_shape=jax.ShapeDtypeStruct((blocks, comps, 4 * BLOCK_SIDE), jnp.float32),
        compiler_params=KERNEL_PARAMS,
        interpret=INTERPRET,
    )(action)


def step_call(action, ghosts, coefs):
    blocks, comps, cells = action.shape
    return pl.pallas_call(
        _step_kernel,
        grid=(blocks // SLOTS_PER_STEP,),
        in_specs=[
            pl.BlockSpec((SLOTS_PER_STEP, comps, cells), lambda b: (b, 0, 0)),
            pl.BlockSpec((SLOTS_PER_STEP, comps, 4 * BLOCK_SIDE), lambda b: (b, 0, 0)),
            pl.BlockSpec((4, comps, 1), lambda b: (0, 0, 0)),
        ],
        out_specs=[
            pl.BlockSpec((SLOTS_PER_STEP, comps, cells), lambda b: (b, 0, 0)),
            pl.BlockSpec((SLOTS_PER_STEP, comps, 4 * BLOCK_SIDE), lambda b: (b, 0, 0)),
        ],
        out_shape=[
            jax.ShapeDtypeStruct((blocks, comps, cells), jnp.float32),
            jax.ShapeDtypeStruct((blocks, comps, 4 * BLOCK_SIDE), jnp.float32),
        ],
        compiler_params=KERNEL_PARAMS,
        interpret=INTERPRET,
    )(action, ghosts, coefs)


def _per_lane(table):
    return jnp.repeat(table, BLOCK_SIDE, axis=1)


def _select_matrix(rows, use, row_of, group_of):
    blocks = use.shape[0]
    shape = (rows, 4 * BLOCK_SIDE, blocks, 4 * BLOCK_SIDE)
    a = lax.broadcasted_iota(jnp.int32, shape, 0)
    i = lax.broadcasted_iota(jnp.int32, shape, 1)
    q = lax.broadcasted_iota(jnp.int32, shape, 3)
    hit = (
        _per_lane(use)[None, None]
        & (_per_lane(row_of)[None, None] == a)
        & (_per_lane(group_of)[None, None] == i // BLOCK_SIDE)
        & (i % BLOCK_SIDE == q % BLOCK_SIDE)
    )
    return hit.astype(jnp.float32)


def routing(neighbours, blocks, devices):
    me = lax.axis_index("space")
    opp = jnp.array([1, 0, 3, 2], jnp.int32)[None, :]
    nb = neighbours
    ok = nb >= 0
    other = jnp.where(ok, nb // blocks, -1)
    own_key = jnp.arange(blocks * 4, dtype=jnp.int32).reshape(blocks, 4)
    src_key = (nb % blocks) * 4 + opp

    def rank(key):
        same = (other.reshape(-1)[None, :] == other.reshape(-1)[:, None]) & ok.reshape(-1)[None, :]
        before = key.reshape(-1)[None, :] < key.reshape(-1)[:, None]
        return (same & before).sum(-1).astype(jnp.int32).reshape(blocks, 4)

    pos_send = rank(own_key)
    pos_recv = rank(src_key)
    remote = ok & (other != me)
    overflow = jnp.any(remote & (pos_send >= CAPACITY)) | jnp.any(remote & (pos_recv >= CAPACITY))

    shape = (devices, blocks, 4 * BLOCK_SIDE, CAPACITY * BLOCK_SIDE)
    b = lax.broadcasted_iota(jnp.int32, shape, 0)
    i = lax.broadcasted_iota(jnp.int32, shape, 2)
    q = lax.broadcasted_iota(jnp.int32, shape, 3)
    send_mat = (
        _per_lane(remote)[None, :, :, None]
        & (_per_lane(other)[None, :, :, None] == b)
        & (_per_lane(pos_send)[None, :, :, None] == q // BLOCK_SIDE)
        & (i % BLOCK_SIDE == q % BLOCK_SIDE)
    ).astype(jnp.bfloat16)

    local = ok & (other == me)
    recv_mat = _select_matrix(
        devices + blocks,
        ok & (local | (pos_recv < CAPACITY)),
        jnp.where(local, devices + nb % blocks, other),
        jnp.where(local, jnp.broadcast_to(opp, nb.shape), pos_recv),
    )
    return overflow, send_mat, recv_mat, (nb, ok, jnp.broadcast_to(opp, nb.shape))


def _split_einsum(spec, x, sel):
    sel = sel.astype(jnp.bfloat16)
    run = lambda part: jnp.einsum(spec, part, sel, preferred_element_type=jnp.float32)
    hi, mid, lo = _split3_xla(x)
    return (run(hi) + run(mid)) + run(lo)


def exchange_fast(edges, tables, flag=None):
    _, send_mat, recv_mat, _ = tables
    comps = edges.shape[1]
    send_buf = _split_einsum("lci,bliq->bcq", edges, send_mat)
    if flag is not None:
        row = jnp.broadcast_to(flag.astype(jnp.float32), (send_buf.shape[0], 1, send_buf.shape[2]))
        send_buf = jnp.concatenate([send_buf, row], axis=1)
    recv = lax.all_to_all(send_buf, "space", 0, 0, tiled=True)
    srcs = jnp.concatenate([recv[:, :comps], edges], axis=0)
    ghosts = jnp.einsum("aci,aiLq->Lcq", srcs, recv_mat, precision=lax.Precision.HIGHEST)
    if flag is None:
        return ghosts
    return ghosts, jnp.any(recv[:, comps, 0] > 0.5)


def exchange_slow(edges, tables):
    nb, ok, opp = tables[3]
    gathered = lax.all_gather(edges, "space", axis=0, tiled=True)
    fmat = _select_matrix(gathered.shape[0], ok, nb, opp)
    return _split_einsum("aci,aiLq->Lcq", gathered, fmat)


def interaction_of(spectra, pairs, coupling):
    plus_vals = jnp.take(spectra, pairs[:, 0], axis=1)
    minus_vals = jnp.take(spectra, pairs[:, 1], axis=1)
    return coupling[None, :, None] * (
        spectra * spectra * (plus_vals + minus_vals) - 2.0 * spectra * plus_vals * minus_vals
    )


def shards(devices, parts, action, coupling, active, neighbours, pairs):
    blocks, comp_dev, cell_count = action.shape
    spec_rank = lax.axis_index("spec")
    comp_ids = spec_rank * comp_dev + jnp.arange(comp_dev, dtype=jnp.int32)
    courant_x, courant_y = courant(comp_ids)
    coefs = jnp.stack(
        [
            jnp.maximum(courant_x, 0.0),
            jnp.minimum(courant_x, 0.0),
            jnp.maximum(courant_y, 0.0),
            jnp.minimum(courant_y, 0.0),
        ]
    )[:, :, None]
    tables = routing(neighbours, blocks, devices)

    def propagate(exchange, first=None):
        current_action = action
        edges = edges_call(action)
        for substep_idx in range(SUBSTEPS):
            if first is not None and substep_idx == 0:
                ghosts = first
            else:
                ghosts = exchange(edges)
            if substep_idx < SUBSTEPS - 1:
                current_action, edges = step_call(current_action, ghosts, coefs)
            else:
                return last_step_call(current_action, ghosts, coefs, parts)

    edges0 = edges_call(action)
    ghosts, anywhere = exchange_fast(edges0, tables, tables[0])
    chunked = propagate(lambda e: exchange_fast(e, tables), ghosts)
    chunked = lax.cond(
        anywhere, lambda c: propagate(lambda e: exchange_slow(e, tables)), lambda c: c, chunked
    )
    mixing = (
        jax.nn.one_hot(pairs[:, 0], SPECTRAL_COUNT, dtype=jnp.float32)
        + jax.nn.one_hot(pairs[:, 1], SPECTRAL_COUNT, dtype=jnp.float32)
        - 2.0 * jnp.eye(SPECTRAL_COUNT, dtype=jnp.float32)
    ).astype(jnp.bfloat16)
    arrived = lax.all_to_all(chunked, "spec", split_axis=0, concat_axis=0, tiled=True)
    points = jnp.transpose(arrived, (1, 0, 2, 3)).reshape(blocks, parts * comp_dev, -1)
    interaction = interaction_of(points, pairs, coupling)
    hi, mid, lo = _split3_xla(interaction)
    mix = lambda part: jnp.einsum("cj,bcx->bjx", mixing, part, preferred_element_type=jnp.float32)
    change = (mix(hi) + mix(mid)) + mix(lo)
    evolved = (points + change).reshape(blocks, parts, comp_dev, -1)
    back = lax.all_to_all(jnp.transpose(evolved, (1, 0, 2, 3)), "spec", 0, 0, tiled=True)
    result = jnp.transpose(back, (1, 2, 0, 3)).reshape(blocks, comp_dev, cell_count)
    return jnp.where(active[:, None, None] > 0, result, 0.0)


def solution(mesh):
    placed = (P("space", "spec", None), P(), P("space"), P("space", None), P())
    return jax.shard_map(
        functools.partial(shards, mesh.shape["space"], mesh.shape["spec"]), mesh=mesh, in_specs=placed, out_specs=P("space", "spec", None), check_vma=False
    )
```
